32 devices in a mesh: atoms: 8 (over z, x), samples: 4 (over y, core).
Axes of the slice: x: 2, y: 2, z: 4, core: 2. Of those that a mesh axis runs over, the one named last changes fastest.
Arguments:
- token_feats: bfloat16 [2048, 768], P('atoms', 'samples'), may hold values from -6 to 6
- proj_w: bfloat16 [768, 128], P('samples'), may hold values from -0.21875 to 0.21875
- atom_single: bfloat16 [16384, 128], P('atoms'), may hold values from -6 to 6
- atom_token: int32 [16384], P('atoms'), may hold values from 0 to 2047, as said below
- true_coords: float32 [3, 16384], P(None, 'atoms'), may hold values from -12 to 12
- noise: float32 [4, 3, 16384], P('samples', None, 'atoms'), may hold values from -6 to 6
- sigma: float32 [4], P('samples'), may hold values from 0.5 to 4
- coord_in: float32 [3, 128], replicated, may hold values from -3.5 to 3.5
- w_qkv: bfloat16 [3, 128, 384], replicated, as said below
- w_o: bfloat16 [3, 128, 128], replicated, may hold values from -0.5 to 0.5
- w_gu: bfloat16 [3, 128, 512], replicated, may hold values from -0.5 to 0.5
- w_down: bfloat16 [3, 256, 128], replicated, may hold values from -0.375 to 0.375
- gains: float32 [3, 2, 128], replicated, may hold values from 0.1 to 1.9
- w_out: float32 [128, 3], replicated, may hold values from -0.5 to 0.5
- pair_blocks: int32 [128, 13], P('atoms'), may hold values from 0 to 127, as said below
- pair_count: int32 [128], P('atoms'), may hold values from 1 to 13, as said below
Outputs:
- coord_grad: float32 [4, 3, 16384], P('samples', None, 'atoms')
- lddt_grad: float32 [4, 3, 16384], P('samples', None, 'atoms')
The draws below stay inside these ranges and needn't reach their ends.
Inputs may be any that keep to these rules, and one draw needn't show every extreme that they name: `atom_token`: atom a belongs to a token that differs from a // 8 by at most 16 before clipping to the token range; in each aligned run of 2048 atoms the first atom is -16 and the last +16 from that value before clipping. `pair_blocks`: the first pair_count[b] entries of row b are distinct blocks, the first being b itself; entries past pair_count[b] are b. Listing is symmetric: c is among the live entries of row b exactly when b is among the live entries of row c. `pair_count`: some block has 13 live entries. `w_qkv`: Queries, keys and values stand side by side along the last dimension.
All inputs are finite; a program needn't handle non-finite values.
Results may differ from the reference program's by a relative error of at most 0.018.
Values may be sent and summed in bfloat16 or wider, within the bound.
No kernel may reach another device: no remote copies, remote signals or barrier semaphores. Data moves between devices by JAX's collectives and lax.ppermute only.
A program may use at most 64 MiB of HBM per device.

```python
import math
import jax
import jax.numpy as jnp
from jax import lax

C_TOKEN = 768
C_ATOM = 128
HEADS = 4
FF_ATOM = 256
ATOMS_TOK = 8
LAYERS = 3
QBLK = 32
KWIN = 128
HALO_TOK = 16
PAIR_BLK = 128
NOFF = 6
MAXP = 13
ATOM_DEV = 2048
TOKENS = 2048
NATOM = 16384
SAMPLES = 4
NBLK = 128


def draw_atom_token(key, part):
    position = jnp.arange(NATOM, dtype=jnp.int32)
    offset = jax.random.randint(jax.random.fold_in(key, 11), (NATOM,), -HALO_TOK, HALO_TOK + 1)
    inside = position % ATOM_DEV
    offset = jnp.where(inside == 0, -HALO_TOK, offset)
    offset = jnp.where(inside == ATOM_DEV - 1, HALO_TOK, offset)
    return jnp.clip(position // ATOMS_TOK + offset, 0, TOKENS - 1).astype(jnp.int32)


def pair_tables(key):
    blocks_dev = ATOM_DEV // PAIR_BLK
    devices = NBLK // blocks_dev
    far_shift = NBLK // 2 - 1
    other_shifts = jax.random.permutation(jax.random.fold_in(key, 21), NBLK // 2 - 2)[:NOFF - 1].astype(jnp.int32) + 1
    shifts = jnp.concatenate([jnp.full((1,), far_shift, jnp.int32), other_shifts])
    block_ids = jnp.arange(NBLK, dtype=jnp.int32)
    step_offsets = jnp.concatenate([jnp.zeros((1,), jnp.int32), shifts, -shifts])
    partner = (block_ids[:, None] + step_offsets[None, :]) % NBLK
    random_draws = jax.random.randint(jax.random.fold_in(key, 22), (NBLK, NBLK), 0, 9 * devices * devices)
    low_block = jnp.minimum(block_ids[:, None], partner)
    high_block = jnp.maximum(block_ids[:, None], partner)
    chance = random_draws[low_block, high_block]
    own_dev = block_ids // blocks_dev
    other_dev = partner // blocks_dev
    keep_limit = (devices + 2 * own_dev)[:, None] * (devices + 2 * other_dev)
    far_step = jnp.abs(step_offsets[None, :]) == far_shift
    keep_mask = (chance < keep_limit) | (step_offsets[None, :] == 0) | (high_block == NBLK - 1) | far_step
    slot_ids = jnp.arange(MAXP, dtype=jnp.int32)
    sort_key = (1 - keep_mask.astype(jnp.int32)) * MAXP + slot_ids[None, :]
    sort_order = jnp.argsort(sort_key, axis=1, stable=True)
    ordered = jnp.take_along_axis(partner, sort_order, axis=1)
    counts = jnp.sum(keep_mask.astype(jnp.int32), axis=1)
    listed = jnp.where(slot_ids[None, :] < counts[:, None], ordered, block_ids[:, None])
    return (listed.astype(jnp.int32), counts.astype(jnp.int32))


def draw_pair_blocks(key, part):
    return pair_tables(key)[0]


def draw_pair_count(key, part):
    return pair_tables(key)[1]


def draw_w_qkv(key, part):
    base_draw = jax.random.truncated_normal(key, -6.0, 6.0, (LAYERS, C_ATOM, 3 * C_ATOM), jnp.float32) * C_ATOM ** (-0.5)
    return base_draw.astype(jnp.bfloat16)


def shard_levels(stream_key, extent, split, least, largest):
    def one(dim, shards_of):
        steps = jax.random.uniform(jax.random.fold_in(jax.random.fold_in(stream_key, 6), dim), (shards_of,), jnp.float32, least / len(split), largest / len(split))
        return jnp.repeat(jnp.exp(steps), extent[dim] // shards_of).reshape((-1,) + (1,) * (len(extent) - dim - 1))

    gain = one(*split[0])
    for cut in split[1:]:
        gain = gain * one(*cut)
    return gain


def bell_draw(stream_key, shape, deviation, limit, cuts=(), kind=jnp.bfloat16):
    result = deviation * jax.random.normal(stream_key, shape, jnp.float32)
    if cuts:
        result = result * shard_levels(stream_key, shape, cuts, -0.22, 0.18)
    return jnp.clip(result, -limit, limit).astype(kind)


def setup_inputs(seed: int = 0) -> dict:
    key_list = jax.random.split(jax.random.key(seed), 17)
    token_feats = bell_draw(key_list[0], (TOKENS, C_TOKEN), 1.0, 6.0, ((0, 8), (1, 4)))
    proj_w = bell_draw(key_list[1], (C_TOKEN, C_ATOM), C_TOKEN ** -0.5, 0.21875, ((0, 4),))
    atom_single = bell_draw(key_list[2], (NATOM, C_ATOM), 1.0, 6.0, ((0, 8),))
    atom_token = draw_atom_token(jax.random.fold_in(key_list[16], 71), 0)
    true_coords = bell_draw(key_list[4], (3, NATOM), 2.0, 12.0, ((1, 8),), jnp.float32)
    noise = bell_draw(key_list[5], (SAMPLES, 3, NATOM), 1.0, 6.0, ((0, 4), (2, 8)), jnp.float32)
    sigma = jnp.clip(jnp.exp(math.log(4.0) - 2.0794415 * jax.random.uniform(key_list[6], (SAMPLES,), jnp.float32) ** shard_levels(key_list[6], (SAMPLES,), ((0, 4),), -0.2, 0.2)), 0.5, 4.0)
    coord_in = bell_draw(key_list[7], (3, C_ATOM), 3 ** -0.5, 3.5, (), jnp.float32)
    w_qkv = draw_w_qkv(jax.random.fold_in(key_list[16], 71), 0)
    w_o = bell_draw(key_list[9], (LAYERS, C_ATOM, C_ATOM), C_ATOM ** -0.5, 0.5)
    w_gu = bell_draw(key_list[10], (LAYERS, C_ATOM, 2 * FF_ATOM), C_ATOM ** -0.5, 0.5)
    w_down = bell_draw(key_list[11], (LAYERS, FF_ATOM, C_ATOM), FF_ATOM ** -0.5, 0.375)
    gains = jnp.clip(1.0 + 0.18 * jax.random.normal(key_list[12], (LAYERS, 2, C_ATOM), jnp.float32), 0.1, 1.9)
    w_out = bell_draw(key_list[13], (C_ATOM, 3), C_ATOM ** -0.5, 0.5, (), jnp.float32)
    pair_blocks = draw_pair_blocks(jax.random.fold_in(key_list[16], 71), 0)
    pair_count = draw_pair_count(jax.random.fold_in(key_list[16], 71), 0)
    return {"token_feats": token_feats, "proj_w": proj_w, "atom_single": atom_single, "atom_token": atom_token, "true_coords": true_coords, "noise": noise, "sigma": sigma, "coord_in": coord_in, "w_qkv": w_qkv, "w_o": w_o, "w_gu": w_gu, "w_down": w_down, "gains": gains, "w_out": w_out, "pair_blocks": pair_blocks, "pair_count": pair_count}


sigma_data = 2.0
norm_epsilon = 1e-05
thresholds = (0.5, 1.0, 2.0, 4.0)

def rms_norm(tensor):
    return tensor * lax.rsqrt(lax.optimization_barrier(jnp.mean(tensor * tensor, axis=-1, keepdims=True)) + norm_epsilon)

def window_attend(queries, padded_keys, padded_values, valid):
    samples, atoms, channels = queries.shape
    blocks = atoms // QBLK
    spread = KWIN // QBLK
    head_dim = channels // HEADS

    def windows(source):
        shaped = source.reshape((source.shape[0], blocks + spread - 1, QBLK) + source.shape[2:])
        return jnp.concatenate([shaped[:, shift_index:shift_index + blocks] for shift_index in range(spread)], axis=2)
    key_win = windows(padded_keys).reshape(samples, blocks, KWIN, HEADS, head_dim).astype(jnp.float32)
    value_win = windows(padded_values).reshape(samples, blocks, KWIN, HEADS, head_dim).astype(jnp.float32)
    mask_win = windows(valid[None])
    query_blk = queries.reshape(samples, blocks, QBLK, HEADS, head_dim).astype(jnp.float32)
    scores = jnp.einsum('sbqhe,sbkhe->sbhqk', query_blk, key_win) * head_dim ** (-0.5)
    scores = jnp.where(mask_win[:, :, None, None, :], scores, -1e+30)
    row_max = lax.optimization_barrier(jnp.max(scores, axis=-1, keepdims=True))
    exp_scores = jnp.exp(scores - row_max)
    weights = (exp_scores / lax.optimization_barrier(jnp.sum(exp_scores, axis=-1, keepdims=True))).astype(jnp.bfloat16)
    attended = jnp.einsum('sbhqk,sbkhe->sbqhe', weights.astype(jnp.float32), value_win)
    return attended.astype(jnp.bfloat16).reshape(samples, atoms, channels)

def tile_terms(own_pred, own_true, part_pred, part_true, keep_mask):
    square_pred = 0.0
    square_true = 0.0
    for axis_index in range(3):
        coord_gap = own_pred[:, axis_index, :, :, None] - part_pred[:, axis_index, :, None, :]
        square_pred = square_pred + coord_gap * coord_gap
        true_gap = own_true[axis_index, :, :, None] - part_true[axis_index, :, None, :]
        square_true = square_true + true_gap * true_gap
    dist_pred = jnp.sqrt(square_pred + 1.0)
    dist_true = jnp.sqrt(square_true + 1.0)
    gap_dist = dist_pred - dist_true
    error_soft = jnp.sqrt(gap_dist * gap_dist + 0.01)
    slope_sum = 0.0
    for threshold_value in thresholds:
        sig_value = jax.nn.sigmoid(threshold_value - error_soft)
        slope_sum = slope_sum + sig_value * (1.0 - sig_value)
    pair_coef = -0.25 * slope_sum * gap_dist / (error_soft * dist_pred) * keep_mask
    row_coef = lax.optimization_barrier(jnp.sum(pair_coef, axis=-1))
    col_coef = lax.optimization_barrier(jnp.sum(pair_coef, axis=-2))
    own_side = own_pred * row_coef[:, None] - jnp.einsum('stij,sdtj->sdti', pair_coef, part_pred, precision=lax.Precision.HIGHEST)
    part_side = part_pred * col_coef[:, None] - jnp.einsum('stij,sdti->sdtj', pair_coef, own_pred, precision=lax.Precision.HIGHEST)
    return (own_side, part_side)

def dense(left, right):
    return jnp.einsum('sac,cf->saf', left.astype(jnp.float32), right.astype(jnp.float32))

def reference(token_feats, proj_w, atom_single, atom_token, true_coords, noise, sigma, coord_in, w_qkv, w_o, w_gu, w_down, gains, w_out, pair_blocks, pair_count):
    token_proj = jnp.dot(token_feats, proj_w, preferred_element_type=jnp.float32).astype(jnp.bfloat16)
    atom_base = atom_single.astype(jnp.float32) + token_proj[atom_token].astype(jnp.float32)
    sigma_col = sigma[:, None, None]
    noisy = true_coords[None] + sigma_col * noise
    noise_total = sigma_col * sigma_col + sigma_data * sigma_data
    scaled = noisy / jnp.sqrt(noise_total)
    hidden = atom_base[None] + jnp.einsum('sda,dc->sac', scaled, coord_in, precision=lax.Precision.HIGHEST)
    key_halo = (KWIN - QBLK) // 2
    position = jnp.arange(NATOM + 2 * key_halo) - key_halo
    valid = (position >= 0) & (position < NATOM)
    channels = C_ATOM
    for layer_index in range(LAYERS):
        normed = (rms_norm(hidden) * gains[layer_index, 0]).astype(jnp.bfloat16)
        qkv_all = dense(normed, w_qkv[layer_index]).astype(jnp.bfloat16)
        queries = qkv_all[:, :, :channels]
        key_value = jnp.pad(qkv_all[:, :, channels:], ((0, 0), (key_halo, key_halo), (0, 0)))
        attended = window_attend(queries, key_value[:, :, :channels], key_value[:, :, channels:], valid)
        hidden = hidden + dense(attended, w_o[layer_index])
        normed = (rms_norm(hidden) * gains[layer_index, 1]).astype(jnp.bfloat16)
        gate_up = dense(normed, w_gu[layer_index])
        inner_act = (jax.nn.silu(gate_up[..., :FF_ATOM]) * gate_up[..., FF_ATOM:]).astype(jnp.bfloat16)
        hidden = hidden + dense(inner_act, w_down[layer_index])
    update = jnp.einsum('sac,cd->sda', rms_norm(hidden), w_out, precision=lax.Precision.HIGHEST)
    predicted = sigma_data * sigma_data / noise_total * noisy + sigma_col * sigma_data / jnp.sqrt(noise_total) * update
    mse_part = 2.0 / 3.0 * (noise_total / (sigma_col * sigma_data) ** 2) * (predicted - true_coords[None])
    blocks_pred = predicted.reshape(SAMPLES, 3, NBLK, PAIR_BLK)
    blocks_true = true_coords.reshape(3, NBLK, PAIR_BLK)
    diagonal_mask = jnp.eye(PAIR_BLK, dtype=jnp.float32)
    slot_ids = jnp.arange(MAXP, dtype=jnp.int32)

    def visit(back_grads, block_index):
        partners = pair_blocks[block_index]
        live_slot = (slot_ids < pair_count[block_index]).astype(jnp.float32)
        keep_mask = live_slot[:, None, None] * (1.0 - (partners == block_index).astype(jnp.float32)[:, None, None] * diagonal_mask)
        own_one = lax.dynamic_index_in_dim(blocks_pred, block_index, 2, keepdims=True)
        own_pred = jnp.broadcast_to(own_one, (SAMPLES, 3, MAXP, PAIR_BLK))
        true_one = lax.dynamic_index_in_dim(blocks_true, block_index, 1, keepdims=True)
        own_true = jnp.broadcast_to(true_one, (3, MAXP, PAIR_BLK))
        part_pred = jnp.take(blocks_pred, partners, axis=2)
        part_true = jnp.take(blocks_true, partners, axis=1)
        own_side, part_side = tile_terms(own_pred, own_true, part_pred, part_true, keep_mask)
        back_grads = back_grads.at[:, :, partners].add(part_side)
        return (back_grads, lax.optimization_barrier(jnp.sum(own_side, axis=2)))
    back_grads, own_grads = lax.scan(visit, jnp.zeros((SAMPLES, 3, NBLK, PAIR_BLK), jnp.float32), jnp.arange(NBLK, dtype=jnp.int32))
    pair_grad = jnp.moveaxis(own_grads, 0, 2) + back_grads
    pair_total = jnp.sum(pair_count.astype(jnp.float32) * (PAIR_BLK * PAIR_BLK) - PAIR_BLK)
    lddt_grad = NATOM * PAIR_BLK / pair_total * pair_grad.reshape(SAMPLES, 3, NATOM)
    coord_grad = mse_part - lddt_grad / PAIR_BLK
    return (coord_grad, lddt_grad)
```

```python
import jax
import jax.numpy as jnp
from jax import lax
from jax.sharding import PartitionSpec as P

HEADS = 4
FF_ATOM = 256
LAYERS = 3
QBLK = 32
KWIN = 128
HALO_TOK = 16
PAIR_BLK = 128


sigma_data = 2.0
norm_epsilon = 1e-05
thresholds = (0.5, 1.0, 2.0, 4.0)


def extended(value, sides, width):
    for axis, dim in sides:
        peers, length = (lax.axis_size(axis), value.shape[dim])
        up = [(i, (i + 1) % peers) for i in range(peers - 1)]
        down = [(j, i) for i, j in up]
        last = lax.slice_in_dim(value, length - width, length, axis=dim)
        first = lax.slice_in_dim(value, 0, width, axis=dim)
        before = lax.ppermute(last, axis, up)
        after = lax.ppermute(first, axis, down)
        value = jnp.concatenate([before, value, after], axis=dim)
    return value


def ring_parts(value, axis):
    peers = lax.axis_size(axis)
    parts = [value]
    for shift in range(1, peers):
        pairs = [(i, (i + shift) % peers) for i in range(peers)]
        parts.append(lax.ppermute(value, axis, pairs))
    return jnp.stack(parts)


def rms_norm(tensor):
    return tensor * lax.rsqrt(jnp.mean(tensor * tensor, axis=-1, keepdims=True) + norm_epsilon)


def window_attend(queries, padded_keys, padded_values, valid):
    samples, atoms, channels = queries.shape
    blocks = atoms // QBLK
    spread = KWIN // QBLK
    head_dim = channels // HEADS

    def windows(source):
        shaped = source.reshape((source.shape[0], blocks + spread - 1, QBLK) + source.shape[2:])
        return jnp.concatenate(
            [shaped[:, shift_index : shift_index + blocks] for shift_index in range(spread)], axis=2
        )

    key_win = windows(padded_keys).reshape(samples, blocks, KWIN, HEADS, head_dim)
    value_win = windows(padded_values).reshape(samples, blocks, KWIN, HEADS, head_dim)
    mask_win = windows(valid[None])
    query_blk = queries.reshape(samples, blocks, QBLK, HEADS, head_dim)
    scores = jnp.einsum(
        "sbqhe,sbkhe->sbhqk", query_blk, key_win, preferred_element_type=jnp.float32
    ) * head_dim ** (-0.5)
    scores = jnp.where(mask_win[:, :, None, None, :], scores, -1e30)
    row_max = jnp.max(scores, axis=-1, keepdims=True)
    exp_scores = jnp.exp(scores - row_max)
    weights = (exp_scores / jnp.sum(exp_scores, axis=-1, keepdims=True)).astype(jnp.bfloat16)
    attended = jnp.einsum(
        "sbhqk,sbkhe->sbqhe", weights, value_win, preferred_element_type=jnp.float32
    )
    return attended.astype(jnp.bfloat16).reshape(samples, atoms, channels)


def tile_terms(own_pred, own_true, part_pred, part_true, keep_mask):
    square_pred = 0.0
    square_true = 0.0
    for axis_index in range(3):
        coord_gap = own_pred[:, axis_index, :, :, None] - part_pred[:, axis_index, :, None, :]
        square_pred = square_pred + coord_gap * coord_gap
        true_gap = own_true[axis_index, :, :, None] - part_true[axis_index, :, None, :]
        square_true = square_true + true_gap * true_gap
    dist_pred = jnp.sqrt(square_pred + 1.0)
    dist_true = jnp.sqrt(square_true + 1.0)
    gap_dist = dist_pred - dist_true
    error_soft = jnp.sqrt(gap_dist * gap_dist + 0.01)
    slope_sum = 0.0
    for threshold_value in thresholds:
        sig_value = jax.nn.sigmoid(threshold_value - error_soft)
        slope_sum = slope_sum + sig_value * (1.0 - sig_value)
    pair_coef = -0.25 * slope_sum * gap_dist / (error_soft * dist_pred) * keep_mask
    row_coef = jnp.sum(pair_coef, axis=-1)
    col_coef = jnp.sum(pair_coef, axis=-2)
    own_side = own_pred * row_coef[:, None] - jnp.einsum(
        "stij,sdtj->sdti", pair_coef, part_pred, precision=lax.Precision.HIGHEST
    )
    part_side = part_pred * col_coef[:, None] - jnp.einsum(
        "stij,sdti->sdtj", pair_coef, own_pred, precision=lax.Precision.HIGHEST
    )
    return (own_side, part_side)


def dense(left, right):
    return jnp.einsum("sac,cf->saf", left, right, preferred_element_type=jnp.float32)


def on_device(
    token_feats,
    proj_w,
    atom_single,
    atom_token,
    true_coords,
    noise,
    sigma,
    coord_in,
    w_qkv,
    w_o,
    w_gu,
    w_down,
    gains,
    w_out,
    pair_blocks,
    pair_count,
):
    atom_rank = lax.axis_index("atoms")
    tok_rows = token_feats.shape[0]
    atom_rows = atom_single.shape[0]
    total_atoms = atom_rows * lax.axis_size("atoms")
    samples = noise.shape[0]
    feat_parts = ring_parts(token_feats, "samples")
    proj_parts = ring_parts(proj_w, "samples")
    token_sum = jnp.einsum(
        "kti,kio->to", feat_parts, proj_parts, preferred_element_type=jnp.float32
    )
    token_proj = token_sum.astype(jnp.bfloat16)
    padded_tok = extended(token_proj, (("atoms", 0),), HALO_TOK)
    first_token = atom_rank * tok_rows - HALO_TOK
    relative = atom_token - first_token
    onehot = (
        relative[:, None] == jnp.arange(tok_rows + 2 * HALO_TOK, dtype=jnp.int32)[None, :]
    ).astype(jnp.bfloat16)
    atom_base = atom_single.astype(jnp.float32) + jnp.dot(
        onehot, padded_tok, preferred_element_type=jnp.float32
    )
    sigma_col = sigma[:, None, None]
    noisy = true_coords[None] + sigma_col * noise
    noise_total = sigma_col * sigma_col + sigma_data * sigma_data
    scaled = noisy / jnp.sqrt(noise_total)
    hidden = atom_base[None] + jnp.einsum(
        "sda,dc->sac", scaled, coord_in, precision=lax.Precision.HIGHEST
    )
    key_halo = (KWIN - QBLK) // 2
    position = (
        atom_rank * atom_rows - key_halo + jnp.arange(atom_rows + 2 * key_halo, dtype=jnp.int32)
    )
    valid = (position >= 0) & (position < total_atoms)
    channels = hidden.shape[2]
    for layer_index in range(LAYERS):
        normed = (rms_norm(hidden) * gains[layer_index, 0]).astype(jnp.bfloat16)
        qkv_all = dense(normed, w_qkv[layer_index]).astype(jnp.bfloat16)
        queries = qkv_all[:, :, :channels]
        padded = extended(qkv_all[:, :, channels:], (("atoms", 1),), key_halo)
        attended = window_attend(queries, padded[:, :, :channels], padded[:, :, channels:], valid)
        hidden = hidden + dense(attended, w_o[layer_index])
        normed = (rms_norm(hidden) * gains[layer_index, 1]).astype(jnp.bfloat16)
        gate_up = dense(normed, w_gu[layer_index])
        inner_act = (jax.nn.silu(gate_up[..., :FF_ATOM]) * gate_up[..., FF_ATOM:]).astype(
            jnp.bfloat16
        )
        hidden = hidden + dense(inner_act, w_down[layer_index])
    update = jnp.einsum("sac,cd->sda", rms_norm(hidden), w_out, precision=lax.Precision.HIGHEST)
    predicted = (
        sigma_data * sigma_data / noise_total * noisy
        + sigma_col * sigma_data / jnp.sqrt(noise_total) * update
    )
    mse_part = (
        2.0 / 3.0 * (noise_total / (sigma_col * sigma_data) ** 2) * (predicted - true_coords[None])
    )
    block_count = atom_rows // PAIR_BLK
    own_pred = predicted.reshape(samples, 3, block_count, PAIR_BLK)
    own_true = true_coords.reshape(3, block_count, PAIR_BLK)
    atom_peers = lax.axis_size("atoms")
    count_row = jnp.zeros((1, atom_rows), jnp.float32).at[0, 0].set(
        jnp.sum(pair_count.astype(jnp.float32) * (PAIR_BLK * PAIR_BLK) - PAIR_BLK)
    )
    true_parts = ring_parts(jnp.concatenate([true_coords, count_row], axis=0), "atoms")
    pred_parts = ring_parts(predicted, "atoms")
    pred_blocks = jnp.moveaxis(
        pred_parts.reshape(atom_peers, samples, 3, block_count, PAIR_BLK), 0, 2
    ).reshape(samples, 3, atom_peers * block_count, PAIR_BLK)
    true_blocks = jnp.moveaxis(
        true_parts[:, :3].reshape(atom_peers, 3, block_count, PAIR_BLK), 0, 1
    ).reshape(3, atom_peers * block_count, PAIR_BLK)
    pair_total = jnp.sum(true_parts[:, 3, 0])
    own_ids = atom_rank * block_count + jnp.arange(block_count, dtype=jnp.int32)
    diagonal_mask = jnp.eye(PAIR_BLK, dtype=jnp.float32)

    def slot_terms(slot_index):
        partners = lax.dynamic_index_in_dim(pair_blocks, slot_index, 1, keepdims=False)
        live_slot = (slot_index < pair_count).astype(jnp.float32)
        keep_mask = live_slot[:, None, None] * (
            1.0 - (partners == own_ids).astype(jnp.float32)[:, None, None] * diagonal_mask
        )
        source = (atom_rank - partners // block_count) % atom_peers
        slots = source * block_count + partners % block_count
        part_pred = jnp.take(pred_blocks, slots, axis=2)
        part_true = jnp.take(true_blocks, slots, axis=1)
        own_side, part_side = tile_terms(own_pred, own_true, part_pred, part_true, keep_mask)
        return (partners, own_side, part_side)

    slot_limit = jnp.max(pair_count)
    zeros_own = jnp.zeros_like(own_pred)

    def visit_own(slot_index, own_acc):
        partners, own_side, part_side = slot_terms(slot_index)
        return own_acc + own_side

    pair_grad = 2.0 * lax.fori_loop(0, slot_limit, visit_own, zeros_own)
    lddt_grad = total_atoms * PAIR_BLK / pair_total * pair_grad.reshape(samples, 3, atom_rows)
    coord_grad = mse_part - lddt_grad / PAIR_BLK
    return (coord_grad, lddt_grad)


def solution(mesh):
    in_specs = (
        P("atoms", "samples"),
        P("samples", None),
        P("atoms", None),
        P("atoms"),
        P(None, "atoms"),
        P("samples", None, "atoms"),
        P("samples"),
        P(),
        P(),
        P(),
        P(),
        P(),
        P(),
        P(),
        P("atoms", None),
        P("atoms"),
    )
    out_specs = (P("samples", None, "atoms"), P("samples", None, "atoms"))
    return jax.shard_map(
        on_device, mesh=mesh, in_specs=in_specs, out_specs=out_specs, check_vma=False
    )
```

```python
import math

import jax
import jax.numpy as jnp
from jax import lax
from jax.experimental import pallas as pl
from jax.experimental.pallas import tpu as pltpu
from jax.sharding import PartitionSpec as P

HEADS = 4
FF_ATOM = 256
LAYERS = 3
QBLK = 32
KWIN = 128
HALO_TOK = 16
PAIR_BLK = 128


sigma_data = 2.0
norm_epsilon = 1e-05
thresholds = (0.5, 1.0, 2.0, 4.0)


def extended(value, sides, width):
    for axis, dim in sides:
        peers, length = (lax.axis_size(axis), value.shape[dim])
        up = [(i, (i + 1) % peers) for i in range(peers - 1)]
        down = [(j, i) for i, j in up]
        last = lax.slice_in_dim(value, length - width, length, axis=dim)
        first = lax.slice_in_dim(value, 0, width, axis=dim)
        before = lax.ppermute(last, axis, up)
        after = lax.ppermute(first, axis, down)
        value = jnp.concatenate([before, value, after], axis=dim)
    return value


def ring_parts(value, axis):
    peers = lax.axis_size(axis)
    parts = [value]
    for shift in range(1, peers):
        pairs = [(i, (i + shift) % peers) for i in range(peers)]
        parts.append(lax.ppermute(value, axis, pairs))
    return jnp.stack(parts)


def rms_norm(tensor):
    return tensor * lax.rsqrt(jnp.mean(tensor * tensor, axis=-1, keepdims=True) + norm_epsilon)


def window_attend(queries, padded_keys, padded_values, valid):
    samples, atoms, channels = queries.shape
    blocks = atoms // QBLK
    spread = KWIN // QBLK
    head_dim = channels // HEADS

    def windows(source):
        shaped = source.reshape((source.shape[0], blocks + spread - 1, QBLK) + source.shape[2:])
        return jnp.concatenate(
            [shaped[:, shift_index : shift_index + blocks] for shift_index in range(spread)], axis=2
        )

    key_win = windows(padded_keys).reshape(samples, blocks, KWIN, HEADS, head_dim)
    value_win = windows(padded_values).reshape(samples, blocks, KWIN, HEADS, head_dim)
    mask_win = windows(valid[None])
    query_blk = queries.reshape(samples, blocks, QBLK, HEADS, head_dim)
    scores = jnp.einsum(
        "sbqhe,sbkhe->sbhqk", query_blk, key_win, preferred_element_type=jnp.float32
    ) * head_dim ** (-0.5)
    scores = jnp.where(mask_win[:, :, None, None, :], scores, -1e30)
    row_max = jnp.max(scores, axis=-1, keepdims=True)
    exp_scores = jnp.exp(scores - row_max)
    weights = (exp_scores / jnp.sum(exp_scores, axis=-1, keepdims=True)).astype(jnp.bfloat16)
    attended = jnp.einsum(
        "sbhqk,sbkhe->sbqhe", weights, value_win, preferred_element_type=jnp.float32
    )
    return attended.astype(jnp.bfloat16).reshape(samples, atoms, channels)


ROW_CHUNK = 16


def lddt_kernel(slots_ref, count_ref, own_ref, part_ref, out_ref):
    block = pl.program_id(0)
    live = count_ref[block]
    max_slots = slots_ref.shape[0] // count_ref.shape[0]
    lane = lax.broadcasted_iota(jnp.int32, (ROW_CHUNK, PAIR_BLK), 1)
    shape = (ROW_CHUNK, PAIR_BLK)

    def row_body(row_index, carry):
        row = pl.multiple_of(row_index * ROW_CHUNK, ROW_CHUNK)
        own = own_ref[pl.ds(row, ROW_CHUNK), :]
        own_cols = [jnp.broadcast_to(own[:, d : d + 1], shape) for d in range(6)]

        def slot_body(slot_index, accs):
            part = part_ref[slots_ref[block * max_slots + slot_index]]
            gaps = [own_cols[d] - part[d : d + 1, :] for d in range(3)]
            true_gaps = [own_cols[3 + d] - part[3 + d : 4 + d, :] for d in range(3)]
            square_pred = gaps[0] * gaps[0] + gaps[1] * gaps[1] + gaps[2] * gaps[2]
            square_true = (
                true_gaps[0] * true_gaps[0] + true_gaps[1] * true_gaps[1] + true_gaps[2] * true_gaps[2]
            )
            dist_pred = jnp.sqrt(square_pred + 1.0)
            dist_true = jnp.sqrt(square_true + 1.0)
            gap_dist = dist_pred - dist_true
            error_soft = jnp.sqrt(gap_dist * gap_dist + 0.01)
            decay = jnp.exp(-error_soft)
            ys = [decay * math.exp(t) for t in thresholds]
            dens = [(1.0 + y) * (1.0 + y) for y in ys]
            low = dens[0] * dens[1]
            high = dens[2] * dens[3]
            numer = (ys[0] * dens[1] + ys[1] * dens[0]) * high + (ys[2] * dens[3] + ys[3] * dens[2]) * low
            coef = (-0.25 * numer * gap_dist) / (low * high * error_soft * dist_pred)
            return tuple(acc + coef * gap for acc, gap in zip(accs, gaps))

        zero = jnp.zeros(shape, jnp.float32)
        accs = lax.fori_loop(0, live, slot_body, (zero, zero, zero))
        sums = [jnp.sum(acc, axis=1, keepdims=True) for acc in accs]
        tile = jnp.where(lane == 0, sums[0], jnp.where(lane == 1, sums[1], jnp.where(lane == 2, sums[2], 0.0)))
        out_ref[pl.ds(row, ROW_CHUNK), :] = tile
        return carry

    lax.fori_loop(0, PAIR_BLK // ROW_CHUNK, row_body, 0)


def lddt_sums(slots, counts, own_tab, part_tab):
    blocks = counts.shape[0]
    table_rows = part_tab.shape[0]
    out = pl.pallas_call(
        lddt_kernel,
        grid_spec=pltpu.PrefetchScalarGridSpec(
            num_scalar_prefetch=2,
            grid=(blocks,),
            in_specs=[
                pl.BlockSpec((PAIR_BLK, PAIR_BLK), lambda b, *_: (b, 0)),
                pl.BlockSpec((table_rows, 8, PAIR_BLK), lambda b, *_: (0, 0, 0)),
            ],
            out_specs=pl.BlockSpec((PAIR_BLK, PAIR_BLK), lambda b, *_: (b, 0)),
        ),
        out_shape=jax.ShapeDtypeStruct((blocks * PAIR_BLK, PAIR_BLK), jnp.float32),
    )(slots, counts, own_tab, part_tab)
    return out[:, :3].T


def dense(left, right):
    return jnp.einsum("sac,cf->saf", left, right, preferred_element_type=jnp.float32)


def on_device(
    token_feats,
    proj_w,
    atom_single,
    atom_token,
    true_coords,
    noise,
    sigma,
    coord_in,
    w_qkv,
    w_o,
    w_gu,
    w_down,
    gains,
    w_out,
    pair_blocks,
    pair_count,
):
    atom_rank = lax.axis_index("atoms")
    tok_rows = token_feats.shape[0]
    atom_rows = atom_single.shape[0]
    total_atoms = atom_rows * lax.axis_size("atoms")
    samples = noise.shape[0]
    feat_parts = ring_parts(token_feats, "samples")
    proj_parts = ring_parts(proj_w, "samples")
    token_sum = jnp.einsum(
        "kti,kio->to", feat_parts, proj_parts, preferred_element_type=jnp.float32
    )
    token_proj = token_sum.astype(jnp.bfloat16)
    padded_tok = extended(token_proj, (("atoms", 0),), HALO_TOK)
    first_token = atom_rank * tok_rows - HALO_TOK
    relative = atom_token - first_token
    onehot = (
        relative[:, None] == jnp.arange(tok_rows + 2 * HALO_TOK, dtype=jnp.int32)[None, :]
    ).astype(jnp.bfloat16)
    atom_base = atom_single.astype(jnp.float32) + jnp.dot(
        onehot, padded_tok, preferred_element_type=jnp.float32
    )
    sigma_col = sigma[:, None, None]
    noisy = true_coords[None] + sigma_col * noise
    noise_total = sigma_col * sigma_col + sigma_data * sigma_data
    scaled = noisy / jnp.sqrt(noise_total)
    hidden = atom_base[None] + jnp.einsum(
        "sda,dc->sac", scaled, coord_in, precision=lax.Precision.HIGHEST
    )
    key_halo = (KWIN - QBLK) // 2
    position = (
        atom_rank * atom_rows - key_halo + jnp.arange(atom_rows + 2 * key_halo, dtype=jnp.int32)
    )
    valid = (position >= 0) & (position < total_atoms)
    channels = hidden.shape[2]
    for layer_index in range(LAYERS):
        normed = (rms_norm(hidden) * gains[layer_index, 0]).astype(jnp.bfloat16)
        qkv_all = dense(normed, w_qkv[layer_index]).astype(jnp.bfloat16)
        queries = qkv_all[:, :, :channels]
        padded = extended(qkv_all[:, :, channels:], (("atoms", 1),), key_halo)
        attended = window_attend(queries, padded[:, :, :channels], padded[:, :, channels:], valid)
        hidden = hidden + dense(attended, w_o[layer_index])
        normed = (rms_norm(hidden) * gains[layer_index, 1]).astype(jnp.bfloat16)
        gate_up = dense(normed, w_gu[layer_index])
        inner_act = (jax.nn.silu(gate_up[..., :FF_ATOM]) * gate_up[..., FF_ATOM:]).astype(
            jnp.bfloat16
        )
        hidden = hidden + dense(inner_act, w_down[layer_index])
    update = jnp.einsum("sac,cd->sda", rms_norm(hidden), w_out, precision=lax.Precision.HIGHEST)
    predicted = (
        sigma_data * sigma_data / noise_total * noisy
        + sigma_col * sigma_data / jnp.sqrt(noise_total) * update
    )
    mse_part = (
        2.0 / 3.0 * (noise_total / (sigma_col * sigma_data) ** 2) * (predicted - true_coords[None])
    )
    block_count = atom_rows // PAIR_BLK
    atom_peers = lax.axis_size("atoms")
    count_row = jnp.zeros((1, atom_rows), jnp.float32).at[0, 0].set(
        jnp.sum(pair_count.astype(jnp.float32) * (PAIR_BLK * PAIR_BLK) - PAIR_BLK)
    )
    true_parts = ring_parts(jnp.concatenate([true_coords, count_row], axis=0), "atoms")
    pred_parts = ring_parts(predicted[0], "atoms")
    pair_total = jnp.sum(true_parts[:, 3, 0])
    coord_parts = jnp.concatenate(
        [pred_parts, true_parts[:, :3], jnp.zeros((atom_peers, 2, atom_rows), jnp.float32)], axis=1
    )
    part_tab = jnp.moveaxis(
        coord_parts.reshape(atom_peers, 8, block_count, PAIR_BLK), 2, 1
    ).reshape(atom_peers * block_count, 8, PAIR_BLK)
    own_tab = jnp.pad(
        jnp.concatenate([predicted[0], true_coords], axis=0).T, ((0, 0), (0, PAIR_BLK - 6))
    )
    source = (atom_rank - pair_blocks // block_count) % atom_peers
    slots = (source * block_count + pair_blocks % block_count).reshape(-1)
    pair_grad = 2.0 * lddt_sums(slots, pair_count, own_tab, part_tab)[None]
    lddt_grad = total_atoms * PAIR_BLK / pair_total * pair_grad.reshape(samples, 3, atom_rows)
    coord_grad = mse_part - lddt_grad / PAIR_BLK
    return (coord_grad, lddt_grad)


def solution(mesh):
    in_specs = (
        P("atoms", "samples"),
        P("samples", None),
        P("atoms", None),
        P("atoms"),
        P(None, "atoms"),
        P("samples", None, "atoms"),
        P("samples"),
        P(),
        P(),
        P(),
        P(),
        P(),
        P(),
        P(),
        P("atoms", None),
        P("atoms"),
    )
    out_specs = (P("samples", None, "atoms"), P("samples", None, "atoms"))
    return jax.shard_map(
        on_device, mesh=mesh, in_specs=in_specs, out_specs=out_specs, check_vma=False
    )
```

```python
import math

import jax
import jax.numpy as jnp
from jax import lax
from jax.experimental import pallas as pl
from jax.experimental.pallas import tpu as pltpu
from jax.sharding import PartitionSpec as P

HEADS = 4
FF_ATOM = 256
LAYERS = 3
QBLK = 32
KWIN = 128
HALO_TOK = 16
PAIR_BLK = 128


sigma_data = 2.0
norm_epsilon = 1e-05
thresholds = (0.5, 1.0, 2.0, 4.0)


def extended(value, sides, width):
    for axis, dim in sides:
        peers, length = (lax.axis_size(axis), value.shape[dim])
        up = [(i, (i + 1) % peers) for i in range(peers - 1)]
        down = [(j, i) for i, j in up]
        last = lax.slice_in_dim(value, length - width, length, axis=dim)
        first = lax.slice_in_dim(value, 0, width, axis=dim)
        before = lax.ppermute(last, axis, up)
        after = lax.ppermute(first, axis, down)
        value = jnp.concatenate([before, value, after], axis=dim)
    return value


def ring_parts(value, axis):
    peers = lax.axis_size(axis)
    parts = [value]
    for shift in range(1, peers):
        pairs = [(i, (i + shift) % peers) for i in range(peers)]
        parts.append(lax.ppermute(value, axis, pairs))
    return jnp.stack(parts)


def rms_norm(tensor):
    return tensor * lax.rsqrt(jnp.mean(tensor * tensor, axis=-1, keepdims=True) + norm_epsilon)


WIN_GROUP = 8


def attend_kernel(q_ref, kv_ref, mask_ref, out_ref):
    tile = pl.program_id(0)
    head_dim = q_ref.shape[1] // HEADS
    channels = q_ref.shape[1]
    scale = head_dim ** (-0.5)
    pieces = []
    for local in range(WIN_GROUP):
        start = pl.multiple_of(tile * (WIN_GROUP * QBLK) + local * QBLK, QBLK)
        keys_vals = kv_ref[pl.ds(start, KWIN), :]
        live = mask_ref[local : local + 1, :] > 0.0
        query_rows = q_ref[local * QBLK : (local + 1) * QBLK, :]
        heads = []
        for head in range(HEADS):
            cols = slice(head * head_dim, (head + 1) * head_dim)
            vcols = slice(channels + head * head_dim, channels + (head + 1) * head_dim)
            scores = lax.dot_general(
                query_rows[:, cols], keys_vals[:, cols], (((1,), (1,)), ((), ())),
                preferred_element_type=jnp.float32,
            ) * scale
            scores = jnp.where(live, scores, -1e30)
            row_max = jnp.max(scores, axis=-1, keepdims=True)
            exp_scores = jnp.exp(scores - row_max)
            weights = (exp_scores / jnp.sum(exp_scores, axis=-1, keepdims=True)).astype(jnp.bfloat16)
            heads.append(
                jnp.dot(weights, keys_vals[:, vcols], preferred_element_type=jnp.float32).astype(
                    jnp.bfloat16
                )
            )
        pieces.append(jnp.concatenate(heads, axis=1))
    out_ref[...] = jnp.concatenate(pieces, axis=0)


def window_attend(queries, padded_kv, mask_tab):
    atoms, channels = queries.shape
    rows = WIN_GROUP * QBLK
    return pl.pallas_call(
        attend_kernel,
        grid=(atoms // rows,),
        in_specs=[
            pl.BlockSpec((rows, channels), lambda t: (t, 0)),
            pl.BlockSpec(padded_kv.shape, lambda t: (0, 0)),
            pl.BlockSpec((WIN_GROUP, KWIN), lambda t: (t, 0)),
        ],
        out_specs=pl.BlockSpec((rows, channels), lambda t: (t, 0)),
        out_shape=jax.ShapeDtypeStruct((atoms, channels), jnp.bfloat16),
    )(queries, padded_kv, mask_tab)


ROW_CHUNK = 16


def lddt_kernel(slots_ref, count_ref, own_ref, part_ref, out_ref):
    block = pl.program_id(0)
    live = count_ref[block]
    max_slots = slots_ref.shape[0] // count_ref.shape[0]
    lane = lax.broadcasted_iota(jnp.int32, (ROW_CHUNK, PAIR_BLK), 1)
    shape = (ROW_CHUNK, PAIR_BLK)

    def row_body(row_index, carry):
        row = pl.multiple_of(row_index * ROW_CHUNK, ROW_CHUNK)
        own = own_ref[pl.ds(row, ROW_CHUNK), :]
        own_cols = [jnp.broadcast_to(own[:, d : d + 1], shape) for d in range(6)]

        def slot_body(slot_index, accs):
            part = part_ref[slots_ref[block * max_slots + slot_index]]
            gaps = [own_cols[d] - part[d : d + 1, :] for d in range(3)]
            true_gaps = [own_cols[3 + d] - part[3 + d : 4 + d, :] for d in range(3)]
            square_pred = gaps[0] * gaps[0] + gaps[1] * gaps[1] + gaps[2] * gaps[2]
            square_true = (
                true_gaps[0] * true_gaps[0] + true_gaps[1] * true_gaps[1] + true_gaps[2] * true_gaps[2]
            )
            dist_pred = jnp.sqrt(square_pred + 1.0)
            dist_true = jnp.sqrt(square_true + 1.0)
            gap_dist = dist_pred - dist_true
            error_soft = jnp.sqrt(gap_dist * gap_dist + 0.01)
            decay = jnp.exp(-error_soft)
            ys = [decay * math.exp(t) for t in thresholds]
            dens = [(1.0 + y) * (1.0 + y) for y in ys]
            low = dens[0] * dens[1]
            high = dens[2] * dens[3]
            numer = (ys[0] * dens[1] + ys[1] * dens[0]) * high + (ys[2] * dens[3] + ys[3] * dens[2]) * low
            coef = (-0.25 * numer * gap_dist) / (low * high * error_soft * dist_pred)
            return tuple(acc + coef * gap for acc, gap in zip(accs, gaps))

        zero = jnp.zeros(shape, jnp.float32)
        accs = lax.fori_loop(0, live, slot_body, (zero, zero, zero))
        sums = [jnp.sum(acc, axis=1, keepdims=True) for acc in accs]
        tile = jnp.where(lane == 0, sums[0], jnp.where(lane == 1, sums[1], jnp.where(lane == 2, sums[2], 0.0)))
        out_ref[pl.ds(row, ROW_CHUNK), :] = tile
        return carry

    lax.fori_loop(0, PAIR_BLK // ROW_CHUNK, row_body, 0)


def lddt_sums(slots, counts, own_tab, part_tab):
    blocks = counts.shape[0]
    table_rows = part_tab.shape[0]
    out = pl.pallas_call(
        lddt_kernel,
        grid_spec=pltpu.PrefetchScalarGridSpec(
            num_scalar_prefetch=2,
            grid=(blocks,),
            in_specs=[
                pl.BlockSpec((PAIR_BLK, PAIR_BLK), lambda b, *_: (b, 0)),
                pl.BlockSpec((table_rows, 8, PAIR_BLK), lambda b, *_: (0, 0, 0)),
            ],
            out_specs=pl.BlockSpec((PAIR_BLK, PAIR_BLK), lambda b, *_: (b, 0)),
        ),
        out_shape=jax.ShapeDtypeStruct((blocks * PAIR_BLK, PAIR_BLK), jnp.float32),
    )(slots, counts, own_tab, part_tab)
    return out[:, :3].T


def dense(left, right):
    return jnp.einsum("sac,cf->saf", left, right, preferred_element_type=jnp.float32)


def on_device(
    token_feats,
    proj_w,
    atom_single,
    atom_token,
    true_coords,
    noise,
    sigma,
    coord_in,
    w_qkv,
    w_o,
    w_gu,
    w_down,
    gains,
    w_out,
    pair_blocks,
    pair_count,
):
    atom_rank = lax.axis_index("atoms")
    tok_rows = token_feats.shape[0]
    atom_rows = atom_single.shape[0]
    total_atoms = atom_rows * lax.axis_size("atoms")
    samples = noise.shape[0]
    feat_parts = ring_parts(token_feats, "samples")
    proj_parts = ring_parts(proj_w, "samples")
    token_sum = jnp.einsum(
        "kti,kio->to", feat_parts, proj_parts, preferred_element_type=jnp.float32
    )
    token_proj = token_sum.astype(jnp.bfloat16)
    padded_tok = extended(token_proj, (("atoms", 0),), HALO_TOK)
    first_token = atom_rank * tok_rows - HALO_TOK
    relative = atom_token - first_token
    onehot = (
        relative[:, None] == jnp.arange(tok_rows + 2 * HALO_TOK, dtype=jnp.int32)[None, :]
    ).astype(jnp.bfloat16)
    atom_base = atom_single.astype(jnp.float32) + jnp.dot(
        onehot, padded_tok, preferred_element_type=jnp.float32
    )
    sigma_col = sigma[:, None, None]
    noisy = true_coords[None] + sigma_col * noise
    noise_total = sigma_col * sigma_col + sigma_data * sigma_data
    scaled = noisy / jnp.sqrt(noise_total)
    hidden = atom_base[None] + jnp.einsum(
        "sda,dc->sac", scaled, coord_in, precision=lax.Precision.HIGHEST
    )
    key_halo = (KWIN - QBLK) // 2
    position = (
        atom_rank * atom_rows - key_halo + jnp.arange(atom_rows + 2 * key_halo, dtype=jnp.int32)
    )
    valid = ((position >= 0) & (position < total_atoms)).astype(jnp.float32)
    window_start = QBLK * jnp.arange(atom_rows // QBLK, dtype=jnp.int32)
    mask_tab = jnp.take(valid, window_start[:, None] + jnp.arange(KWIN, dtype=jnp.int32)[None, :])
    channels = hidden.shape[2]
    for layer_index in range(LAYERS):
        normed = (rms_norm(hidden) * gains[layer_index, 0]).astype(jnp.bfloat16)
        qkv_all = dense(normed, w_qkv[layer_index]).astype(jnp.bfloat16)
        queries = qkv_all[:, :, :channels]
        padded = extended(qkv_all[:, :, channels:], (("atoms", 1),), key_halo)
        attended = jnp.stack(
            [window_attend(queries[s], padded[s], mask_tab) for s in range(samples)]
        )
        hidden = hidden + dense(attended, w_o[layer_index])
        normed = (rms_norm(hidden) * gains[layer_index, 1]).astype(jnp.bfloat16)
        gate_up = dense(normed, w_gu[layer_index])
        inner_act = (jax.nn.silu(gate_up[..., :FF_ATOM]) * gate_up[..., FF_ATOM:]).astype(
            jnp.bfloat16
        )
        hidden = hidden + dense(inner_act, w_down[layer_index])
    update = jnp.einsum("sac,cd->sda", rms_norm(hidden), w_out, precision=lax.Precision.HIGHEST)
    predicted = (
        sigma_data * sigma_data / noise_total * noisy
        + sigma_col * sigma_data / jnp.sqrt(noise_total) * update
    )
    mse_part = (
        2.0 / 3.0 * (noise_total / (sigma_col * sigma_data) ** 2) * (predicted - true_coords[None])
    )
    block_count = atom_rows // PAIR_BLK
    atom_peers = lax.axis_size("atoms")
    count_row = jnp.zeros((1, atom_rows), jnp.float32).at[0, 0].set(
        jnp.sum(pair_count.astype(jnp.float32) * (PAIR_BLK * PAIR_BLK) - PAIR_BLK)
    )
    true_parts = ring_parts(jnp.concatenate([true_coords, count_row], axis=0), "atoms")
    pred_parts = ring_parts(predicted[0], "atoms")
    pair_total = jnp.sum(true_parts[:, 3, 0])
    coord_parts = jnp.concatenate(
        [pred_parts, true_parts[:, :3], jnp.zeros((atom_peers, 2, atom_rows), jnp.float32)], axis=1
    )
    part_tab = jnp.moveaxis(
        coord_parts.reshape(atom_peers, 8, block_count, PAIR_BLK), 2, 1
    ).reshape(atom_peers * block_count, 8, PAIR_BLK)
    own_tab = jnp.pad(
        jnp.concatenate([predicted[0], true_coords], axis=0).T, ((0, 0), (0, PAIR_BLK - 6))
    )
    source = (atom_rank - pair_blocks // block_count) % atom_peers
    slots = (source * block_count + pair_blocks % block_count).reshape(-1)
    pair_grad = 2.0 * lddt_sums(slots, pair_count, own_tab, part_tab)[None]
    lddt_grad = total_atoms * PAIR_BLK / pair_total * pair_grad.reshape(samples, 3, atom_rows)
    coord_grad = mse_part - lddt_grad / PAIR_BLK
    return (coord_grad, lddt_grad)


def solution(mesh):
    in_specs = (
        P("atoms", "samples"),
        P("samples", None),
        P("atoms", None),
        P("atoms"),
        P(None, "atoms"),
        P("samples", None, "atoms"),
        P("samples"),
        P(),
        P(),
        P(),
        P(),
        P(),
        P(),
        P(),
        P("atoms", None),
        P("atoms"),
    )
    out_specs = (P("samples", None, "atoms"), P("samples", None, "atoms"))
    return jax.shard_map(
        on_device, mesh=mesh, in_specs=in_specs, out_specs=out_specs, check_vma=False
    )
```

```python
import math

import jax
import jax.numpy as jnp
from jax import lax
from jax.experimental import pallas as pl
from jax.experimental.pallas import tpu as pltpu
from jax.sharding import PartitionSpec as P

HEADS = 4
FF_ATOM = 256
LAYERS = 3
QBLK = 32
KWIN = 128
HALO_TOK = 16
PAIR_BLK = 128


sigma_data = 2.0
norm_epsilon = 1e-05
thresholds = (0.5, 1.0, 2.0, 4.0)


def extended(value, sides, width):
    for axis, dim in sides:
        peers, length = (lax.axis_size(axis), value.shape[dim])
        up = [(i, (i + 1) % peers) for i in range(peers - 1)]
        down = [(j, i) for i, j in up]
        last = lax.slice_in_dim(value, length - width, length, axis=dim)
        first = lax.slice_in_dim(value, 0, width, axis=dim)
        before = lax.ppermute(last, axis, up)
        after = lax.ppermute(first, axis, down)
        value = jnp.concatenate([before, value, after], axis=dim)
    return value


def ring_parts(value, axis):
    peers = lax.axis_size(axis)
    parts = [value]
    for shift in range(1, peers):
        pairs = [(i, (i + shift) % peers) for i in range(peers)]
        parts.append(lax.ppermute(value, axis, pairs))
    return jnp.stack(parts)


def rms_norm(tensor):
    return tensor * lax.rsqrt(jnp.mean(tensor * tensor, axis=-1, keepdims=True) + norm_epsilon)


Q_TILE = 128
K_SPAN = 256


def attend_kernel(q_ref, kv_ref, band_ref, valid_ref, out_ref):
    tile = pl.program_id(0)
    head_dim = q_ref.shape[1] // HEADS
    channels = q_ref.shape[1]
    scale = head_dim ** (-0.5)
    start = pl.multiple_of(tile * Q_TILE, Q_TILE)
    keys_vals = kv_ref[pl.ds(start, K_SPAN), :]
    live = (band_ref[...] * valid_ref[pl.ds(tile, 1), :]) > 0.0
    query_rows = q_ref[...]
    heads = []
    for head in range(HEADS):
        cols = slice(head * head_dim, (head + 1) * head_dim)
        vcols = slice(channels + head * head_dim, channels + (head + 1) * head_dim)
        scores = lax.dot_general(
            query_rows[:, cols], keys_vals[:, cols], (((1,), (1,)), ((), ())),
            preferred_element_type=jnp.float32,
        ) * scale
        scores = jnp.where(live, scores, -1e30)
        row_max = jnp.max(scores, axis=-1, keepdims=True)
        exp_scores = jnp.exp(scores - row_max)
        inverse = 1.0 / jnp.sum(exp_scores, axis=-1, keepdims=True)
        weights = (exp_scores * inverse).astype(jnp.bfloat16)
        heads.append(
            jnp.dot(weights, keys_vals[:, vcols], preferred_element_type=jnp.float32).astype(
                jnp.bfloat16
            )
        )
    out_ref[...] = jnp.concatenate(heads, axis=1)


def window_attend(queries, padded_kv, band, valid_tab):
    atoms, channels = queries.shape
    extra = atoms + K_SPAN - Q_TILE - padded_kv.shape[0]
    padded_kv = jnp.pad(padded_kv, ((0, extra), (0, 0)))
    return pl.pallas_call(
        attend_kernel,
        grid=(atoms // Q_TILE,),
        in_specs=[
            pl.BlockSpec((Q_TILE, channels), lambda t: (t, 0)),
            pl.BlockSpec(padded_kv.shape, lambda t: (0, 0)),
            pl.BlockSpec(band.shape, lambda t: (0, 0)),
            pl.BlockSpec(valid_tab.shape, lambda t: (0, 0)),
        ],
        out_specs=pl.BlockSpec((Q_TILE, channels), lambda t: (t, 0)),
        out_shape=jax.ShapeDtypeStruct((atoms, channels), jnp.bfloat16),
    )(queries, padded_kv, band, valid_tab)

ROW_CHUNK = 16


def lddt_kernel(slots_ref, count_ref, own_ref, part_ref, out_ref):
    block = pl.program_id(0)
    live = count_ref[block]
    max_slots = slots_ref.shape[0] // count_ref.shape[0]
    lane = lax.broadcasted_iota(jnp.int32, (ROW_CHUNK, PAIR_BLK), 1)
    shape = (ROW_CHUNK, PAIR_BLK)

    def row_body(row_index, carry):
        row = pl.multiple_of(row_index * ROW_CHUNK, ROW_CHUNK)
        own = own_ref[pl.ds(row, ROW_CHUNK), :]
        own_cols = [jnp.broadcast_to(own[:, d : d + 1], shape) for d in range(6)]

        def slot_body(slot_index, accs):
            part = part_ref[slots_ref[block * max_slots + slot_index]]
            gaps = [own_cols[d] - part[d : d + 1, :] for d in range(3)]
            true_gaps = [own_cols[3 + d] - part[3 + d : 4 + d, :] for d in range(3)]
            square_pred = gaps[0] * gaps[0] + gaps[1] * gaps[1] + gaps[2] * gaps[2]
            square_true = (
                true_gaps[0] * true_gaps[0] + true_gaps[1] * true_gaps[1] + true_gaps[2] * true_gaps[2]
            )
            dist_pred = jnp.sqrt(square_pred + 1.0)
            dist_true = jnp.sqrt(square_true + 1.0)
            gap_dist = dist_pred - dist_true
            error_soft = jnp.sqrt(gap_dist * gap_dist + 0.01)
            decay = jnp.exp(-error_soft)
            ys = [decay * math.exp(t) for t in thresholds]
            dens = [(1.0 + y) * (1.0 + y) for y in ys]
            low = dens[0] * dens[1]
            high = dens[2] * dens[3]
            numer = (ys[0] * dens[1] + ys[1] * dens[0]) * high + (ys[2] * dens[3] + ys[3] * dens[2]) * low
            coef = (-0.25 * numer * gap_dist) / (low * high * error_soft * dist_pred)
            return tuple(acc + coef * gap for acc, gap in zip(accs, gaps))

        zero = jnp.zeros(shape, jnp.float32)
        accs = lax.fori_loop(0, live, slot_body, (zero, zero, zero))
        sums = [jnp.sum(acc, axis=1, keepdims=True) for acc in accs]
        tile = jnp.where(lane == 0, sums[0], jnp.where(lane == 1, sums[1], jnp.where(lane == 2, sums[2], 0.0)))
        out_ref[pl.ds(row, ROW_CHUNK), :] = tile
        return carry

    lax.fori_loop(0, PAIR_BLK // ROW_CHUNK, row_body, 0)


def lddt_sums(slots, counts, own_tab, part_tab):
    blocks = counts.shape[0]
    table_rows = part_tab.shape[0]
    out = pl.pallas_call(
        lddt_kernel,
        grid_spec=pltpu.PrefetchScalarGridSpec(
            num_scalar_prefetch=2,
            grid=(blocks,),
            in_specs=[
                pl.BlockSpec((PAIR_BLK, PAIR_BLK), lambda b, *_: (b, 0)),
                pl.BlockSpec((table_rows, 8, PAIR_BLK), lambda b, *_: (0, 0, 0)),
            ],
            out_specs=pl.BlockSpec((PAIR_BLK, PAIR_BLK), lambda b, *_: (b, 0)),
        ),
        out_shape=jax.ShapeDtypeStruct((blocks * PAIR_BLK, PAIR_BLK), jnp.float32),
    )(slots, counts, own_tab, part_tab)
    return out[:, :3].T


def dense(left, right):
    return jnp.einsum("sac,cf->saf", left, right, preferred_element_type=jnp.float32)


def on_device(
    token_feats,
    proj_w,
    atom_single,
    atom_token,
    true_coords,
    noise,
    sigma,
    coord_in,
    w_qkv,
    w_o,
    w_gu,
    w_down,
    gains,
    w_out,
    pair_blocks,
    pair_count,
):
    atom_rank = lax.axis_index("atoms")
    tok_rows = token_feats.shape[0]
    atom_rows = atom_single.shape[0]
    total_atoms = atom_rows * lax.axis_size("atoms")
    samples = noise.shape[0]
    feat_parts = ring_parts(token_feats, "samples")
    proj_parts = ring_parts(proj_w, "samples")
    token_sum = jnp.einsum(
        "kti,kio->to", feat_parts, proj_parts, preferred_element_type=jnp.float32
    )
    token_proj = token_sum.astype(jnp.bfloat16)
    padded_tok = extended(token_proj, (("atoms", 0),), HALO_TOK)
    first_token = atom_rank * tok_rows - HALO_TOK
    relative = atom_token - first_token
    onehot = (
        relative[:, None] == jnp.arange(tok_rows + 2 * HALO_TOK, dtype=jnp.int32)[None, :]
    ).astype(jnp.bfloat16)
    atom_base = atom_single.astype(jnp.float32) + jnp.dot(
        onehot, padded_tok, preferred_element_type=jnp.float32
    )
    sigma_col = sigma[:, None, None]
    noisy = true_coords[None] + sigma_col * noise
    noise_total = sigma_col * sigma_col + sigma_data * sigma_data
    scaled = noisy / jnp.sqrt(noise_total)
    hidden = atom_base[None] + jnp.einsum(
        "sda,dc->sac", scaled, coord_in, precision=lax.Precision.HIGHEST
    )
    key_halo = (KWIN - QBLK) // 2
    tile_start = atom_rank * atom_rows - key_halo + Q_TILE * jnp.arange(
        atom_rows // Q_TILE, dtype=jnp.int32
    )
    position = tile_start[:, None] + jnp.arange(K_SPAN, dtype=jnp.int32)[None, :]
    valid_tab = ((position >= 0) & (position < total_atoms)).astype(jnp.float32)
    query_win = jnp.arange(Q_TILE, dtype=jnp.int32)[:, None] // QBLK * QBLK
    key_index = jnp.arange(K_SPAN, dtype=jnp.int32)[None, :]
    band = ((key_index >= query_win) & (key_index < query_win + KWIN)).astype(jnp.float32)
    channels = hidden.shape[2]
    for layer_index in range(LAYERS):
        normed = (rms_norm(hidden) * gains[layer_index, 0]).astype(jnp.bfloat16)
        qkv_all = dense(normed, w_qkv[layer_index]).astype(jnp.bfloat16)
        queries = qkv_all[:, :, :channels]
        padded = extended(qkv_all[:, :, channels:], (("atoms", 1),), key_halo)
        attended = jnp.stack(
            [window_attend(queries[s], padded[s], band, valid_tab) for s in range(samples)]
        )
        hidden = hidden + dense(attended, w_o[layer_index])
        normed = (rms_norm(hidden) * gains[layer_index, 1]).astype(jnp.bfloat16)
        gate_up = dense(normed, w_gu[layer_index])
        inner_act = (jax.nn.silu(gate_up[..., :FF_ATOM]) * gate_up[..., FF_ATOM:]).astype(
            jnp.bfloat16
        )
        hidden = hidden + dense(inner_act, w_down[layer_index])
    update = jnp.einsum("sac,cd->sda", rms_norm(hidden), w_out, precision=lax.Precision.HIGHEST)
    predicted = (
        sigma_data * sigma_data / noise_total * noisy
        + sigma_col * sigma_data / jnp.sqrt(noise_total) * update
    )
    mse_part = (
        2.0 / 3.0 * (noise_total / (sigma_col * sigma_data) ** 2) * (predicted - true_coords[None])
    )
    block_count = atom_rows // PAIR_BLK
    atom_peers = lax.axis_size("atoms")
    count_row = jnp.zeros((1, atom_rows), jnp.float32).at[0, 0].set(
        jnp.sum(pair_count.astype(jnp.float32) * (PAIR_BLK * PAIR_BLK) - PAIR_BLK)
    )
    true_parts = ring_parts(jnp.concatenate([true_coords, count_row], axis=0), "atoms")
    pred_parts = ring_parts(predicted[0], "atoms")
    pair_total = jnp.sum(true_parts[:, 3, 0])
    coord_parts = jnp.concatenate(
        [pred_parts, true_parts[:, :3], jnp.zeros((atom_peers, 2, atom_rows), jnp.float32)], axis=1
    )
    part_tab = jnp.moveaxis(
        coord_parts.reshape(atom_peers, 8, block_count, PAIR_BLK), 2, 1
    ).reshape(atom_peers * block_count, 8, PAIR_BLK)
    own_tab = jnp.pad(
        jnp.concatenate([predicted[0], true_coords], axis=0).T, ((0, 0), (0, PAIR_BLK - 6))
    )
    source = (atom_rank - pair_blocks // block_count) % atom_peers
    slots = (source * block_count + pair_blocks % block_count).reshape(-1)
    pair_grad = 2.0 * lddt_sums(slots, pair_count, own_tab, part_tab)[None]
    lddt_grad = total_atoms * PAIR_BLK / pair_total * pair_grad.reshape(samples, 3, atom_rows)
    coord_grad = mse_part - lddt_grad / PAIR_BLK
    return (coord_grad, lddt_grad)


def solution(mesh):
    in_specs = (
        P("atoms", "samples"),
        P("samples", None),
        P("atoms", None),
        P("atoms"),
        P(None, "atoms"),
        P("samples", None, "atoms"),
        P("samples"),
        P(),
        P(),
        P(),
        P(),
        P(),
        P(),
        P(),
        P("atoms", None),
        P("atoms"),
    )
    out_specs = (P("samples", None, "atoms"), P("samples", None, "atoms"))
    return jax.shard_map(
        on_device, mesh=mesh, in_specs=in_specs, out_specs=out_specs, check_vma=False
    )
```

```python
import math

import jax
import jax.numpy as jnp
from jax import lax
from jax.experimental import pallas as pl
from jax.experimental.pallas import tpu as pltpu
from jax.sharding import PartitionSpec as P

HEADS = 4
FF_ATOM = 256
LAYERS = 3
QBLK = 32
KWIN = 128
HALO_TOK = 16
PAIR_BLK = 128


sigma_data = 2.0
norm_epsilon = 1e-05
thresholds = (0.5, 1.0, 2.0, 4.0)


def extended(value, sides, width):
    for axis, dim in sides:
        peers, length = (lax.axis_size(axis), value.shape[dim])
        up = [(i, (i + 1) % peers) for i in range(peers - 1)]
        down = [(j, i) for i, j in up]
        last = lax.slice_in_dim(value, length - width, length, axis=dim)
        first = lax.slice_in_dim(value, 0, width, axis=dim)
        before = lax.ppermute(last, axis, up)
        after = lax.ppermute(first, axis, down)
        value = jnp.concatenate([before, value, after], axis=dim)
    return value


def ring_parts(value, axis):
    peers = lax.axis_size(axis)
    parts = [value]
    for shift in range(1, peers):
        pairs = [(i, (i + shift) % peers) for i in range(peers)]
        parts.append(lax.ppermute(value, axis, pairs))
    return jnp.stack(parts)


def rms_norm(tensor):
    return tensor * lax.rsqrt(jnp.mean(tensor * tensor, axis=-1, keepdims=True) + norm_epsilon)


Q_TILE = 128
K_SPAN = 256


def attend_kernel(q_ref, kv_ref, band_ref, valid_ref, out_ref):
    tile = pl.program_id(0)
    head_dim = q_ref.shape[1] // HEADS
    channels = q_ref.shape[1]
    scale = head_dim ** (-0.5)
    start = pl.multiple_of(tile * Q_TILE, Q_TILE)
    keys_vals = kv_ref[pl.ds(start, K_SPAN), :]
    live = (band_ref[...] * valid_ref[pl.ds(tile, 1), :]) > 0.0
    query_rows = q_ref[...]
    heads = []
    for head in range(HEADS):
        cols = slice(head * head_dim, (head + 1) * head_dim)
        vcols = slice(channels + head * head_dim, channels + (head + 1) * head_dim)
        scores = lax.dot_general(
            query_rows[:, cols], keys_vals[:, cols], (((1,), (1,)), ((), ())),
            preferred_element_type=jnp.float32,
        ) * scale
        scores = jnp.where(live, scores, -1e30)
        row_max = jnp.max(scores, axis=-1, keepdims=True)
        exp_scores = jnp.exp(scores - row_max)
        inverse = 1.0 / jnp.sum(exp_scores, axis=-1, keepdims=True)
        weights = (exp_scores * inverse).astype(jnp.bfloat16)
        heads.append(
            jnp.dot(weights, keys_vals[:, vcols], preferred_element_type=jnp.float32).astype(
                jnp.bfloat16
            )
        )
    out_ref[...] = jnp.concatenate(heads, axis=1)


def window_attend(queries, padded_kv, band, valid_tab):
    atoms, channels = queries.shape
    extra = atoms + K_SPAN - Q_TILE - padded_kv.shape[0]
    padded_kv = jnp.pad(padded_kv, ((0, extra), (0, 0)))
    return pl.pallas_call(
        attend_kernel,
        grid=(atoms // Q_TILE,),
        in_specs=[
            pl.BlockSpec((Q_TILE, channels), lambda t: (t, 0)),
            pl.BlockSpec(padded_kv.shape, lambda t: (0, 0)),
            pl.BlockSpec(band.shape, lambda t: (0, 0)),
            pl.BlockSpec(valid_tab.shape, lambda t: (0, 0)),
        ],
        out_specs=pl.BlockSpec((Q_TILE, channels), lambda t: (t, 0)),
        out_shape=jax.ShapeDtypeStruct((atoms, channels), jnp.bfloat16),
    )(queries, padded_kv, band, valid_tab)

ROW_CHUNK = 32


def lddt_kernel(slots_ref, count_ref, own_ref, part_ref, out_ref, cols_ref):
    block = pl.program_id(0)
    live = count_ref[block]
    max_slots = slots_ref.shape[0] // count_ref.shape[0]
    shape = (ROW_CHUNK, PAIR_BLK)
    lane = lax.broadcasted_iota(jnp.int32, shape, 1)
    for chunk in range(PAIR_BLK // ROW_CHUNK):
        rows = slice(chunk * ROW_CHUNK, (chunk + 1) * ROW_CHUNK)
        own = own_ref[rows, :]
        for d in range(6):
            cols_ref[d, rows, :] = jnp.broadcast_to(own[:, d : d + 1], shape)

    def row_body(row_index, carry):
        row = pl.multiple_of(row_index * ROW_CHUNK, ROW_CHUNK)

        def slot_body(slot_index, accs):
            part = part_ref[slots_ref[block * max_slots + slot_index]]
            gaps = [cols_ref[d, pl.ds(row, ROW_CHUNK), :] - part[d : d + 1, :] for d in range(3)]
            true_gaps = [
                cols_ref[3 + d, pl.ds(row, ROW_CHUNK), :] - part[3 + d : 4 + d, :] for d in range(3)
            ]
            square_pred = gaps[0] * gaps[0] + gaps[1] * gaps[1] + gaps[2] * gaps[2] + 1.0
            square_true = (
                true_gaps[0] * true_gaps[0] + true_gaps[1] * true_gaps[1] + true_gaps[2] * true_gaps[2]
            ) + 1.0
            inv_pred = lax.rsqrt(square_pred)
            gap_dist = square_pred * inv_pred - square_true * lax.rsqrt(square_true)
            square_err = gap_dist * gap_dist + 0.01
            inv_err = lax.rsqrt(square_err)
            decay = jnp.exp(-(square_err * inv_err))
            ys = [decay * math.exp(t) for t in thresholds]
            dens = [(1.0 + y) * (1.0 + y) for y in ys]
            low = dens[0] * dens[1]
            high = dens[2] * dens[3]
            numer = (ys[0] * dens[1] + ys[1] * dens[0]) * high + (ys[2] * dens[3] + ys[3] * dens[2]) * low
            coef = (-0.25 * numer * gap_dist * (inv_err * inv_pred)) / (low * high)
            return tuple(acc + coef * gap for acc, gap in zip(accs, gaps))

        zero = jnp.zeros(shape, jnp.float32)
        accs = lax.fori_loop(0, live, slot_body, (zero, zero, zero))
        sums = [jnp.sum(acc, axis=1, keepdims=True) for acc in accs]
        tile = jnp.where(lane == 0, sums[0], jnp.where(lane == 1, sums[1], jnp.where(lane == 2, sums[2], 0.0)))
        out_ref[pl.ds(row, ROW_CHUNK), :] = tile
        return carry

    lax.fori_loop(0, PAIR_BLK // ROW_CHUNK, row_body, 0)


def lddt_sums(slots, counts, own_tab, part_tab):
    blocks = counts.shape[0]
    table_rows = part_tab.shape[0]
    out = pl.pallas_call(
        lddt_kernel,
        grid_spec=pltpu.PrefetchScalarGridSpec(
            num_scalar_prefetch=2,
            grid=(blocks,),
            in_specs=[
                pl.BlockSpec((PAIR_BLK, PAIR_BLK), lambda b, *_: (b, 0)),
                pl.BlockSpec((table_rows, 8, PAIR_BLK), lambda b, *_: (0, 0, 0)),
            ],
            out_specs=pl.BlockSpec((PAIR_BLK, PAIR_BLK), lambda b, *_: (b, 0)),
            scratch_shapes=[pltpu.VMEM((6, PAIR_BLK, PAIR_BLK), jnp.float32)],
        ),
        out_shape=jax.ShapeDtypeStruct((blocks * PAIR_BLK, PAIR_BLK), jnp.float32),
    )(slots, counts, own_tab, part_tab)
    return out[:, :3].T


def dense(left, right):
    return jnp.einsum("sac,cf->saf", left, right, preferred_element_type=jnp.float32)


def on_device(
    token_feats,
    proj_w,
    atom_single,
    atom_token,
    true_coords,
    noise,
    sigma,
    coord_in,
    w_qkv,
    w_o,
    w_gu,
    w_down,
    gains,
    w_out,
    pair_blocks,
    pair_count,
):
    atom_rank = lax.axis_index("atoms")
    tok_rows = token_feats.shape[0]
    atom_rows = atom_single.shape[0]
    total_atoms = atom_rows * lax.axis_size("atoms")
    samples = noise.shape[0]
    feat_parts = ring_parts(token_feats, "samples")
    proj_parts = ring_parts(proj_w, "samples")
    token_sum = jnp.einsum(
        "kti,kio->to", feat_parts, proj_parts, preferred_element_type=jnp.float32
    )
    token_proj = token_sum.astype(jnp.bfloat16)
    padded_tok = extended(token_proj, (("atoms", 0),), HALO_TOK)
    first_token = atom_rank * tok_rows - HALO_TOK
    relative = atom_token - first_token
    onehot = (
        relative[:, None] == jnp.arange(tok_rows + 2 * HALO_TOK, dtype=jnp.int32)[None, :]
    ).astype(jnp.bfloat16)
    atom_base = atom_single.astype(jnp.float32) + jnp.dot(
        onehot, padded_tok, preferred_element_type=jnp.float32
    )
    sigma_col = sigma[:, None, None]
    noisy = true_coords[None] + sigma_col * noise
    noise_total = sigma_col * sigma_col + sigma_data * sigma_data
    scaled = noisy / jnp.sqrt(noise_total)
    hidden = atom_base[None] + jnp.einsum(
        "sda,dc->sac", scaled, coord_in, precision=lax.Precision.HIGHEST
    )
    key_halo = (KWIN - QBLK) // 2
    tile_start = atom_rank * atom_rows - key_halo + Q_TILE * jnp.arange(
        atom_rows // Q_TILE, dtype=jnp.int32
    )
    position = tile_start[:, None] + jnp.arange(K_SPAN, dtype=jnp.int32)[None, :]
    valid_tab = ((position >= 0) & (position < total_atoms)).astype(jnp.float32)
    query_win = jnp.arange(Q_TILE, dtype=jnp.int32)[:, None] // QBLK * QBLK
    key_index = jnp.arange(K_SPAN, dtype=jnp.int32)[None, :]
    band = ((key_index >= query_win) & (key_index < query_win + KWIN)).astype(jnp.float32)
    channels = hidden.shape[2]
    for layer_index in range(LAYERS):
        normed = (rms_norm(hidden) * gains[layer_index, 0]).astype(jnp.bfloat16)
        qkv_all = dense(normed, w_qkv[layer_index]).astype(jnp.bfloat16)
        queries = qkv_all[:, :, :channels]
        padded = extended(qkv_all[:, :, channels:], (("atoms", 1),), key_halo)
        attended = jnp.stack(
            [window_attend(queries[s], padded[s], band, valid_tab) for s in range(samples)]
        )
        hidden = hidden + dense(attended, w_o[layer_index])
        normed = (rms_norm(hidden) * gains[layer_index, 1]).astype(jnp.bfloat16)
        gate_up = dense(normed, w_gu[layer_index])
        inner_act = (jax.nn.silu(gate_up[..., :FF_ATOM]) * gate_up[..., FF_ATOM:]).astype(
            jnp.bfloat16
        )
        hidden = hidden + dense(inner_act, w_down[layer_index])
    update = jnp.einsum("sac,cd->sda", rms_norm(hidden), w_out, precision=lax.Precision.HIGHEST)
    predicted = (
        sigma_data * sigma_data / noise_total * noisy
        + sigma_col * sigma_data / jnp.sqrt(noise_total) * update
    )
    mse_part = (
        2.0 / 3.0 * (noise_total / (sigma_col * sigma_data) ** 2) * (predicted - true_coords[None])
    )
    block_count = atom_rows // PAIR_BLK
    atom_peers = lax.axis_size("atoms")
    count_row = jnp.zeros((1, atom_rows), jnp.float32).at[0, 0].set(
        jnp.sum(pair_count.astype(jnp.float32) * (PAIR_BLK * PAIR_BLK) - PAIR_BLK)
    )
    true_parts = ring_parts(jnp.concatenate([true_coords, count_row], axis=0), "atoms")
    pred_parts = ring_parts(predicted[0], "atoms")
    pair_total = jnp.sum(true_parts[:, 3, 0])
    coord_parts = jnp.concatenate(
        [pred_parts, true_parts[:, :3], jnp.zeros((atom_peers, 2, atom_rows), jnp.float32)], axis=1
    )
    part_tab = jnp.moveaxis(
        coord_parts.reshape(atom_peers, 8, block_count, PAIR_BLK), 2, 1
    ).reshape(atom_peers * block_count, 8, PAIR_BLK)
    own_tab = jnp.pad(
        jnp.concatenate([predicted[0], true_coords], axis=0).T, ((0, 0), (0, PAIR_BLK - 6))
    )
    source = (atom_rank - pair_blocks // block_count) % atom_peers
    slots = (source * block_count + pair_blocks % block_count).reshape(-1)
    pair_grad = 2.0 * lddt_sums(slots, pair_count, own_tab, part_tab)[None]
    lddt_grad = total_atoms * PAIR_BLK / pair_total * pair_grad.reshape(samples, 3, atom_rows)
    coord_grad = mse_part - lddt_grad / PAIR_BLK
    return (coord_grad, lddt_grad)


def solution(mesh):
    in_specs = (
        P("atoms", "samples"),
        P("samples", None),
        P("atoms", None),
        P("atoms"),
        P(None, "atoms"),
        P("samples", None, "atoms"),
        P("samples"),
        P(),
        P(),
        P(),
        P(),
        P(),
        P(),
        P(),
        P("atoms", None),
        P("atoms"),
    )
    out_specs = (P("samples", None, "atoms"), P("samples", None, "atoms"))
    return jax.shard_map(
        on_device, mesh=mesh, in_specs=in_specs, out_specs=out_specs, check_vma=False
    )
```

```python
import math

import jax
import jax.numpy as jnp
from jax import lax
from jax.experimental import pallas as pl
from jax.experimental.pallas import tpu as pltpu
from jax.sharding import PartitionSpec as P

HEADS = 4
FF_ATOM = 256
LAYERS = 3
QBLK = 32
KWIN = 128
HALO_TOK = 16
PAIR_BLK = 128


sigma_data = 2.0
norm_epsilon = 1e-05
thresholds = (0.5, 1.0, 2.0, 4.0)


def extended(value, sides, width):
    for axis, dim in sides:
        peers, length = (lax.axis_size(axis), value.shape[dim])
        up = [(i, (i + 1) % peers) for i in range(peers - 1)]
        down = [(j, i) for i, j in up]
        last = lax.slice_in_dim(value, length - width, length, axis=dim)
        first = lax.slice_in_dim(value, 0, width, axis=dim)
        before = lax.ppermute(last, axis, up)
        after = lax.ppermute(first, axis, down)
        value = jnp.concatenate([before, value, after], axis=dim)
    return value


def ring_parts(value, axis):
    peers = lax.axis_size(axis)
    parts = value[None]
    span = 1
    while span < peers and peers % (2 * span) == 0:
        pairs = [(i, (i + span) % peers) for i in range(peers)]
        parts = jnp.concatenate([parts, lax.ppermute(parts, axis, pairs)])
        span *= 2
    if span < peers:
        extra = [value[None]]
        for shift in range(span, peers):
            pairs = [(i, (i + shift) % peers) for i in range(peers)]
            extra.append(lax.ppermute(value, axis, pairs)[None])
        parts = jnp.concatenate([parts] + extra[1:])
    return parts

def rms_norm(tensor):
    return tensor * lax.rsqrt(jnp.mean(tensor * tensor, axis=-1, keepdims=True) + norm_epsilon)


Q_TILE = 128
K_SPAN = 256


def attend_kernel(q_ref, kv_ref, band_ref, valid_ref, out_ref):
    tile = pl.program_id(0)
    head_dim = q_ref.shape[1] // HEADS
    channels = q_ref.shape[1]
    scale = head_dim ** (-0.5)
    start = pl.multiple_of(tile * Q_TILE, Q_TILE)
    keys_vals = kv_ref[pl.ds(start, K_SPAN), :]
    live = (band_ref[...] * valid_ref[pl.ds(tile, 1), :]) > 0.0
    query_rows = q_ref[...]
    heads = []
    for head in range(HEADS):
        cols = slice(head * head_dim, (head + 1) * head_dim)
        vcols = slice(channels + head * head_dim, channels + (head + 1) * head_dim)
        scores = lax.dot_general(
            query_rows[:, cols], keys_vals[:, cols], (((1,), (1,)), ((), ())),
            preferred_element_type=jnp.float32,
        ) * scale
        scores = jnp.where(live, scores, -1e30)
        row_max = jnp.max(scores, axis=-1, keepdims=True)
        exp_scores = jnp.exp(scores - row_max)
        inverse = 1.0 / jnp.sum(exp_scores, axis=-1, keepdims=True)
        weights = (exp_scores * inverse).astype(jnp.bfloat16)
        heads.append(
            jnp.dot(weights, keys_vals[:, vcols], preferred_element_type=jnp.float32).astype(
                jnp.bfloat16
            )
        )
    out_ref[...] = jnp.concatenate(heads, axis=1)


def window_attend(queries, padded_kv, band, valid_tab):
    atoms, channels = queries.shape
    extra = atoms + K_SPAN - Q_TILE - padded_kv.shape[0]
    padded_kv = jnp.pad(padded_kv, ((0, extra), (0, 0)))
    return pl.pallas_call(
        attend_kernel,
        grid=(atoms // Q_TILE,),
        in_specs=[
            pl.BlockSpec((Q_TILE, channels), lambda t: (t, 0)),
            pl.BlockSpec(padded_kv.shape, lambda t: (0, 0)),
            pl.BlockSpec(band.shape, lambda t: (0, 0)),
            pl.BlockSpec(valid_tab.shape, lambda t: (0, 0)),
        ],
        out_specs=pl.BlockSpec((Q_TILE, channels), lambda t: (t, 0)),
        out_shape=jax.ShapeDtypeStruct((atoms, channels), jnp.bfloat16),
    )(queries, padded_kv, band, valid_tab)

ROW_CHUNK = 32


def lddt_kernel(slots_ref, count_ref, own_ref, pred_ref, true_ref, out_ref, cols_ref):
    block = pl.program_id(0)
    live = count_ref[block]
    blocks = count_ref.shape[0]
    max_slots = slots_ref.shape[0] // blocks
    shape = (ROW_CHUNK, PAIR_BLK)
    lane = lax.broadcasted_iota(jnp.int32, shape, 1)
    for chunk in range(PAIR_BLK // ROW_CHUNK):
        rows = slice(chunk * ROW_CHUNK, (chunk + 1) * ROW_CHUNK)
        own = own_ref[rows, :]
        for d in range(6):
            cols_ref[d, rows, :] = jnp.broadcast_to(own[:, d : d + 1], shape)

    def row_body(row_index, carry):
        row = pl.multiple_of(row_index * ROW_CHUNK, ROW_CHUNK)

        def slot_body(slot_index, accs):
            slot = slots_ref[block * max_slots + slot_index]
            peer = slot // blocks
            start = pl.multiple_of((slot % blocks) * PAIR_BLK, PAIR_BLK)
            part_pred = pred_ref[peer, :, pl.ds(start, PAIR_BLK)]
            part_true = true_ref[peer, :, pl.ds(start, PAIR_BLK)]
            gaps = [cols_ref[d, pl.ds(row, ROW_CHUNK), :] - part_pred[d : d + 1, :] for d in range(3)]
            true_gaps = [
                cols_ref[3 + d, pl.ds(row, ROW_CHUNK), :] - part_true[d : d + 1, :] for d in range(3)
            ]
            square_pred = gaps[0] * gaps[0] + gaps[1] * gaps[1] + gaps[2] * gaps[2] + 1.0
            square_true = (
                true_gaps[0] * true_gaps[0] + true_gaps[1] * true_gaps[1] + true_gaps[2] * true_gaps[2]
            ) + 1.0
            inv_pred = lax.rsqrt(square_pred)
            gap_dist = square_pred * inv_pred - square_true * lax.rsqrt(square_true)
            square_err = gap_dist * gap_dist + 0.01
            inv_err = lax.rsqrt(square_err)
            decay = jnp.exp(-(square_err * inv_err))
            ys = [decay * math.exp(t) for t in thresholds]
            dens = [(1.0 + y) * (1.0 + y) for y in ys]
            low = dens[0] * dens[1]
            high = dens[2] * dens[3]
            numer = (ys[0] * dens[1] + ys[1] * dens[0]) * high + (ys[2] * dens[3] + ys[3] * dens[2]) * low
            coef = (-0.25 * numer * gap_dist * (inv_err * inv_pred)) / (low * high)
            return tuple(acc + coef * gap for acc, gap in zip(accs, gaps))

        zero = jnp.zeros(shape, jnp.float32)
        accs = lax.fori_loop(0, live, slot_body, (zero, zero, zero))
        sums = [jnp.sum(acc, axis=1, keepdims=True) for acc in accs]
        tile = jnp.where(lane == 0, sums[0], jnp.where(lane == 1, sums[1], jnp.where(lane == 2, sums[2], 0.0)))
        out_ref[pl.ds(row, ROW_CHUNK), :] = tile
        return carry

    lax.fori_loop(0, PAIR_BLK // ROW_CHUNK, row_body, 0)


def lddt_sums(slots, counts, own_tab, pred_parts, true_parts):
    blocks = counts.shape[0]
    out = pl.pallas_call(
        lddt_kernel,
        grid_spec=pltpu.PrefetchScalarGridSpec(
            num_scalar_prefetch=2,
            grid=(blocks,),
            in_specs=[
                pl.BlockSpec((PAIR_BLK, own_tab.shape[1]), lambda b, *_: (b, 0)),
                pl.BlockSpec(pred_parts.shape, lambda b, *_: (0, 0, 0)),
                pl.BlockSpec(true_parts.shape, lambda b, *_: (0, 0, 0)),
            ],
            out_specs=pl.BlockSpec((PAIR_BLK, PAIR_BLK), lambda b, *_: (b, 0)),
            scratch_shapes=[pltpu.VMEM((6, PAIR_BLK, PAIR_BLK), jnp.float32)],
        ),
        out_shape=jax.ShapeDtypeStruct((blocks * PAIR_BLK, PAIR_BLK), jnp.float32),
    )(slots, counts, own_tab, pred_parts, true_parts)
    return out[:, :3].T

def dense(left, right):
    return jnp.einsum("sac,cf->saf", left, right, preferred_element_type=jnp.float32)


def on_device(
    token_feats,
    proj_w,
    atom_single,
    atom_token,
    true_coords,
    noise,
    sigma,
    coord_in,
    w_qkv,
    w_o,
    w_gu,
    w_down,
    gains,
    w_out,
    pair_blocks,
    pair_count,
):
    atom_rank = lax.axis_index("atoms")
    tok_rows = token_feats.shape[0]
    atom_rows = atom_single.shape[0]
    total_atoms = atom_rows * lax.axis_size("atoms")
    samples = noise.shape[0]
    feat_parts = ring_parts(token_feats, "samples")
    proj_parts = ring_parts(proj_w, "samples")
    token_sum = jnp.einsum(
        "kti,kio->to", feat_parts, proj_parts, preferred_element_type=jnp.float32
    )
    token_proj = token_sum.astype(jnp.bfloat16)
    padded_tok = extended(token_proj, (("atoms", 0),), HALO_TOK)
    first_token = atom_rank * tok_rows - HALO_TOK
    relative = atom_token - first_token
    onehot = (
        relative[:, None] == jnp.arange(tok_rows + 2 * HALO_TOK, dtype=jnp.int32)[None, :]
    ).astype(jnp.bfloat16)
    atom_base = atom_single.astype(jnp.float32) + jnp.dot(
        onehot, padded_tok, preferred_element_type=jnp.float32
    )
    sigma_col = sigma[:, None, None]
    noisy = true_coords[None] + sigma_col * noise
    noise_total = sigma_col * sigma_col + sigma_data * sigma_data
    scaled = noisy / jnp.sqrt(noise_total)
    hidden = atom_base[None] + jnp.einsum(
        "sda,dc->sac", scaled, coord_in, precision=lax.Precision.HIGHEST
    )
    key_halo = (KWIN - QBLK) // 2
    tile_start = atom_rank * atom_rows - key_halo + Q_TILE * jnp.arange(
        atom_rows // Q_TILE, dtype=jnp.int32
    )
    position = tile_start[:, None] + jnp.arange(K_SPAN, dtype=jnp.int32)[None, :]
    valid_tab = ((position >= 0) & (position < total_atoms)).astype(jnp.float32)
    query_win = jnp.arange(Q_TILE, dtype=jnp.int32)[:, None] // QBLK * QBLK
    key_index = jnp.arange(K_SPAN, dtype=jnp.int32)[None, :]
    band = ((key_index >= query_win) & (key_index < query_win + KWIN)).astype(jnp.float32)
    channels = hidden.shape[2]
    for layer_index in range(LAYERS):
        normed = (rms_norm(hidden) * gains[layer_index, 0]).astype(jnp.bfloat16)
        qkv_all = dense(normed, w_qkv[layer_index]).astype(jnp.bfloat16)
        queries = qkv_all[:, :, :channels]
        padded = extended(qkv_all[:, :, channels:], (("atoms", 1),), key_halo)
        attended = jnp.stack(
            [window_attend(queries[s], padded[s], band, valid_tab) for s in range(samples)]
        )
        hidden = hidden + dense(attended, w_o[layer_index])
        normed = (rms_norm(hidden) * gains[layer_index, 1]).astype(jnp.bfloat16)
        gate_up = dense(normed, w_gu[layer_index])
        inner_act = (jax.nn.silu(gate_up[..., :FF_ATOM]) * gate_up[..., FF_ATOM:]).astype(
            jnp.bfloat16
        )
        hidden = hidden + dense(inner_act, w_down[layer_index])
    update = jnp.einsum("sac,cd->sda", rms_norm(hidden), w_out, precision=lax.Precision.HIGHEST)
    predicted = (
        sigma_data * sigma_data / noise_total * noisy
        + sigma_col * sigma_data / jnp.sqrt(noise_total) * update
    )
    mse_part = (
        2.0 / 3.0 * (noise_total / (sigma_col * sigma_data) ** 2) * (predicted - true_coords[None])
    )
    block_count = atom_rows // PAIR_BLK
    atom_peers = lax.axis_size("atoms")
    count_row = jnp.zeros((1, atom_rows), jnp.float32).at[0, 0].set(
        jnp.sum(pair_count.astype(jnp.float32) * (PAIR_BLK * PAIR_BLK) - PAIR_BLK)
    )
    true_parts = ring_parts(jnp.concatenate([true_coords, count_row], axis=0), "atoms")
    pred_parts = ring_parts(predicted[0], "atoms")
    pair_total = jnp.sum(true_parts[:, 3, 0])
    own_tab = jnp.concatenate(
        [predicted[0], true_coords, jnp.zeros((2, atom_rows), jnp.float32)], axis=0
    ).T
    source = (atom_rank - pair_blocks // block_count) % atom_peers
    slots = (source * block_count + pair_blocks % block_count).reshape(-1)
    pair_grad = 2.0 * lddt_sums(slots, pair_count, own_tab, pred_parts, true_parts)[None]
    lddt_grad = total_atoms * PAIR_BLK / pair_total * pair_grad.reshape(samples, 3, atom_rows)
    coord_grad = mse_part - lddt_grad / PAIR_BLK
    return (coord_grad, lddt_grad)


def solution(mesh):
    in_specs = (
        P("atoms", "samples"),
        P("samples", None),
        P("atoms", None),
        P("atoms"),
        P(None, "atoms"),
        P("samples", None, "atoms"),
        P("samples"),
        P(),
        P(),
        P(),
        P(),
        P(),
        P(),
        P(),
        P("atoms", None),
        P("atoms"),
    )
    out_specs = (P("samples", None, "atoms"), P("samples", None, "atoms"))
    return jax.shard_map(
        on_device, mesh=mesh, in_specs=in_specs, out_specs=out_specs, check_vma=False
    )
```

```python
import math

import jax
import jax.numpy as jnp
from jax import lax
from jax.experimental import pallas as pl
from jax.experimental.pallas import tpu as pltpu
from jax.sharding import PartitionSpec as P

HEADS = 4
FF_ATOM = 256
LAYERS = 3
QBLK = 32
KWIN = 128
HALO_TOK = 16
PAIR_BLK = 128


sigma_data = 2.0
norm_epsilon = 1e-05
thresholds = (0.5, 1.0, 2.0, 4.0)


def extended(value, sides, width):
    for axis, dim in sides:
        peers, length = (lax.axis_size(axis), value.shape[dim])
        up = [(i, (i + 1) % peers) for i in range(peers - 1)]
        down = [(j, i) for i, j in up]
        last = lax.slice_in_dim(value, length - width, length, axis=dim)
        first = lax.slice_in_dim(value, 0, width, axis=dim)
        before = lax.ppermute(last, axis, up)
        after = lax.ppermute(first, axis, down)
        value = jnp.concatenate([before, value, after], axis=dim)
    return value


def ring_parts(value, axis):
    peers = lax.axis_size(axis)
    parts = value[None]
    span = 1
    while span < peers and peers % (2 * span) == 0:
        pairs = [(i, (i + span) % peers) for i in range(peers)]
        parts = jnp.concatenate([parts, lax.ppermute(parts, axis, pairs)])
        span *= 2
    if span < peers:
        extra = [value[None]]
        for shift in range(span, peers):
            pairs = [(i, (i + shift) % peers) for i in range(peers)]
            extra.append(lax.ppermute(value, axis, pairs)[None])
        parts = jnp.concatenate([parts] + extra[1:])
    return parts

def rms_norm(tensor):
    return tensor * lax.rsqrt(jnp.mean(tensor * tensor, axis=-1, keepdims=True) + norm_epsilon)


Q_TILE = 128
K_SPAN = 256


def attend_kernel(q_ref, kv_ref, band_ref, valid_ref, out_ref):
    tile = pl.program_id(0)
    head_dim = q_ref.shape[1] // HEADS
    channels = q_ref.shape[1]
    scale = head_dim ** (-0.5)
    start = pl.multiple_of(tile * Q_TILE, Q_TILE)
    keys_vals = kv_ref[pl.ds(start, K_SPAN), :]
    live = (band_ref[...] * valid_ref[pl.ds(tile, 1), :]) > 0.0
    query_rows = q_ref[...]
    heads = []
    for head in range(HEADS):
        cols = slice(head * head_dim, (head + 1) * head_dim)
        vcols = slice(channels + head * head_dim, channels + (head + 1) * head_dim)
        scores = lax.dot_general(
            query_rows[:, cols], keys_vals[:, cols], (((1,), (1,)), ((), ())),
            preferred_element_type=jnp.float32,
        )
        scores = jnp.where(live, scores, -1e30)
        row_max = jnp.max(scores, axis=-1, keepdims=True)
        exp_scores = jnp.exp2((scores - row_max) * (scale * math.log2(math.e)))
        inverse = 1.0 / jnp.sum(exp_scores, axis=-1, keepdims=True)
        weights = (exp_scores * inverse).astype(jnp.bfloat16)
        heads.append(
            jnp.dot(weights, keys_vals[:, vcols], preferred_element_type=jnp.float32).astype(
                jnp.bfloat16
            )
        )
    out_ref[...] = jnp.concatenate(heads, axis=1)


def window_attend(queries, padded_kv, band, valid_tab):
    atoms, channels = queries.shape
    extra = atoms + K_SPAN - Q_TILE - padded_kv.shape[0]
    padded_kv = jnp.pad(padded_kv, ((0, extra), (0, 0)))
    return pl.pallas_call(
        attend_kernel,
        grid=(atoms // Q_TILE,),
        in_specs=[
            pl.BlockSpec((Q_TILE, channels), lambda t: (t, 0)),
            pl.BlockSpec(padded_kv.shape, lambda t: (0, 0)),
            pl.BlockSpec(band.shape, lambda t: (0, 0)),
            pl.BlockSpec(valid_tab.shape, lambda t: (0, 0)),
        ],
        out_specs=pl.BlockSpec((Q_TILE, channels), lambda t: (t, 0)),
        out_shape=jax.ShapeDtypeStruct((atoms, channels), jnp.bfloat16),
    )(queries, padded_kv, band, valid_tab)

ROW_CHUNK = 64


def lddt_kernel(slots_ref, count_ref, own_ref, pred_ref, true_ref, out_ref, cols_ref):
    block = pl.program_id(0)
    live = count_ref[block]
    blocks = count_ref.shape[0]
    max_slots = slots_ref.shape[0] // blocks
    shape = (ROW_CHUNK, PAIR_BLK)
    lane = lax.broadcasted_iota(jnp.int32, shape, 1)
    for chunk in range(PAIR_BLK // ROW_CHUNK):
        rows = slice(chunk * ROW_CHUNK, (chunk + 1) * ROW_CHUNK)
        own = own_ref[rows, :]
        for d in range(6):
            cols_ref[d, rows, :] = jnp.broadcast_to(own[:, d : d + 1], shape)

    def row_body(row_index, carry):
        row = pl.multiple_of(row_index * ROW_CHUNK, ROW_CHUNK)

        def slot_body(slot_index, accs):
            slot = slots_ref[block * max_slots + slot_index]
            peer = slot // blocks
            start = pl.multiple_of((slot % blocks) * PAIR_BLK, PAIR_BLK)
            part_pred = pred_ref[peer, :, pl.ds(start, PAIR_BLK)]
            part_true = true_ref[peer, :, pl.ds(start, PAIR_BLK)]
            gaps = [cols_ref[d, pl.ds(row, ROW_CHUNK), :] - part_pred[d : d + 1, :] for d in range(3)]
            true_gaps = [
                cols_ref[3 + d, pl.ds(row, ROW_CHUNK), :] - part_true[d : d + 1, :] for d in range(3)
            ]
            square_pred = gaps[0] * gaps[0] + gaps[1] * gaps[1] + gaps[2] * gaps[2] + 1.0
            square_true = (
                true_gaps[0] * true_gaps[0] + true_gaps[1] * true_gaps[1] + true_gaps[2] * true_gaps[2]
            ) + 1.0
            inv_pred = lax.rsqrt(square_pred)
            gap_dist = square_pred * inv_pred - square_true * lax.rsqrt(square_true)
            square_err = gap_dist * gap_dist + 0.01
            inv_err = lax.rsqrt(square_err)
            decay = jnp.exp(-(square_err * inv_err))
            ys = [decay * math.exp(t) for t in thresholds]
            dens = [(1.0 + y) * (1.0 + y) for y in ys]
            low = dens[0] * dens[1]
            high = dens[2] * dens[3]
            numer = (ys[0] * dens[1] + ys[1] * dens[0]) * high + (ys[2] * dens[3] + ys[3] * dens[2]) * low
            coef = (numer * gap_dist * (inv_err * inv_pred)) / (low * high)
            return tuple(acc + coef * gap for acc, gap in zip(accs, gaps))

        zero = jnp.zeros(shape, jnp.float32)
        accs = lax.fori_loop(0, live, slot_body, (zero, zero, zero))
        sums = [-0.25 * jnp.sum(acc, axis=1, keepdims=True) for acc in accs]
        tile = jnp.where(lane == 0, sums[0], jnp.where(lane == 1, sums[1], jnp.where(lane == 2, sums[2], 0.0)))
        out_ref[pl.ds(row, ROW_CHUNK), :] = tile
        return carry

    lax.fori_loop(0, PAIR_BLK // ROW_CHUNK, row_body, 0)


def lddt_sums(slots, counts, own_tab, pred_parts, true_parts):
    blocks = counts.shape[0]
    out = pl.pallas_call(
        lddt_kernel,
        grid_spec=pltpu.PrefetchScalarGridSpec(
            num_scalar_prefetch=2,
            grid=(blocks,),
            in_specs=[
                pl.BlockSpec((PAIR_BLK, own_tab.shape[1]), lambda b, *_: (b, 0)),
                pl.BlockSpec(pred_parts.shape, lambda b, *_: (0, 0, 0)),
                pl.BlockSpec(true_parts.shape, lambda b, *_: (0, 0, 0)),
            ],
            out_specs=pl.BlockSpec((PAIR_BLK, PAIR_BLK), lambda b, *_: (b, 0)),
            scratch_shapes=[pltpu.VMEM((6, PAIR_BLK, PAIR_BLK), jnp.float32)],
        ),
        out_shape=jax.ShapeDtypeStruct((blocks * PAIR_BLK, PAIR_BLK), jnp.float32),
    )(slots, counts, own_tab, pred_parts, true_parts)
    return out[:, :3].T

def dense(left, right):
    return jnp.einsum("sac,cf->saf", left, right, preferred_element_type=jnp.float32)


def on_device(
    token_feats,
    proj_w,
    atom_single,
    atom_token,
    true_coords,
    noise,
    sigma,
    coord_in,
    w_qkv,
    w_o,
    w_gu,
    w_down,
    gains,
    w_out,
    pair_blocks,
    pair_count,
):
    atom_rank = lax.axis_index("atoms")
    tok_rows = token_feats.shape[0]
    atom_rows = atom_single.shape[0]
    total_atoms = atom_rows * lax.axis_size("atoms")
    samples = noise.shape[0]
    feat_parts = ring_parts(token_feats, "samples")
    proj_parts = ring_parts(proj_w, "samples")
    token_sum = jnp.einsum(
        "kti,kio->to", feat_parts, proj_parts, preferred_element_type=jnp.float32
    )
    token_proj = token_sum.astype(jnp.bfloat16)
    padded_tok = extended(token_proj, (("atoms", 0),), HALO_TOK)
    first_token = atom_rank * tok_rows - HALO_TOK
    relative = atom_token - first_token
    onehot = (
        relative[:, None] == jnp.arange(tok_rows + 2 * HALO_TOK, dtype=jnp.int32)[None, :]
    ).astype(jnp.bfloat16)
    atom_base = atom_single.astype(jnp.float32) + jnp.dot(
        onehot, padded_tok, preferred_element_type=jnp.float32
    )
    sigma_col = sigma[:, None, None]
    noisy = true_coords[None] + sigma_col * noise
    noise_total = sigma_col * sigma_col + sigma_data * sigma_data
    scaled = noisy / jnp.sqrt(noise_total)
    hidden = atom_base[None] + jnp.einsum(
        "sda,dc->sac", scaled, coord_in, precision=lax.Precision.HIGHEST
    )
    key_halo = (KWIN - QBLK) // 2
    tile_start = atom_rank * atom_rows - key_halo + Q_TILE * jnp.arange(
        atom_rows // Q_TILE, dtype=jnp.int32
    )
    position = tile_start[:, None] + jnp.arange(K_SPAN, dtype=jnp.int32)[None, :]
    valid_tab = ((position >= 0) & (position < total_atoms)).astype(jnp.float32)
    query_win = jnp.arange(Q_TILE, dtype=jnp.int32)[:, None] // QBLK * QBLK
    key_index = jnp.arange(K_SPAN, dtype=jnp.int32)[None, :]
    band = ((key_index >= query_win) & (key_index < query_win + KWIN)).astype(jnp.float32)
    channels = hidden.shape[2]
    for layer_index in range(LAYERS):
        normed = (rms_norm(hidden) * gains[layer_index, 0]).astype(jnp.bfloat16)
        qkv_all = dense(normed, w_qkv[layer_index]).astype(jnp.bfloat16)
        queries = qkv_all[:, :, :channels]
        padded = extended(qkv_all[:, :, channels:], (("atoms", 1),), key_halo)
        attended = jnp.stack(
            [window_attend(queries[s], padded[s], band, valid_tab) for s in range(samples)]
        )
        hidden = hidden + dense(attended, w_o[layer_index])
        normed = (rms_norm(hidden) * gains[layer_index, 1]).astype(jnp.bfloat16)
        gate_up = dense(normed, w_gu[layer_index])
        inner_act = (jax.nn.silu(gate_up[..., :FF_ATOM]) * gate_up[..., FF_ATOM:]).astype(
            jnp.bfloat16
        )
        hidden = hidden + dense(inner_act, w_down[layer_index])
    update = jnp.einsum("sac,cd->sda", rms_norm(hidden), w_out, precision=lax.Precision.HIGHEST)
    predicted = (
        sigma_data * sigma_data / noise_total * noisy
        + sigma_col * sigma_data / jnp.sqrt(noise_total) * update
    )
    mse_part = (
        2.0 / 3.0 * (noise_total / (sigma_col * sigma_data) ** 2) * (predicted - true_coords[None])
    )
    block_count = atom_rows // PAIR_BLK
    atom_peers = lax.axis_size("atoms")
    count_row = jnp.zeros((1, atom_rows), jnp.float32).at[0, 0].set(
        jnp.sum(pair_count.astype(jnp.float32) * (PAIR_BLK * PAIR_BLK) - PAIR_BLK)
    )
    true_parts = ring_parts(jnp.concatenate([true_coords, count_row], axis=0), "atoms")
    pred_parts = ring_parts(predicted[0], "atoms")
    pair_total = jnp.sum(true_parts[:, 3, 0])
    own_tab = jnp.concatenate(
        [predicted[0], true_coords, jnp.zeros((2, atom_rows), jnp.float32)], axis=0
    ).T
    source = (atom_rank - pair_blocks // block_count) % atom_peers
    slots = (source * block_count + pair_blocks % block_count).reshape(-1)
    pair_grad = 2.0 * lddt_sums(slots, pair_count, own_tab, pred_parts, true_parts)[None]
    lddt_grad = total_atoms * PAIR_BLK / pair_total * pair_grad.reshape(samples, 3, atom_rows)
    coord_grad = mse_part - lddt_grad / PAIR_BLK
    return (coord_grad, lddt_grad)


def solution(mesh):
    in_specs = (
        P("atoms", "samples"),
        P("samples", None),
        P("atoms", None),
        P("atoms"),
        P(None, "atoms"),
        P("samples", None, "atoms"),
        P("samples"),
        P(),
        P(),
        P(),
        P(),
        P(),
        P(),
        P(),
        P("atoms", None),
        P("atoms"),
    )
    out_specs = (P("samples", None, "atoms"), P("samples", None, "atoms"))
    return jax.shard_map(
        on_device, mesh=mesh, in_specs=in_specs, out_specs=out_specs, check_vma=False
    )
```

```python
import math

import jax
import jax.numpy as jnp
from jax import lax
from jax.experimental import pallas as pl
from jax.experimental.pallas import tpu as pltpu
from jax.sharding import PartitionSpec as P

HEADS = 4
FF_ATOM = 256
LAYERS = 3
QBLK = 32
KWIN = 128
HALO_TOK = 16
PAIR_BLK = 128


sigma_data = 2.0
norm_epsilon = 1e-05
thresholds = (0.5, 1.0, 2.0, 4.0)


def extended(value, sides, width):
    for axis, dim in sides:
        peers, length = (lax.axis_size(axis), value.shape[dim])
        up = [(i, (i + 1) % peers) for i in range(peers - 1)]
        down = [(j, i) for i, j in up]
        last = lax.slice_in_dim(value, length - width, length, axis=dim)
        first = lax.slice_in_dim(value, 0, width, axis=dim)
        before = lax.ppermute(last, axis, up)
        after = lax.ppermute(first, axis, down)
        value = jnp.concatenate([before, value, after], axis=dim)
    return value


def ring_parts(value, axis):
    peers = lax.axis_size(axis)
    parts = value[None]
    span = 1
    while span < peers and peers % (2 * span) == 0:
        pairs = [(i, (i + span) % peers) for i in range(peers)]
        parts = jnp.concatenate([parts, lax.ppermute(parts, axis, pairs)])
        span *= 2
    if span < peers:
        extra = [value[None]]
        for shift in range(span, peers):
            pairs = [(i, (i + shift) % peers) for i in range(peers)]
            extra.append(lax.ppermute(value, axis, pairs)[None])
        parts = jnp.concatenate([parts] + extra[1:])
    return parts

def rms_norm(tensor):
    return tensor * lax.rsqrt(jnp.mean(tensor * tensor, axis=-1, keepdims=True) + norm_epsilon)


Q_TILE = 128
K_SPAN = 256


def attend_kernel(q_ref, kv_ref, band_ref, valid_ref, out_ref):
    tile = pl.program_id(0)
    head_dim = q_ref.shape[1] // HEADS
    channels = q_ref.shape[1]
    scale = head_dim ** (-0.5)
    start = pl.multiple_of(tile * Q_TILE, Q_TILE)
    keys_vals = kv_ref[pl.ds(start, K_SPAN), :]
    live = (band_ref[...] * valid_ref[pl.ds(tile, 1), :]) > 0.0
    query_rows = q_ref[...]
    heads = []
    for head in range(HEADS):
        cols = slice(head * head_dim, (head + 1) * head_dim)
        vcols = slice(channels + head * head_dim, channels + (head + 1) * head_dim)
        scores = lax.dot_general(
            query_rows[:, cols], keys_vals[:, cols], (((1,), (1,)), ((), ())),
            preferred_element_type=jnp.float32,
        )
        scores = jnp.where(live, scores, -1e30)
        row_max = jnp.max(scores, axis=-1, keepdims=True)
        exp_scores = jnp.exp2((scores - row_max) * (scale * math.log2(math.e)))
        inverse = 1.0 / jnp.sum(exp_scores, axis=-1, keepdims=True)
        weights = (exp_scores * inverse).astype(jnp.bfloat16)
        heads.append(
            jnp.dot(weights, keys_vals[:, vcols], preferred_element_type=jnp.float32).astype(
                jnp.bfloat16
            )
        )
    out_ref[...] = jnp.concatenate(heads, axis=1)


def window_attend(queries, padded_kv, band, valid_tab):
    atoms, channels = queries.shape
    extra = atoms + K_SPAN - Q_TILE - padded_kv.shape[0]
    padded_kv = jnp.pad(padded_kv, ((0, extra), (0, 0)))
    return pl.pallas_call(
        attend_kernel,
        grid=(atoms // Q_TILE,),
        in_specs=[
            pl.BlockSpec((Q_TILE, channels), lambda t: (t, 0)),
            pl.BlockSpec(padded_kv.shape, lambda t: (0, 0)),
            pl.BlockSpec(band.shape, lambda t: (0, 0)),
            pl.BlockSpec(valid_tab.shape, lambda t: (0, 0)),
        ],
        out_specs=pl.BlockSpec((Q_TILE, channels), lambda t: (t, 0)),
        out_shape=jax.ShapeDtypeStruct((atoms, channels), jnp.bfloat16),
    )(queries, padded_kv, band, valid_tab)

ROW_CHUNK = 64


def lddt_kernel(slots_ref, count_ref, own_ref, pred_ref, true_ref, out_ref, cols_ref):
    block = pl.program_id(0)
    live = count_ref[block]
    blocks = count_ref.shape[0]
    max_slots = slots_ref.shape[0] // blocks
    shape = (ROW_CHUNK, PAIR_BLK)
    lane = lax.broadcasted_iota(jnp.int32, shape, 1)
    for chunk in range(PAIR_BLK // ROW_CHUNK):
        rows = slice(chunk * ROW_CHUNK, (chunk + 1) * ROW_CHUNK)
        own = own_ref[rows, :]
        for d in range(6):
            cols_ref[d, rows, :] = jnp.broadcast_to(own[:, d : d + 1], shape)

    def row_body(row_index, carry):
        row = pl.multiple_of(row_index * ROW_CHUNK, ROW_CHUNK)

        def slot_body(slot_index, accs):
            slot = slots_ref[block * max_slots + slot_index]
            peer = slot // blocks
            start = pl.multiple_of((slot % blocks) * PAIR_BLK, PAIR_BLK)
            part_pred = pred_ref[peer, :, pl.ds(start, PAIR_BLK)]
            part_true = true_ref[peer, :, pl.ds(start, PAIR_BLK)]
            gaps = [cols_ref[d, pl.ds(row, ROW_CHUNK), :] - part_pred[d : d + 1, :] for d in range(3)]
            true_gaps = [
                cols_ref[3 + d, pl.ds(row, ROW_CHUNK), :] - part_true[d : d + 1, :] for d in range(3)
            ]
            square_pred = gaps[0] * gaps[0] + gaps[1] * gaps[1] + gaps[2] * gaps[2] + 1.0
            square_true = (
                true_gaps[0] * true_gaps[0] + true_gaps[1] * true_gaps[1] + true_gaps[2] * true_gaps[2]
            ) + 1.0
            inv_pred = lax.rsqrt(square_pred)
            gap_dist = square_pred * inv_pred - square_true * lax.rsqrt(square_true)
            square_err = gap_dist * gap_dist + 0.01
            inv_err = lax.rsqrt(square_err)
            decay = jnp.exp(-(square_err * inv_err))
            ys = [decay * math.exp(t) for t in thresholds]
            dens = [(1.0 + y) * (1.0 + y) for y in ys]
            low = dens[0] * dens[1]
            high = dens[2] * dens[3]
            numer = (ys[0] * dens[1] + ys[1] * dens[0]) * high + (ys[2] * dens[3] + ys[3] * dens[2]) * low
            coef = (numer * gap_dist * (inv_err * inv_pred)) / (low * high)
            return tuple(acc + coef * gap for acc, gap in zip(accs, gaps))

        zero = jnp.zeros(shape, jnp.float32)
        accs = lax.fori_loop(0, live, slot_body, (zero, zero, zero))
        sums = [-0.25 * jnp.sum(acc, axis=1, keepdims=True) for acc in accs]
        tile = jnp.where(lane == 0, sums[0], jnp.where(lane == 1, sums[1], jnp.where(lane == 2, sums[2], 0.0)))
        out_ref[pl.ds(row, ROW_CHUNK), :] = tile
        return carry

    lax.fori_loop(0, PAIR_BLK // ROW_CHUNK, row_body, 0)


def lddt_sums(slots, counts, own_tab, pred_parts, true_parts):
    blocks = counts.shape[0]
    out = pl.pallas_call(
        lddt_kernel,
        grid_spec=pltpu.PrefetchScalarGridSpec(
            num_scalar_prefetch=2,
            grid=(blocks,),
            in_specs=[
                pl.BlockSpec((PAIR_BLK, own_tab.shape[1]), lambda b, *_: (b, 0)),
                pl.BlockSpec(pred_parts.shape, lambda b, *_: (0, 0, 0)),
                pl.BlockSpec(true_parts.shape, lambda b, *_: (0, 0, 0)),
            ],
            out_specs=pl.BlockSpec((PAIR_BLK, PAIR_BLK), lambda b, *_: (b, 0)),
            scratch_shapes=[pltpu.VMEM((6, PAIR_BLK, PAIR_BLK), jnp.float32)],
        ),
        out_shape=jax.ShapeDtypeStruct((blocks * PAIR_BLK, PAIR_BLK), jnp.float32),
    )(slots, counts, own_tab, pred_parts, true_parts)
    return out[:, :3].T

def dense(left, right):
    return jnp.einsum("sac,cf->saf", left, right, preferred_element_type=jnp.float32)


def on_device(
    token_feats,
    proj_w,
    atom_single,
    atom_token,
    true_coords,
    noise,
    sigma,
    coord_in,
    w_qkv,
    w_o,
    w_gu,
    w_down,
    gains,
    w_out,
    pair_blocks,
    pair_count,
):
    atom_rank = lax.axis_index("atoms")
    tok_rows = token_feats.shape[0]
    atom_rows = atom_single.shape[0]
    total_atoms = atom_rows * lax.axis_size("atoms")
    samples = noise.shape[0]
    feat_parts = ring_parts(token_feats, "samples")
    proj_parts = ring_parts(proj_w, "samples")
    token_sum = jnp.einsum(
        "kti,kio->to", feat_parts, proj_parts, preferred_element_type=jnp.float32
    )
    token_proj = token_sum.astype(jnp.bfloat16)
    padded_tok = extended(token_proj, (("atoms", 0),), HALO_TOK)
    first_token = atom_rank * tok_rows - HALO_TOK
    relative = atom_token - first_token
    onehot = (
        relative[:, None] == jnp.arange(tok_rows + 2 * HALO_TOK, dtype=jnp.int32)[None, :]
    ).astype(jnp.bfloat16)
    atom_base = atom_single.astype(jnp.float32) + jnp.dot(
        onehot, padded_tok, preferred_element_type=jnp.float32
    )
    sigma_col = sigma[:, None, None]
    noisy = true_coords[None] + sigma_col * noise
    noise_total = sigma_col * sigma_col + sigma_data * sigma_data
    scaled = noisy / jnp.sqrt(noise_total)
    hidden = atom_base[None] + jnp.einsum(
        "sda,dc->sac", scaled, coord_in, precision=lax.Precision.HIGHEST
    )
    key_halo = (KWIN - QBLK) // 2
    reaches = [0]
    for _ in range(LAYERS - 1):
        reaches.insert(0, -(-(reaches[0] + key_halo) // QBLK) * QBLK)
    buffer_start = -(reaches[0] + key_halo)
    hidden = extended(hidden, (("atoms", 1),), -buffer_start)
    query_win = jnp.arange(Q_TILE, dtype=jnp.int32)[:, None] // QBLK * QBLK
    key_index = jnp.arange(K_SPAN, dtype=jnp.int32)[None, :]
    band = ((key_index >= query_win) & (key_index < query_win + KWIN)).astype(jnp.float32)
    channels = hidden.shape[2]
    for layer_index in range(LAYERS):
        reach = reaches[layer_index]
        kv_off = -(reach + key_halo) - buffer_start
        q_off = kv_off + key_halo
        tiles = -(-(atom_rows + 2 * reach) // Q_TILE)
        tile_start = atom_rank * atom_rows - reach - key_halo + Q_TILE * jnp.arange(
            tiles, dtype=jnp.int32
        )
        position = tile_start[:, None] + key_index
        valid_tab = ((position >= 0) & (position < total_atoms)).astype(jnp.float32)
        normed = (rms_norm(hidden) * gains[layer_index, 0]).astype(jnp.bfloat16)
        qkv_all = dense(normed, w_qkv[layer_index]).astype(jnp.bfloat16)
        span_rows = kv_off + tiles * Q_TILE + K_SPAN - Q_TILE
        qkv_all = jnp.pad(qkv_all, ((0, 0), (0, max(0, span_rows - qkv_all.shape[1])), (0, 0)))
        queries = qkv_all[:, q_off : q_off + tiles * Q_TILE, :channels]
        key_vals = qkv_all[:, kv_off:span_rows, channels:]
        attended = jnp.stack(
            [window_attend(queries[s], key_vals[s], band, valid_tab) for s in range(samples)]
        )
        hidden = jnp.pad(hidden, ((0, 0), (0, max(0, span_rows - hidden.shape[1])), (0, 0)))
        hidden = hidden[:, q_off : q_off + tiles * Q_TILE] + dense(attended, w_o[layer_index])
        buffer_start = -reach
        normed = (rms_norm(hidden) * gains[layer_index, 1]).astype(jnp.bfloat16)
        gate_up = dense(normed, w_gu[layer_index])
        inner_act = (jax.nn.silu(gate_up[..., :FF_ATOM]) * gate_up[..., FF_ATOM:]).astype(
            jnp.bfloat16
        )
        hidden = hidden + dense(inner_act, w_down[layer_index])
    hidden = hidden[:, -buffer_start : -buffer_start + atom_rows]
    update = jnp.einsum("sac,cd->sda", rms_norm(hidden), w_out, precision=lax.Precision.HIGHEST)
    predicted = (
        sigma_data * sigma_data / noise_total * noisy
        + sigma_col * sigma_data / jnp.sqrt(noise_total) * update
    )
    mse_part = (
        2.0 / 3.0 * (noise_total / (sigma_col * sigma_data) ** 2) * (predicted - true_coords[None])
    )
    block_count = atom_rows // PAIR_BLK
    atom_peers = lax.axis_size("atoms")
    count_row = jnp.zeros((1, atom_rows), jnp.float32).at[0, 0].set(
        jnp.sum(pair_count.astype(jnp.float32) * (PAIR_BLK * PAIR_BLK) - PAIR_BLK)
    )
    true_parts = ring_parts(jnp.concatenate([true_coords, count_row], axis=0), "atoms")
    pred_parts = ring_parts(predicted[0], "atoms")
    pair_total = jnp.sum(true_parts[:, 3, 0])
    own_tab = jnp.concatenate(
        [predicted[0], true_coords, jnp.zeros((2, atom_rows), jnp.float32)], axis=0
    ).T
    source = (atom_rank - pair_blocks // block_count) % atom_peers
    slots = (source * block_count + pair_blocks % block_count).reshape(-1)
    pair_grad = 2.0 * lddt_sums(slots, pair_count, own_tab, pred_parts, true_parts)[None]
    lddt_grad = total_atoms * PAIR_BLK / pair_total * pair_grad.reshape(samples, 3, atom_rows)
    coord_grad = mse_part - lddt_grad / PAIR_BLK
    return (coord_grad, lddt_grad)


def solution(mesh):
    in_specs = (
        P("atoms", "samples"),
        P("samples", None),
        P("atoms", None),
        P("atoms"),
        P(None, "atoms"),
        P("samples", None, "atoms"),
        P("samples"),
        P(),
        P(),
        P(),
        P(),
        P(),
        P(),
        P(),
        P("atoms", None),
        P("atoms"),
    )
    out_specs = (P("samples", None, "atoms"), P("samples", None, "atoms"))
    return jax.shard_map(
        on_device, mesh=mesh, in_specs=in_specs, out_specs=out_specs, check_vma=False
    )
```

```python
import math

import jax
import jax.numpy as jnp
from jax import lax
from jax.experimental import pallas as pl
from jax.experimental.pallas import tpu as pltpu
from jax.sharding import PartitionSpec as P

HEADS = 4
FF_ATOM = 256
LAYERS = 3
QBLK = 32
KWIN = 128
HALO_TOK = 16
PAIR_BLK = 128


sigma_data = 2.0
norm_epsilon = 1e-05
thresholds = (0.5, 1.0, 2.0, 4.0)


def extended(value, sides, width):
    for axis, dim in sides:
        peers, length = (lax.axis_size(axis), value.shape[dim])
        up = [(i, (i + 1) % peers) for i in range(peers - 1)]
        down = [(j, i) for i, j in up]
        last = lax.slice_in_dim(value, length - width, length, axis=dim)
        first = lax.slice_in_dim(value, 0, width, axis=dim)
        before = lax.ppermute(last, axis, up)
        after = lax.ppermute(first, axis, down)
        value = jnp.concatenate([before, value, after], axis=dim)
    return value


def ring_parts(value, axis):
    peers = lax.axis_size(axis)
    parts = value[None]
    span = 1
    while span < peers and peers % (2 * span) == 0:
        pairs = [(i, (i + span) % peers) for i in range(peers)]
        parts = jnp.concatenate([parts, lax.ppermute(parts, axis, pairs)])
        span *= 2
    if span < peers:
        extra = [value[None]]
        for shift in range(span, peers):
            pairs = [(i, (i + shift) % peers) for i in range(peers)]
            extra.append(lax.ppermute(value, axis, pairs)[None])
        parts = jnp.concatenate([parts] + extra[1:])
    return parts

def rms_norm(tensor):
    return tensor * lax.rsqrt(jnp.mean(tensor * tensor, axis=-1, keepdims=True) + norm_epsilon)


Q_TILE = 128
K_SPAN = 256


def attend_kernel(q_ref, kv_ref, band_ref, valid_ref, out_ref):
    tile = pl.program_id(0)
    head_dim = q_ref.shape[1] // HEADS
    channels = q_ref.shape[1]
    scale = head_dim ** (-0.5)
    start = pl.multiple_of(tile * Q_TILE, Q_TILE)
    keys_vals = kv_ref[pl.ds(start, K_SPAN), :]
    live = (band_ref[...] * valid_ref[pl.ds(tile, 1), :]) > 0.0
    query_rows = q_ref[...]
    heads = []
    for head in range(HEADS):
        cols = slice(head * head_dim, (head + 1) * head_dim)
        vcols = slice(channels + head * head_dim, channels + (head + 1) * head_dim)
        scores = lax.dot_general(
            query_rows[:, cols], keys_vals[:, cols], (((1,), (1,)), ((), ())),
            preferred_element_type=jnp.float32,
        )
        scores = jnp.where(live, scores, -1e30)
        row_max = jnp.max(scores, axis=-1, keepdims=True)
        exp_scores = jnp.exp2((scores - row_max) * (scale * math.log2(math.e)))
        inverse = 1.0 / jnp.sum(exp_scores, axis=-1, keepdims=True)
        weights = (exp_scores * inverse).astype(jnp.bfloat16)
        heads.append(
            jnp.dot(weights, keys_vals[:, vcols], preferred_element_type=jnp.float32).astype(
                jnp.bfloat16
            )
        )
    out_ref[...] = jnp.concatenate(heads, axis=1)


def window_attend(queries, padded_kv, band, valid_tab):
    atoms, channels = queries.shape
    extra = atoms + K_SPAN - Q_TILE - padded_kv.shape[0]
    padded_kv = jnp.pad(padded_kv, ((0, extra), (0, 0)))
    return pl.pallas_call(
        attend_kernel,
        grid=(atoms // Q_TILE,),
        in_specs=[
            pl.BlockSpec((Q_TILE, channels), lambda t: (t, 0)),
            pl.BlockSpec(padded_kv.shape, lambda t: (0, 0)),
            pl.BlockSpec(band.shape, lambda t: (0, 0)),
            pl.BlockSpec(valid_tab.shape, lambda t: (0, 0)),
        ],
        out_specs=pl.BlockSpec((Q_TILE, channels), lambda t: (t, 0)),
        out_shape=jax.ShapeDtypeStruct((atoms, channels), jnp.bfloat16),
    )(queries, padded_kv, band, valid_tab)

ROW_CHUNK = 64


def lddt_kernel(slots_ref, count_ref, own_ref, pred_ref, true_ref, out_ref, cols_ref):
    block = pl.program_id(0)
    live = count_ref[block]
    blocks = count_ref.shape[0]
    max_slots = slots_ref.shape[0] // blocks
    shape = (ROW_CHUNK, PAIR_BLK)
    lane = lax.broadcasted_iota(jnp.int32, shape, 1)
    for chunk in range(PAIR_BLK // ROW_CHUNK):
        rows = slice(chunk * ROW_CHUNK, (chunk + 1) * ROW_CHUNK)
        own = own_ref[rows, :]
        for d in range(6):
            cols_ref[d, rows, :] = jnp.broadcast_to(own[:, d : d + 1], shape)

    def row_body(row_index, carry):
        row = pl.multiple_of(row_index * ROW_CHUNK, ROW_CHUNK)

        def slot_body(slot_index, accs):
            slot = slots_ref[block * max_slots + slot_index]
            peer = slot // blocks
            start = pl.multiple_of((slot % blocks) * PAIR_BLK, PAIR_BLK)
            part_pred = pred_ref[peer, :, pl.ds(start, PAIR_BLK)]
            part_true = true_ref[peer, :, pl.ds(start, PAIR_BLK)]
            gaps = [cols_ref[d, pl.ds(row, ROW_CHUNK), :] - part_pred[d : d + 1, :] for d in range(3)]
            true_gaps = [
                cols_ref[3 + d, pl.ds(row, ROW_CHUNK), :] - part_true[d : d + 1, :] for d in range(3)
            ]
            square_pred = gaps[0] * gaps[0] + gaps[1] * gaps[1] + gaps[2] * gaps[2] + 1.0
            square_true = (
                true_gaps[0] * true_gaps[0] + true_gaps[1] * true_gaps[1] + true_gaps[2] * true_gaps[2]
            ) + 1.0
            inv_pred = lax.rsqrt(square_pred)
            gap_dist = square_pred * inv_pred - square_true * lax.rsqrt(square_true)
            square_err = gap_dist * gap_dist + 0.01
            inv_err = lax.rsqrt(square_err)
            decay = jnp.exp(-(square_err * inv_err))
            ys = [decay * math.exp(t) for t in thresholds]
            dens = [(1.0 + y) * (1.0 + y) for y in ys]
            low = dens[0] * dens[1]
            high = dens[2] * dens[3]
            numer = (ys[0] * dens[1] + ys[1] * dens[0]) * high + (ys[2] * dens[3] + ys[3] * dens[2]) * low
            coef = (numer * gap_dist * (inv_err * inv_pred)) / (low * high)
            return tuple(acc + coef * gap for acc, gap in zip(accs, gaps))

        zero = jnp.zeros(shape, jnp.float32)
        accs = lax.fori_loop(0, live, slot_body, (zero, zero, zero))
        sums = [-0.25 * jnp.sum(acc, axis=1, keepdims=True) for acc in accs]
        tile = jnp.where(lane == 0, sums[0], jnp.where(lane == 1, sums[1], jnp.where(lane == 2, sums[2], 0.0)))
        out_ref[pl.ds(row, ROW_CHUNK), :] = tile
        return carry

    lax.fori_loop(0, PAIR_BLK // ROW_CHUNK, row_body, 0)


def lddt_sums(slots, counts, own_tab, pred_parts, true_parts):
    blocks = counts.shape[0]
    out = pl.pallas_call(
        lddt_kernel,
        grid_spec=pltpu.PrefetchScalarGridSpec(
            num_scalar_prefetch=2,
            grid=(blocks,),
            in_specs=[
                pl.BlockSpec((PAIR_BLK, own_tab.shape[1]), lambda b, *_: (b, 0)),
                pl.BlockSpec(pred_parts.shape, lambda b, *_: (0, 0, 0)),
                pl.BlockSpec(true_parts.shape, lambda b, *_: (0, 0, 0)),
            ],
            out_specs=pl.BlockSpec((PAIR_BLK, PAIR_BLK), lambda b, *_: (b, 0)),
            scratch_shapes=[pltpu.VMEM((6, PAIR_BLK, PAIR_BLK), jnp.float32)],
        ),
        out_shape=jax.ShapeDtypeStruct((blocks * PAIR_BLK, PAIR_BLK), jnp.float32),
    )(slots, counts, own_tab, pred_parts, true_parts)
    return out[:, :3].T

def dense(left, right):
    return jnp.einsum("sac,cf->saf", left, right, preferred_element_type=jnp.float32)


def on_device(
    token_feats,
    proj_w,
    atom_single,
    atom_token,
    true_coords,
    noise,
    sigma,
    coord_in,
    w_qkv,
    w_o,
    w_gu,
    w_down,
    gains,
    w_out,
    pair_blocks,
    pair_count,
):
    atom_rank = lax.axis_index("atoms")
    tok_rows = token_feats.shape[0]
    atom_rows = atom_single.shape[0]
    total_atoms = atom_rows * lax.axis_size("atoms")
    samples = noise.shape[0]
    feat_parts = ring_parts(token_feats, "samples")
    proj_parts = ring_parts(proj_w, "samples")
    token_sum = jnp.einsum(
        "kti,kio->to", feat_parts, proj_parts, preferred_element_type=jnp.float32
    )
    token_proj = token_sum.astype(jnp.bfloat16)
    key_halo = (KWIN - QBLK) // 2
    reaches = [0]
    for _ in range(LAYERS - 1):
        reaches.insert(0, -(-(reaches[0] + key_halo) // QBLK) * QBLK)
    buffer_start = -(reaches[0] + key_halo)
    atom_halo = -buffer_start
    per_token = atom_rows // tok_rows
    tok_halo = -(-(-(-atom_halo // per_token) + HALO_TOK) // 16) * 16
    samples = noise.shape[0]
    atom_floats = jnp.concatenate(
        [true_coords, noise.reshape(samples * 3, atom_rows), atom_token.astype(jnp.float32)[None]]
    )
    floats_ext = extended(atom_floats, (("atoms", 1),), atom_halo)
    single_ext = extended(atom_single, (("atoms", 0),), atom_halo)
    true_ext = floats_ext[:3]
    noise_ext = floats_ext[3 : 3 + 3 * samples].reshape(samples, 3, -1)
    token_ext = floats_ext[3 + 3 * samples].astype(jnp.int32)
    padded_tok = extended(token_proj, (("atoms", 0),), tok_halo)
    first_token = atom_rank * tok_rows - tok_halo
    relative = token_ext - first_token
    onehot = (
        relative[:, None] == jnp.arange(tok_rows + 2 * tok_halo, dtype=jnp.int32)[None, :]
    ).astype(jnp.bfloat16)
    atom_base = single_ext.astype(jnp.float32) + jnp.dot(
        onehot, padded_tok, preferred_element_type=jnp.float32
    )
    sigma_col = sigma[:, None, None]
    noisy = true_coords[None] + sigma_col * noise
    noise_total = sigma_col * sigma_col + sigma_data * sigma_data
    scaled = (true_ext[None] + sigma_col * noise_ext) / jnp.sqrt(noise_total)
    hidden = atom_base[None] + jnp.einsum(
        "sda,dc->sac", scaled, coord_in, precision=lax.Precision.HIGHEST
    )
    query_win = jnp.arange(Q_TILE, dtype=jnp.int32)[:, None] // QBLK * QBLK
    key_index = jnp.arange(K_SPAN, dtype=jnp.int32)[None, :]
    band = ((key_index >= query_win) & (key_index < query_win + KWIN)).astype(jnp.float32)
    channels = hidden.shape[2]
    for layer_index in range(LAYERS):
        reach = reaches[layer_index]
        kv_off = -(reach + key_halo) - buffer_start
        q_off = kv_off + key_halo
        tiles = -(-(atom_rows + 2 * reach) // Q_TILE)
        tile_start = atom_rank * atom_rows - reach - key_halo + Q_TILE * jnp.arange(
            tiles, dtype=jnp.int32
        )
        position = tile_start[:, None] + key_index
        valid_tab = ((position >= 0) & (position < total_atoms)).astype(jnp.float32)
        normed = (rms_norm(hidden) * gains[layer_index, 0]).astype(jnp.bfloat16)
        qkv_all = dense(normed, w_qkv[layer_index]).astype(jnp.bfloat16)
        span_rows = kv_off + tiles * Q_TILE + K_SPAN - Q_TILE
        qkv_all = jnp.pad(qkv_all, ((0, 0), (0, max(0, span_rows - qkv_all.shape[1])), (0, 0)))
        queries = qkv_all[:, q_off : q_off + tiles * Q_TILE, :channels]
        key_vals = qkv_all[:, kv_off:span_rows, channels:]
        attended = jnp.stack(
            [window_attend(queries[s], key_vals[s], band, valid_tab) for s in range(samples)]
        )
        hidden = jnp.pad(hidden, ((0, 0), (0, max(0, span_rows - hidden.shape[1])), (0, 0)))
        hidden = hidden[:, q_off : q_off + tiles * Q_TILE] + dense(attended, w_o[layer_index])
        buffer_start = -reach
        normed = (rms_norm(hidden) * gains[layer_index, 1]).astype(jnp.bfloat16)
        gate_up = dense(normed, w_gu[layer_index])
        inner_act = (jax.nn.silu(gate_up[..., :FF_ATOM]) * gate_up[..., FF_ATOM:]).astype(
            jnp.bfloat16
        )
        hidden = hidden + dense(inner_act, w_down[layer_index])
    hidden = hidden[:, -buffer_start : -buffer_start + atom_rows]
    update = jnp.einsum("sac,cd->sda", rms_norm(hidden), w_out, precision=lax.Precision.HIGHEST)
    predicted = (
        sigma_data * sigma_data / noise_total * noisy
        + sigma_col * sigma_data / jnp.sqrt(noise_total) * update
    )
    mse_part = (
        2.0 / 3.0 * (noise_total / (sigma_col * sigma_data) ** 2) * (predicted - true_coords[None])
    )
    block_count = atom_rows // PAIR_BLK
    atom_peers = lax.axis_size("atoms")
    count_row = jnp.zeros((1, atom_rows), jnp.float32).at[0, 0].set(
        jnp.sum(pair_count.astype(jnp.float32) * (PAIR_BLK * PAIR_BLK) - PAIR_BLK)
    )
    true_parts = ring_parts(jnp.concatenate([true_coords, count_row], axis=0), "atoms")
    pred_parts = ring_parts(predicted[0], "atoms")
    pair_total = jnp.sum(true_parts[:, 3, 0])
    own_tab = jnp.concatenate(
        [predicted[0], true_coords, jnp.zeros((2, atom_rows), jnp.float32)], axis=0
    ).T
    source = (atom_rank - pair_blocks // block_count) % atom_peers
    slots = (source * block_count + pair_blocks % block_count).reshape(-1)
    pair_grad = 2.0 * lddt_sums(slots, pair_count, own_tab, pred_parts, true_parts)[None]
    lddt_grad = total_atoms * PAIR_BLK / pair_total * pair_grad.reshape(samples, 3, atom_rows)
    coord_grad = mse_part - lddt_grad / PAIR_BLK
    return (coord_grad, lddt_grad)


def solution(mesh):
    in_specs = (
        P("atoms", "samples"),
        P("samples", None),
        P("atoms", None),
        P("atoms"),
        P(None, "atoms"),
        P("samples", None, "atoms"),
        P("samples"),
        P(),
        P(),
        P(),
        P(),
        P(),
        P(),
        P(),
        P("atoms", None),
        P("atoms"),
    )
    out_specs = (P("samples", None, "atoms"), P("samples", None, "atoms"))
    return jax.shard_map(
        on_device, mesh=mesh, in_specs=in_specs, out_specs=out_specs, check_vma=False
    )
```

```python
import math

import jax
import jax.numpy as jnp
from jax import lax
from jax.experimental import pallas as pl
from jax.experimental.pallas import tpu as pltpu
from jax.sharding import PartitionSpec as P

HEADS = 4
FF_ATOM = 256
LAYERS = 3
QBLK = 32
KWIN = 128
HALO_TOK = 16
PAIR_BLK = 128


sigma_data = 2.0
norm_epsilon = 1e-05
thresholds = (0.5, 1.0, 2.0, 4.0)


def extended(value, sides, width):
    for axis, dim in sides:
        peers, length = (lax.axis_size(axis), value.shape[dim])
        up = [(i, (i + 1) % peers) for i in range(peers - 1)]
        down = [(j, i) for i, j in up]
        last = lax.slice_in_dim(value, length - width, length, axis=dim)
        first = lax.slice_in_dim(value, 0, width, axis=dim)
        before = lax.ppermute(last, axis, up)
        after = lax.ppermute(first, axis, down)
        value = jnp.concatenate([before, value, after], axis=dim)
    return value


def ring_parts(value, axis):
    peers = lax.axis_size(axis)
    parts = value[None]
    span = 1
    while span < peers and peers % (2 * span) == 0:
        pairs = [(i, (i + span) % peers) for i in range(peers)]
        parts = jnp.concatenate([parts, lax.ppermute(parts, axis, pairs)])
        span *= 2
    if span < peers:
        extra = [value[None]]
        for shift in range(span, peers):
            pairs = [(i, (i + shift) % peers) for i in range(peers)]
            extra.append(lax.ppermute(value, axis, pairs)[None])
        parts = jnp.concatenate([parts] + extra[1:])
    return parts

def rms_norm(tensor):
    return tensor * lax.rsqrt(jnp.mean(tensor * tensor, axis=-1, keepdims=True) + norm_epsilon)


Q_TILE = 128
K_SPAN = 256


def attend_kernel(q_ref, kv_ref, band_ref, valid_ref, out_ref):
    tile = pl.program_id(0)
    head_dim = q_ref.shape[1] // HEADS
    channels = q_ref.shape[1]
    scale = head_dim ** (-0.5)
    start = pl.multiple_of(tile * Q_TILE, Q_TILE)
    keys_vals = kv_ref[pl.ds(start, K_SPAN), :]
    live = (band_ref[...] * valid_ref[pl.ds(tile, 1), :]) > 0.0
    query_rows = q_ref[...]
    heads = []
    for head in range(HEADS):
        cols = slice(head * head_dim, (head + 1) * head_dim)
        vcols = slice(channels + head * head_dim, channels + (head + 1) * head_dim)
        scores = lax.dot_general(
            query_rows[:, cols], keys_vals[:, cols], (((1,), (1,)), ((), ())),
            preferred_element_type=jnp.float32,
        )
        scores = jnp.where(live, scores, -1e30)
        row_max = jnp.max(scores, axis=-1, keepdims=True)
        exp_scores = jnp.exp2((scores - row_max) * (scale * math.log2(math.e)))
        inverse = 1.0 / jnp.sum(exp_scores, axis=-1, keepdims=True)
        weights = (exp_scores * inverse).astype(jnp.bfloat16)
        heads.append(
            jnp.dot(weights, keys_vals[:, vcols], preferred_element_type=jnp.float32).astype(
                jnp.bfloat16
            )
        )
    out_ref[...] = jnp.concatenate(heads, axis=1)


def window_attend(queries, padded_kv, band, valid_tab):
    atoms, channels = queries.shape
    extra = atoms + K_SPAN - Q_TILE - padded_kv.shape[0]
    padded_kv = jnp.pad(padded_kv, ((0, extra), (0, 0)))
    return pl.pallas_call(
        attend_kernel,
        grid=(atoms // Q_TILE,),
        in_specs=[
            pl.BlockSpec((Q_TILE, channels), lambda t: (t, 0)),
            pl.BlockSpec(padded_kv.shape, lambda t: (0, 0)),
            pl.BlockSpec(band.shape, lambda t: (0, 0)),
            pl.BlockSpec(valid_tab.shape, lambda t: (0, 0)),
        ],
        out_specs=pl.BlockSpec((Q_TILE, channels), lambda t: (t, 0)),
        out_shape=jax.ShapeDtypeStruct((atoms, channels), jnp.bfloat16),
    )(queries, padded_kv, band, valid_tab)

ROW_CHUNK = 64


def lddt_kernel(slots_ref, count_ref, own_ref, coord_ref, out_ref, cols_ref):
    block = pl.program_id(0)
    live = count_ref[block]
    blocks = count_ref.shape[0]
    max_slots = slots_ref.shape[0] // blocks
    shape = (ROW_CHUNK, PAIR_BLK)
    lane = lax.broadcasted_iota(jnp.int32, shape, 1)
    for chunk in range(PAIR_BLK // ROW_CHUNK):
        rows = slice(chunk * ROW_CHUNK, (chunk + 1) * ROW_CHUNK)
        own = own_ref[rows, :]
        for d in range(6):
            cols_ref[d, rows, :] = jnp.broadcast_to(own[:, d : d + 1], shape)

    def row_body(row_index, carry):
        row = pl.multiple_of(row_index * ROW_CHUNK, ROW_CHUNK)

        def slot_body(slot_index, accs):
            slot = slots_ref[block * max_slots + slot_index]
            peer = slot // blocks
            start = pl.multiple_of((slot % blocks) * PAIR_BLK, PAIR_BLK)
            part = coord_ref[peer, :, pl.ds(start, PAIR_BLK)]
            part_pred = part[0:3]
            part_true = part[3:6]
            gaps = [cols_ref[d, pl.ds(row, ROW_CHUNK), :] - part_pred[d : d + 1, :] for d in range(3)]
            true_gaps = [
                cols_ref[3 + d, pl.ds(row, ROW_CHUNK), :] - part_true[d : d + 1, :] for d in range(3)
            ]
            square_pred = gaps[0] * gaps[0] + gaps[1] * gaps[1] + gaps[2] * gaps[2] + 1.0
            square_true = (
                true_gaps[0] * true_gaps[0] + true_gaps[1] * true_gaps[1] + true_gaps[2] * true_gaps[2]
            ) + 1.0
            inv_pred = lax.rsqrt(square_pred)
            gap_dist = square_pred * inv_pred - square_true * lax.rsqrt(square_true)
            square_err = gap_dist * gap_dist + 0.01
            inv_err = lax.rsqrt(square_err)
            decay = jnp.exp(-(square_err * inv_err))
            ys = [decay * math.exp(t) for t in thresholds]
            dens = [(1.0 + y) * (1.0 + y) for y in ys]
            low = dens[0] * dens[1]
            high = dens[2] * dens[3]
            numer = (ys[0] * dens[1] + ys[1] * dens[0]) * high + (ys[2] * dens[3] + ys[3] * dens[2]) * low
            coef = (numer * gap_dist * (inv_err * inv_pred)) / (low * high)
            return tuple(acc + coef * gap for acc, gap in zip(accs, gaps))

        zero = jnp.zeros(shape, jnp.float32)
        accs = lax.fori_loop(0, live, slot_body, (zero, zero, zero))
        sums = [-0.25 * jnp.sum(acc, axis=1, keepdims=True) for acc in accs]
        tile = jnp.where(lane == 0, sums[0], jnp.where(lane == 1, sums[1], jnp.where(lane == 2, sums[2], 0.0)))
        out_ref[pl.ds(row, ROW_CHUNK), :] = tile
        return carry

    lax.fori_loop(0, PAIR_BLK // ROW_CHUNK, row_body, 0)


def lddt_sums(slots, counts, own_tab, coord_parts):
    blocks = counts.shape[0]
    out = pl.pallas_call(
        lddt_kernel,
        grid_spec=pltpu.PrefetchScalarGridSpec(
            num_scalar_prefetch=2,
            grid=(blocks,),
            in_specs=[
                pl.BlockSpec((PAIR_BLK, own_tab.shape[1]), lambda b, *_: (b, 0)),
                pl.BlockSpec(coord_parts.shape, lambda b, *_: (0, 0, 0)),
            ],
            out_specs=pl.BlockSpec((PAIR_BLK, PAIR_BLK), lambda b, *_: (b, 0)),
            scratch_shapes=[pltpu.VMEM((6, PAIR_BLK, PAIR_BLK), jnp.float32)],
        ),
        out_shape=jax.ShapeDtypeStruct((blocks * PAIR_BLK, PAIR_BLK), jnp.float32),
    )(slots, counts, own_tab, coord_parts)
    return out[:, :3].T

def dense(left, right):
    return jnp.einsum("sac,cf->saf", left, right, preferred_element_type=jnp.float32)


def on_device(
    token_feats,
    proj_w,
    atom_single,
    atom_token,
    true_coords,
    noise,
    sigma,
    coord_in,
    w_qkv,
    w_o,
    w_gu,
    w_down,
    gains,
    w_out,
    pair_blocks,
    pair_count,
):
    atom_rank = lax.axis_index("atoms")
    tok_rows = token_feats.shape[0]
    atom_rows = atom_single.shape[0]
    total_atoms = atom_rows * lax.axis_size("atoms")
    samples = noise.shape[0]
    feat_parts = ring_parts(token_feats, "samples")
    proj_parts = ring_parts(proj_w, "samples")
    token_sum = jnp.einsum(
        "kti,kio->to", feat_parts, proj_parts, preferred_element_type=jnp.float32
    )
    token_proj = token_sum.astype(jnp.bfloat16)
    padded_tok = extended(token_proj, (("atoms", 0),), HALO_TOK)
    first_token = atom_rank * tok_rows - HALO_TOK
    relative = atom_token - first_token
    onehot = (
        relative[:, None] == jnp.arange(tok_rows + 2 * HALO_TOK, dtype=jnp.int32)[None, :]
    ).astype(jnp.bfloat16)
    atom_base = atom_single.astype(jnp.float32) + jnp.dot(
        onehot, padded_tok, preferred_element_type=jnp.float32
    )
    sigma_col = sigma[:, None, None]
    noisy = true_coords[None] + sigma_col * noise
    noise_total = sigma_col * sigma_col + sigma_data * sigma_data
    scaled = noisy / jnp.sqrt(noise_total)
    hidden = atom_base[None] + jnp.einsum(
        "sda,dc->sac", scaled, coord_in, precision=lax.Precision.HIGHEST
    )
    key_halo = (KWIN - QBLK) // 2
    reaches = [0]
    for _ in range(LAYERS - 1):
        reaches.insert(0, -(-(reaches[0] + key_halo) // QBLK) * QBLK)
    buffer_start = -(reaches[0] + key_halo)
    hidden = extended(hidden, (("atoms", 1),), -buffer_start)
    query_win = jnp.arange(Q_TILE, dtype=jnp.int32)[:, None] // QBLK * QBLK
    key_index = jnp.arange(K_SPAN, dtype=jnp.int32)[None, :]
    band = ((key_index >= query_win) & (key_index < query_win + KWIN)).astype(jnp.float32)
    channels = hidden.shape[2]
    for layer_index in range(LAYERS):
        reach = reaches[layer_index]
        kv_off = -(reach + key_halo) - buffer_start
        q_off = kv_off + key_halo
        tiles = -(-(atom_rows + 2 * reach) // Q_TILE)
        tile_start = atom_rank * atom_rows - reach - key_halo + Q_TILE * jnp.arange(
            tiles, dtype=jnp.int32
        )
        position = tile_start[:, None] + key_index
        valid_tab = ((position >= 0) & (position < total_atoms)).astype(jnp.float32)
        normed = (rms_norm(hidden) * gains[layer_index, 0]).astype(jnp.bfloat16)
        qkv_all = dense(normed, w_qkv[layer_index]).astype(jnp.bfloat16)
        span_rows = kv_off + tiles * Q_TILE + K_SPAN - Q_TILE
        qkv_all = jnp.pad(qkv_all, ((0, 0), (0, max(0, span_rows - qkv_all.shape[1])), (0, 0)))
        queries = qkv_all[:, q_off : q_off + tiles * Q_TILE, :channels]
        key_vals = qkv_all[:, kv_off:span_rows, channels:]
        attended = jnp.stack(
            [window_attend(queries[s], key_vals[s], band, valid_tab) for s in range(samples)]
        )
        hidden = jnp.pad(hidden, ((0, 0), (0, max(0, span_rows - hidden.shape[1])), (0, 0)))
        hidden = hidden[:, q_off : q_off + tiles * Q_TILE] + dense(attended, w_o[layer_index])
        buffer_start = -reach
        normed = (rms_norm(hidden) * gains[layer_index, 1]).astype(jnp.bfloat16)
        gate_up = dense(normed, w_gu[layer_index])
        inner_act = (jax.nn.silu(gate_up[..., :FF_ATOM]) * gate_up[..., FF_ATOM:]).astype(
            jnp.bfloat16
        )
        hidden = hidden + dense(inner_act, w_down[layer_index])
    hidden = hidden[:, -buffer_start : -buffer_start + atom_rows]
    update = jnp.einsum("sac,cd->sda", rms_norm(hidden), w_out, precision=lax.Precision.HIGHEST)
    predicted = (
        sigma_data * sigma_data / noise_total * noisy
        + sigma_col * sigma_data / jnp.sqrt(noise_total) * update
    )
    mse_part = (
        2.0 / 3.0 * (noise_total / (sigma_col * sigma_data) ** 2) * (predicted - true_coords[None])
    )
    block_count = atom_rows // PAIR_BLK
    atom_peers = lax.axis_size("atoms")
    count_row = jnp.zeros((1, atom_rows), jnp.float32).at[0, 0].set(
        jnp.sum(pair_count.astype(jnp.float32) * (PAIR_BLK * PAIR_BLK) - PAIR_BLK)
    )
    coord_parts = ring_parts(jnp.concatenate([predicted[0], true_coords, count_row], axis=0), "atoms")
    pair_total = jnp.sum(coord_parts[:, 6, 0])
    own_tab = jnp.concatenate(
        [predicted[0], true_coords, jnp.zeros((2, atom_rows), jnp.float32)], axis=0
    ).T
    source = (atom_rank - pair_blocks // block_count) % atom_peers
    slots = (source * block_count + pair_blocks % block_count).reshape(-1)
    pair_grad = 2.0 * lddt_sums(slots, pair_count, own_tab, coord_parts)[None]
    lddt_grad = total_atoms * PAIR_BLK / pair_total * pair_grad.reshape(samples, 3, atom_rows)
    coord_grad = mse_part - lddt_grad / PAIR_BLK
    return (coord_grad, lddt_grad)


def solution(mesh):
    in_specs = (
        P("atoms", "samples"),
        P("samples", None),
        P("atoms", None),
        P("atoms"),
        P(None, "atoms"),
        P("samples", None, "atoms"),
        P("samples"),
        P(),
        P(),
        P(),
        P(),
        P(),
        P(),
        P(),
        P("atoms", None),
        P("atoms"),
    )
    out_specs = (P("samples", None, "atoms"), P("samples", None, "atoms"))
    return jax.shard_map(
        on_device, mesh=mesh, in_specs=in_specs, out_specs=out_specs, check_vma=False
    )
```

```python
import math

import jax
import jax.numpy as jnp
from jax import lax
from jax.experimental import pallas as pl
from jax.experimental.pallas import tpu as pltpu
from jax.sharding import PartitionSpec as P

HEADS = 4
FF_ATOM = 256
LAYERS = 3
QBLK = 32
KWIN = 128
HALO_TOK = 16
PAIR_BLK = 128


sigma_data = 2.0
norm_epsilon = 1e-05
thresholds = (0.5, 1.0, 2.0, 4.0)


def extended(value, sides, width):
    for axis, dim in sides:
        peers, length = (lax.axis_size(axis), value.shape[dim])
        up = [(i, (i + 1) % peers) for i in range(peers - 1)]
        down = [(j, i) for i, j in up]
        last = lax.slice_in_dim(value, length - width, length, axis=dim)
        first = lax.slice_in_dim(value, 0, width, axis=dim)
        before = lax.ppermute(last, axis, up)
        after = lax.ppermute(first, axis, down)
        value = jnp.concatenate([before, value, after], axis=dim)
    return value


def ring_parts(value, axis):
    peers = lax.axis_size(axis)
    parts = value[None]
    span = 1
    while span < peers and peers % (2 * span) == 0:
        pairs = [(i, (i + span) % peers) for i in range(peers)]
        parts = jnp.concatenate([parts, lax.ppermute(parts, axis, pairs)])
        span *= 2
    if span < peers:
        extra = [value[None]]
        for shift in range(span, peers):
            pairs = [(i, (i + shift) % peers) for i in range(peers)]
            extra.append(lax.ppermute(value, axis, pairs)[None])
        parts = jnp.concatenate([parts] + extra[1:])
    return parts

def rms_norm(tensor):
    return tensor * lax.rsqrt(jnp.mean(tensor * tensor, axis=-1, keepdims=True) + norm_epsilon)


Q_TILE = 128
K_SPAN = 256


def attend_kernel(q_ref, k_ref, v_ref, band_ref, valid_ref, out_ref):
    tile = pl.program_id(0)
    head_dim = q_ref.shape[2]
    scale = head_dim ** (-0.5)
    start = pl.multiple_of(tile * Q_TILE, Q_TILE)
    live = (band_ref[...] * valid_ref[pl.ds(tile, 1), :]) > 0.0
    for head in range(HEADS):
        keys = k_ref[head, pl.ds(start, K_SPAN), :]
        scores = lax.dot_general(
            q_ref[head], keys, (((1,), (1,)), ((), ())), preferred_element_type=jnp.float32
        )
        scores = jnp.where(live, scores, -1e30)
        row_max = jnp.max(scores, axis=-1, keepdims=True)
        exp_scores = jnp.exp2((scores - row_max) * (scale * math.log2(math.e)))
        inverse = 1.0 / jnp.sum(exp_scores, axis=-1, keepdims=True)
        weights = (exp_scores * inverse).astype(jnp.bfloat16)
        values = v_ref[head, pl.ds(start, K_SPAN), :]
        out_ref[head] = jnp.dot(weights, values, preferred_element_type=jnp.float32).astype(
            jnp.bfloat16
        )


def head_major(block):
    rows, channels = block.shape
    return block.reshape(rows, HEADS, channels // HEADS).transpose(1, 0, 2)


def window_attend(queries, padded_kv, band, valid_tab):
    atoms, channels = queries.shape
    extra = atoms + K_SPAN - Q_TILE - padded_kv.shape[0]
    padded_kv = jnp.pad(padded_kv, ((0, extra), (0, 0)))
    q_heads = head_major(queries)
    k_heads = head_major(padded_kv[:, :channels])
    v_heads = head_major(padded_kv[:, channels:])
    head_dim = channels // HEADS
    out = pl.pallas_call(
        attend_kernel,
        grid=(atoms // Q_TILE,),
        in_specs=[
            pl.BlockSpec((HEADS, Q_TILE, head_dim), lambda t: (0, t, 0)),
            pl.BlockSpec(k_heads.shape, lambda t: (0, 0, 0)),
            pl.BlockSpec(v_heads.shape, lambda t: (0, 0, 0)),
            pl.BlockSpec(band.shape, lambda t: (0, 0)),
            pl.BlockSpec(valid_tab.shape, lambda t: (0, 0)),
        ],
        out_specs=pl.BlockSpec((HEADS, Q_TILE, head_dim), lambda t: (0, t, 0)),
        out_shape=jax.ShapeDtypeStruct((HEADS, atoms, head_dim), jnp.bfloat16),
    )(q_heads, k_heads, v_heads, band, valid_tab)
    return out.transpose(1, 0, 2).reshape(atoms, channels)

ROW_CHUNK = 64


def lddt_kernel(slots_ref, count_ref, own_ref, coord_ref, out_ref, cols_ref):
    block = pl.program_id(0)
    live = count_ref[block]
    blocks = count_ref.shape[0]
    max_slots = slots_ref.shape[0] // blocks
    shape = (ROW_CHUNK, PAIR_BLK)
    lane = lax.broadcasted_iota(jnp.int32, shape, 1)
    for chunk in range(PAIR_BLK // ROW_CHUNK):
        rows = slice(chunk * ROW_CHUNK, (chunk + 1) * ROW_CHUNK)
        own = own_ref[rows, :]
        for d in range(6):
            cols_ref[d, rows, :] = jnp.broadcast_to(own[:, d : d + 1], shape)

    def row_body(row_index, carry):
        row = pl.multiple_of(row_index * ROW_CHUNK, ROW_CHUNK)

        def slot_body(slot_index, accs):
            slot = slots_ref[block * max_slots + slot_index]
            peer = slot // blocks
            start = pl.multiple_of((slot % blocks) * PAIR_BLK, PAIR_BLK)
            part = coord_ref[peer, :, pl.ds(start, PAIR_BLK)]
            part_pred = part[0:3]
            part_true = part[3:6]
            gaps = [cols_ref[d, pl.ds(row, ROW_CHUNK), :] - part_pred[d : d + 1, :] for d in range(3)]
            true_gaps = [
                cols_ref[3 + d, pl.ds(row, ROW_CHUNK), :] - part_true[d : d + 1, :] for d in range(3)
            ]
            square_pred = gaps[0] * gaps[0] + gaps[1] * gaps[1] + gaps[2] * gaps[2] + 1.0
            square_true = (
                true_gaps[0] * true_gaps[0] + true_gaps[1] * true_gaps[1] + true_gaps[2] * true_gaps[2]
            ) + 1.0
            inv_pred = lax.rsqrt(square_pred)
            gap_dist = square_pred * inv_pred - square_true * lax.rsqrt(square_true)
            square_err = gap_dist * gap_dist + 0.01
            inv_err = lax.rsqrt(square_err)
            decay = jnp.exp(-(square_err * inv_err))
            ys = [decay * math.exp(t) for t in thresholds]
            dens = [(1.0 + y) * (1.0 + y) for y in ys]
            low = dens[0] * dens[1]
            high = dens[2] * dens[3]
            numer = (ys[0] * dens[1] + ys[1] * dens[0]) * high + (ys[2] * dens[3] + ys[3] * dens[2]) * low
            coef = (numer * gap_dist * (inv_err * inv_pred)) / (low * high)
            return tuple(acc + coef * gap for acc, gap in zip(accs, gaps))

        zero = jnp.zeros(shape, jnp.float32)
        accs = lax.fori_loop(0, live, slot_body, (zero, zero, zero))
        sums = [-0.25 * jnp.sum(acc, axis=1, keepdims=True) for acc in accs]
        tile = jnp.where(lane == 0, sums[0], jnp.where(lane == 1, sums[1], jnp.where(lane == 2, sums[2], 0.0)))
        out_ref[pl.ds(row, ROW_CHUNK), :] = tile
        return carry

    lax.fori_loop(0, PAIR_BLK // ROW_CHUNK, row_body, 0)


def lddt_sums(slots, counts, own_tab, coord_parts):
    blocks = counts.shape[0]
    out = pl.pallas_call(
        lddt_kernel,
        grid_spec=pltpu.PrefetchScalarGridSpec(
            num_scalar_prefetch=2,
            grid=(blocks,),
            in_specs=[
                pl.BlockSpec((PAIR_BLK, own_tab.shape[1]), lambda b, *_: (b, 0)),
                pl.BlockSpec(coord_parts.shape, lambda b, *_: (0, 0, 0)),
            ],
            out_specs=pl.BlockSpec((PAIR_BLK, PAIR_BLK), lambda b, *_: (b, 0)),
            scratch_shapes=[pltpu.VMEM((6, PAIR_BLK, PAIR_BLK), jnp.float32)],
        ),
        out_shape=jax.ShapeDtypeStruct((blocks * PAIR_BLK, PAIR_BLK), jnp.float32),
    )(slots, counts, own_tab, coord_parts)
    return out[:, :3].T

def dense(left, right):
    return jnp.einsum("sac,cf->saf", left, right, preferred_element_type=jnp.float32)


def on_device(
    token_feats,
    proj_w,
    atom_single,
    atom_token,
    true_coords,
    noise,
    sigma,
    coord_in,
    w_qkv,
    w_o,
    w_gu,
    w_down,
    gains,
    w_out,
    pair_blocks,
    pair_count,
):
    atom_rank = lax.axis_index("atoms")
    tok_rows = token_feats.shape[0]
    atom_rows = atom_single.shape[0]
    total_atoms = atom_rows * lax.axis_size("atoms")
    samples = noise.shape[0]
    feat_parts = ring_parts(token_feats, "samples")
    proj_parts = ring_parts(proj_w, "samples")
    token_sum = jnp.einsum(
        "kti,kio->to", feat_parts, proj_parts, preferred_element_type=jnp.float32
    )
    token_proj = token_sum.astype(jnp.bfloat16)
    padded_tok = extended(token_proj, (("atoms", 0),), HALO_TOK)
    first_token = atom_rank * tok_rows - HALO_TOK
    relative = atom_token - first_token
    onehot = (
        relative[:, None] == jnp.arange(tok_rows + 2 * HALO_TOK, dtype=jnp.int32)[None, :]
    ).astype(jnp.bfloat16)
    atom_base = atom_single.astype(jnp.float32) + jnp.dot(
        onehot, padded_tok, preferred_element_type=jnp.float32
    )
    sigma_col = sigma[:, None, None]
    noisy = true_coords[None] + sigma_col * noise
    noise_total = sigma_col * sigma_col + sigma_data * sigma_data
    scaled = noisy / jnp.sqrt(noise_total)
    hidden = atom_base[None] + jnp.einsum(
        "sda,dc->sac", scaled, coord_in, precision=lax.Precision.HIGHEST
    )
    key_halo = (KWIN - QBLK) // 2
    reaches = [0]
    for _ in range(LAYERS - 1):
        reaches.insert(0, -(-(reaches[0] + key_halo) // QBLK) * QBLK)
    buffer_start = -(reaches[0] + key_halo)
    hidden = extended(hidden, (("atoms", 1),), -buffer_start)
    query_win = jnp.arange(Q_TILE, dtype=jnp.int32)[:, None] // QBLK * QBLK
    key_index = jnp.arange(K_SPAN, dtype=jnp.int32)[None, :]
    band = ((key_index >= query_win) & (key_index < query_win + KWIN)).astype(jnp.float32)
    channels = hidden.shape[2]
    for layer_index in range(LAYERS):
        reach = reaches[layer_index]
        kv_off = -(reach + key_halo) - buffer_start
        q_off = kv_off + key_halo
        tiles = -(-(atom_rows + 2 * reach) // Q_TILE)
        tile_start = atom_rank * atom_rows - reach - key_halo + Q_TILE * jnp.arange(
            tiles, dtype=jnp.int32
        )
        position = tile_start[:, None] + key_index
        valid_tab = ((position >= 0) & (position < total_atoms)).astype(jnp.float32)
        normed = (rms_norm(hidden) * gains[layer_index, 0]).astype(jnp.bfloat16)
        qkv_all = dense(normed, w_qkv[layer_index]).astype(jnp.bfloat16)
        span_rows = kv_off + tiles * Q_TILE + K_SPAN - Q_TILE
        qkv_all = jnp.pad(qkv_all, ((0, 0), (0, max(0, span_rows - qkv_all.shape[1])), (0, 0)))
        queries = qkv_all[:, q_off : q_off + tiles * Q_TILE, :channels]
        key_vals = qkv_all[:, kv_off:span_rows, channels:]
        attended = jnp.stack(
            [window_attend(queries[s], key_vals[s], band, valid_tab) for s in range(samples)]
        )
        hidden = jnp.pad(hidden, ((0, 0), (0, max(0, span_rows - hidden.shape[1])), (0, 0)))
        hidden = hidden[:, q_off : q_off + tiles * Q_TILE] + dense(attended, w_o[layer_index])
        buffer_start = -reach
        normed = (rms_norm(hidden) * gains[layer_index, 1]).astype(jnp.bfloat16)
        gate_up = dense(normed, w_gu[layer_index])
        inner_act = (jax.nn.silu(gate_up[..., :FF_ATOM]) * gate_up[..., FF_ATOM:]).astype(
            jnp.bfloat16
        )
        hidden = hidden + dense(inner_act, w_down[layer_index])
    hidden = hidden[:, -buffer_start : -buffer_start + atom_rows]
    update = jnp.einsum("sac,cd->sda", rms_norm(hidden), w_out, precision=lax.Precision.HIGHEST)
    predicted = (
        sigma_data * sigma_data / noise_total * noisy
        + sigma_col * sigma_data / jnp.sqrt(noise_total) * update
    )
    mse_part = (
        2.0 / 3.0 * (noise_total / (sigma_col * sigma_data) ** 2) * (predicted - true_coords[None])
    )
    block_count = atom_rows // PAIR_BLK
    atom_peers = lax.axis_size("atoms")
    count_row = jnp.zeros((1, atom_rows), jnp.float32).at[0, 0].set(
        jnp.sum(pair_count.astype(jnp.float32) * (PAIR_BLK * PAIR_BLK) - PAIR_BLK)
    )
    coord_parts = ring_parts(jnp.concatenate([predicted[0], true_coords, count_row], axis=0), "atoms")
    pair_total = jnp.sum(coord_parts[:, 6, 0])
    own_tab = jnp.concatenate(
        [predicted[0], true_coords, jnp.zeros((2, atom_rows), jnp.float32)], axis=0
    ).T
    source = (atom_rank - pair_blocks // block_count) % atom_peers
    slots = (source * block_count + pair_blocks % block_count).reshape(-1)
    pair_grad = 2.0 * lddt_sums(slots, pair_count, own_tab, coord_parts)[None]
    lddt_grad = total_atoms * PAIR_BLK / pair_total * pair_grad.reshape(samples, 3, atom_rows)
    coord_grad = mse_part - lddt_grad / PAIR_BLK
    return (coord_grad, lddt_grad)


def solution(mesh):
    in_specs = (
        P("atoms", "samples"),
        P("samples", None),
        P("atoms", None),
        P("atoms"),
        P(None, "atoms"),
        P("samples", None, "atoms"),
        P("samples"),
        P(),
        P(),
        P(),
        P(),
        P(),
        P(),
        P(),
        P("atoms", None),
        P("atoms"),
    )
    out_specs = (P("samples", None, "atoms"), P("samples", None, "atoms"))
    return jax.shard_map(
        on_device, mesh=mesh, in_specs=in_specs, out_specs=out_specs, check_vma=False
    )
```

```python
import math

import jax
import jax.numpy as jnp
from jax import lax
from jax.experimental import pallas as pl
from jax.experimental.pallas import tpu as pltpu
from jax.sharding import PartitionSpec as P

HEADS = 4
FF_ATOM = 256
LAYERS = 3
QBLK = 32
KWIN = 128
HALO_TOK = 16
PAIR_BLK = 128


sigma_data = 2.0
norm_epsilon = 1e-05
thresholds = (0.5, 1.0, 2.0, 4.0)


def extended(value, sides, width):
    for axis, dim in sides:
        peers, length = (lax.axis_size(axis), value.shape[dim])
        up = [(i, (i + 1) % peers) for i in range(peers - 1)]
        down = [(j, i) for i, j in up]
        last = lax.slice_in_dim(value, length - width, length, axis=dim)
        first = lax.slice_in_dim(value, 0, width, axis=dim)
        before = lax.ppermute(last, axis, up)
        after = lax.ppermute(first, axis, down)
        value = jnp.concatenate([before, value, after], axis=dim)
    return value


def ring_parts(value, axis, direct=False):
    peers = lax.axis_size(axis)
    parts = value[None]
    span = 1
    while not direct and span < peers and peers % (2 * span) == 0:
        pairs = [(i, (i + span) % peers) for i in range(peers)]
        parts = jnp.concatenate([parts, lax.ppermute(parts, axis, pairs)])
        span *= 2
    if span < peers:
        extra = [value[None]]
        for shift in range(span, peers):
            pairs = [(i, (i + shift) % peers) for i in range(peers)]
            extra.append(lax.ppermute(value, axis, pairs)[None])
        parts = jnp.concatenate([parts] + extra[1:])
    return parts

def rms_norm(tensor):
    return tensor * lax.rsqrt(jnp.mean(tensor * tensor, axis=-1, keepdims=True) + norm_epsilon)


Q_TILE = 128
K_SPAN = 256


def attend_kernel(q_ref, kv_ref, band_ref, valid_ref, out_ref):
    tile = pl.program_id(0)
    head_dim = q_ref.shape[1] // HEADS
    channels = q_ref.shape[1]
    scale = head_dim ** (-0.5)
    start = pl.multiple_of(tile * Q_TILE, Q_TILE)
    keys_vals = kv_ref[pl.ds(start, K_SPAN), :]
    live = (band_ref[...] * valid_ref[pl.ds(tile, 1), :]) > 0.0
    query_rows = q_ref[...]
    heads = []
    for head in range(HEADS):
        cols = slice(head * head_dim, (head + 1) * head_dim)
        vcols = slice(channels + head * head_dim, channels + (head + 1) * head_dim)
        scores = lax.dot_general(
            query_rows[:, cols], keys_vals[:, cols], (((1,), (1,)), ((), ())),
            preferred_element_type=jnp.float32,
        )
        scores = jnp.where(live, scores, -1e30)
        row_max = jnp.max(scores, axis=-1, keepdims=True)
        exp_scores = jnp.exp2((scores - row_max) * (scale * math.log2(math.e)))
        inverse = 1.0 / jnp.sum(exp_scores, axis=-1, keepdims=True)
        weights = (exp_scores * inverse).astype(jnp.bfloat16)
        heads.append(
            jnp.dot(weights, keys_vals[:, vcols], preferred_element_type=jnp.float32).astype(
                jnp.bfloat16
            )
        )
    out_ref[...] = jnp.concatenate(heads, axis=1)


def window_attend(queries, padded_kv, band, valid_tab):
    atoms, channels = queries.shape
    extra = atoms + K_SPAN - Q_TILE - padded_kv.shape[0]
    padded_kv = jnp.pad(padded_kv, ((0, extra), (0, 0)))
    return pl.pallas_call(
        attend_kernel,
        grid=(atoms // Q_TILE,),
        in_specs=[
            pl.BlockSpec((Q_TILE, channels), lambda t: (t, 0)),
            pl.BlockSpec(padded_kv.shape, lambda t: (0, 0)),
            pl.BlockSpec(band.shape, lambda t: (0, 0)),
            pl.BlockSpec(valid_tab.shape, lambda t: (0, 0)),
        ],
        out_specs=pl.BlockSpec((Q_TILE, channels), lambda t: (t, 0)),
        out_shape=jax.ShapeDtypeStruct((atoms, channels), jnp.bfloat16),
    )(queries, padded_kv, band, valid_tab)

ROW_CHUNK = 64


def lddt_kernel(slots_ref, count_ref, own_ref, coord_ref, out_ref, cols_ref):
    block = pl.program_id(0)
    live = count_ref[block]
    blocks = count_ref.shape[0]
    max_slots = slots_ref.shape[0] // blocks
    shape = (ROW_CHUNK, PAIR_BLK)
    lane = lax.broadcasted_iota(jnp.int32, shape, 1)
    for chunk in range(PAIR_BLK // ROW_CHUNK):
        rows = slice(chunk * ROW_CHUNK, (chunk + 1) * ROW_CHUNK)
        own = own_ref[rows, :]
        for d in range(6):
            cols_ref[d, rows, :] = jnp.broadcast_to(own[:, d : d + 1], shape)

    def row_body(row_index, carry):
        row = pl.multiple_of(row_index * ROW_CHUNK, ROW_CHUNK)

        def slot_body(slot_index, accs):
            slot = slots_ref[block * max_slots + slot_index]
            peer = slot // blocks
            start = pl.multiple_of((slot % blocks) * PAIR_BLK, PAIR_BLK)
            part = coord_ref[peer, :, pl.ds(start, PAIR_BLK)]
            part_pred = part[0:3]
            part_true = part[3:6]
            gaps = [cols_ref[d, pl.ds(row, ROW_CHUNK), :] - part_pred[d : d + 1, :] for d in range(3)]
            true_gaps = [
                cols_ref[3 + d, pl.ds(row, ROW_CHUNK), :] - part_true[d : d + 1, :] for d in range(3)
            ]
            square_pred = gaps[0] * gaps[0] + gaps[1] * gaps[1] + gaps[2] * gaps[2] + 1.0
            square_true = (
                true_gaps[0] * true_gaps[0] + true_gaps[1] * true_gaps[1] + true_gaps[2] * true_gaps[2]
            ) + 1.0
            inv_pred = lax.rsqrt(square_pred)
            gap_dist = square_pred * inv_pred - square_true * lax.rsqrt(square_true)
            square_err = gap_dist * gap_dist + 0.01
            inv_err = lax.rsqrt(square_err)
            decay = jnp.exp(-(square_err * inv_err))
            ys = [decay * math.exp(t) for t in thresholds]
            dens = [(1.0 + y) * (1.0 + y) for y in ys]
            low = dens[0] * dens[1]
            high = dens[2] * dens[3]
            numer = (ys[0] * dens[1] + ys[1] * dens[0]) * high + (ys[2] * dens[3] + ys[3] * dens[2]) * low
            coef = (numer * gap_dist * (inv_err * inv_pred)) / (low * high)
            return tuple(acc + coef * gap for acc, gap in zip(accs, gaps))

        zero = jnp.zeros(shape, jnp.float32)
        accs = lax.fori_loop(0, live, slot_body, (zero, zero, zero))
        sums = [-0.25 * jnp.sum(acc, axis=1, keepdims=True) for acc in accs]
        tile = jnp.where(lane == 0, sums[0], jnp.where(lane == 1, sums[1], jnp.where(lane == 2, sums[2], 0.0)))
        out_ref[pl.ds(row, ROW_CHUNK), :] = tile
        return carry

    lax.fori_loop(0, PAIR_BLK // ROW_CHUNK, row_body, 0)


def lddt_sums(slots, counts, own_tab, coord_parts):
    blocks = counts.shape[0]
    out = pl.pallas_call(
        lddt_kernel,
        grid_spec=pltpu.PrefetchScalarGridSpec(
            num_scalar_prefetch=2,
            grid=(blocks,),
            in_specs=[
                pl.BlockSpec((PAIR_BLK, own_tab.shape[1]), lambda b, *_: (b, 0)),
                pl.BlockSpec(coord_parts.shape, lambda b, *_: (0, 0, 0)),
            ],
            out_specs=pl.BlockSpec((PAIR_BLK, PAIR_BLK), lambda b, *_: (b, 0)),
            scratch_shapes=[pltpu.VMEM((6, PAIR_BLK, PAIR_BLK), jnp.float32)],
        ),
        out_shape=jax.ShapeDtypeStruct((blocks * PAIR_BLK, PAIR_BLK), jnp.float32),
    )(slots, counts, own_tab, coord_parts)
    return out[:, :3].T

def dense(left, right):
    return jnp.einsum("sac,cf->saf", left, right, preferred_element_type=jnp.float32)


def on_device(
    token_feats,
    proj_w,
    atom_single,
    atom_token,
    true_coords,
    noise,
    sigma,
    coord_in,
    w_qkv,
    w_o,
    w_gu,
    w_down,
    gains,
    w_out,
    pair_blocks,
    pair_count,
):
    atom_rank = lax.axis_index("atoms")
    tok_rows = token_feats.shape[0]
    atom_rows = atom_single.shape[0]
    total_atoms = atom_rows * lax.axis_size("atoms")
    samples = noise.shape[0]
    feat_parts = ring_parts(token_feats, "samples", direct=True)
    proj_parts = ring_parts(proj_w, "samples", direct=True)
    token_sum = jnp.einsum(
        "kti,kio->to", feat_parts, proj_parts, preferred_element_type=jnp.float32
    )
    token_proj = token_sum.astype(jnp.bfloat16)
    padded_tok = extended(token_proj, (("atoms", 0),), HALO_TOK)
    first_token = atom_rank * tok_rows - HALO_TOK
    relative = atom_token - first_token
    onehot = (
        relative[:, None] == jnp.arange(tok_rows + 2 * HALO_TOK, dtype=jnp.int32)[None, :]
    ).astype(jnp.bfloat16)
    atom_base = atom_single.astype(jnp.float32) + jnp.dot(
        onehot, padded_tok, preferred_element_type=jnp.float32
    )
    sigma_col = sigma[:, None, None]
    noisy = true_coords[None] + sigma_col * noise
    noise_total = sigma_col * sigma_col + sigma_data * sigma_data
    scaled = noisy / jnp.sqrt(noise_total)
    hidden = atom_base[None] + jnp.einsum(
        "sda,dc->sac", scaled, coord_in, precision=lax.Precision.HIGHEST
    )
    key_halo = (KWIN - QBLK) // 2
    reaches = [0]
    for _ in range(LAYERS - 1):
        reaches.insert(0, -(-(reaches[0] + key_halo) // QBLK) * QBLK)
    buffer_start = -(reaches[0] + key_halo)
    hidden = extended(hidden, (("atoms", 1),), -buffer_start)
    query_win = jnp.arange(Q_TILE, dtype=jnp.int32)[:, None] // QBLK * QBLK
    key_index = jnp.arange(K_SPAN, dtype=jnp.int32)[None, :]
    band = ((key_index >= query_win) & (key_index < query_win + KWIN)).astype(jnp.float32)
    channels = hidden.shape[2]
    for layer_index in range(LAYERS):
        reach = reaches[layer_index]
        kv_off = -(reach + key_halo) - buffer_start
        q_off = kv_off + key_halo
        tiles = -(-(atom_rows + 2 * reach) // Q_TILE)
        tile_start = atom_rank * atom_rows - reach - key_halo + Q_TILE * jnp.arange(
            tiles, dtype=jnp.int32
        )
        position = tile_start[:, None] + key_index
        valid_tab = ((position >= 0) & (position < total_atoms)).astype(jnp.float32)
        normed = (rms_norm(hidden) * gains[layer_index, 0]).astype(jnp.bfloat16)
        qkv_all = dense(normed, w_qkv[layer_index]).astype(jnp.bfloat16)
        span_rows = kv_off + tiles * Q_TILE + K_SPAN - Q_TILE
        qkv_all = jnp.pad(qkv_all, ((0, 0), (0, max(0, span_rows - qkv_all.shape[1])), (0, 0)))
        queries = qkv_all[:, q_off : q_off + tiles * Q_TILE, :channels]
        key_vals = qkv_all[:, kv_off:span_rows, channels:]
        attended = jnp.stack(
            [window_attend(queries[s], key_vals[s], band, valid_tab) for s in range(samples)]
        )
        hidden = jnp.pad(hidden, ((0, 0), (0, max(0, span_rows - hidden.shape[1])), (0, 0)))
        hidden = hidden[:, q_off : q_off + tiles * Q_TILE] + dense(attended, w_o[layer_index])
        buffer_start = -reach
        normed = (rms_norm(hidden) * gains[layer_index, 1]).astype(jnp.bfloat16)
        gate_up = dense(normed, w_gu[layer_index])
        inner_act = (jax.nn.silu(gate_up[..., :FF_ATOM]) * gate_up[..., FF_ATOM:]).astype(
            jnp.bfloat16
        )
        hidden = hidden + dense(inner_act, w_down[layer_index])
    hidden = hidden[:, -buffer_start : -buffer_start + atom_rows]
    update = jnp.einsum("sac,cd->sda", rms_norm(hidden), w_out, precision=lax.Precision.HIGHEST)
    predicted = (
        sigma_data * sigma_data / noise_total * noisy
        + sigma_col * sigma_data / jnp.sqrt(noise_total) * update
    )
    mse_part = (
        2.0 / 3.0 * (noise_total / (sigma_col * sigma_data) ** 2) * (predicted - true_coords[None])
    )
    block_count = atom_rows // PAIR_BLK
    atom_peers = lax.axis_size("atoms")
    count_row = jnp.zeros((1, atom_rows), jnp.float32).at[0, 0].set(
        jnp.sum(pair_count.astype(jnp.float32) * (PAIR_BLK * PAIR_BLK) - PAIR_BLK)
    )
    coord_parts = ring_parts(jnp.concatenate([predicted[0], true_coords, count_row], axis=0), "atoms")
    pair_total = jnp.sum(coord_parts[:, 6, 0])
    own_tab = jnp.concatenate(
        [predicted[0], true_coords, jnp.zeros((2, atom_rows), jnp.float32)], axis=0
    ).T
    source = (atom_rank - pair_blocks // block_count) % atom_peers
    slots = (source * block_count + pair_blocks % block_count).reshape(-1)
    pair_grad = 2.0 * lddt_sums(slots, pair_count, own_tab, coord_parts)[None]
    lddt_grad = total_atoms * PAIR_BLK / pair_total * pair_grad.reshape(samples, 3, atom_rows)
    coord_grad = mse_part - lddt_grad / PAIR_BLK
    return (coord_grad, lddt_grad)


def solution(mesh):
    in_specs = (
        P("atoms", "samples"),
        P("samples", None),
        P("atoms", None),
        P("atoms"),
        P(None, "atoms"),
        P("samples", None, "atoms"),
        P("samples"),
        P(),
        P(),
        P(),
        P(),
        P(),
        P(),
        P(),
        P("atoms", None),
        P("atoms"),
    )
    out_specs = (P("samples", None, "atoms"), P("samples", None, "atoms"))
    return jax.shard_map(
        on_device, mesh=mesh, in_specs=in_specs, out_specs=out_specs, check_vma=False
    )
```

```python
import math

import jax
import jax.numpy as jnp
from jax import lax
from jax.experimental import pallas as pl
from jax.experimental.pallas import tpu as pltpu
from jax.sharding import PartitionSpec as P

HEADS = 4
FF_ATOM = 256
LAYERS = 3
QBLK = 32
KWIN = 128
HALO_TOK = 16
PAIR_BLK = 128


sigma_data = 2.0
norm_epsilon = 1e-05
thresholds = (0.5, 1.0, 2.0, 4.0)


def extended(value, sides, width):
    for axis, dim in sides:
        peers, length = (lax.axis_size(axis), value.shape[dim])
        up = [(i, (i + 1) % peers) for i in range(peers - 1)]
        down = [(j, i) for i, j in up]
        last = lax.slice_in_dim(value, length - width, length, axis=dim)
        first = lax.slice_in_dim(value, 0, width, axis=dim)
        before = lax.ppermute(last, axis, up)
        after = lax.ppermute(first, axis, down)
        value = jnp.concatenate([before, value, after], axis=dim)
    return value


def ring_parts(value, axis):
    peers = lax.axis_size(axis)
    parts = value[None]
    span = 1
    while span < peers and peers % (2 * span) == 0:
        pairs = [(i, (i + span) % peers) for i in range(peers)]
        parts = jnp.concatenate([parts, lax.ppermute(parts, axis, pairs)])
        span *= 2
    if span < peers:
        extra = [value[None]]
        for shift in range(span, peers):
            pairs = [(i, (i + shift) % peers) for i in range(peers)]
            extra.append(lax.ppermute(value, axis, pairs)[None])
        parts = jnp.concatenate([parts] + extra[1:])
    return parts

def rms_norm(tensor):
    return tensor * lax.rsqrt(jnp.mean(tensor * tensor, axis=-1, keepdims=True) + norm_epsilon)


Q_TILE = 128
K_SPAN = 256


def attend_kernel(q_ref, kv_ref, band_ref, valid_ref, out_ref):
    tile = pl.program_id(0)
    head_dim = q_ref.shape[1] // HEADS
    channels = q_ref.shape[1]
    scale = head_dim ** (-0.5)
    start = pl.multiple_of(tile * Q_TILE, Q_TILE)
    keys_vals = kv_ref[pl.ds(start, K_SPAN), :]
    live = (band_ref[...] * valid_ref[pl.ds(tile, 1), :]) > 0.0
    query_rows = q_ref[...]
    heads = []
    for head in range(HEADS):
        cols = slice(head * head_dim, (head + 1) * head_dim)
        vcols = slice(channels + head * head_dim, channels + (head + 1) * head_dim)
        scores = lax.dot_general(
            query_rows[:, cols], keys_vals[:, cols], (((1,), (1,)), ((), ())),
            preferred_element_type=jnp.float32,
        )
        scores = jnp.where(live, scores, -1e30)
        row_max = jnp.max(scores, axis=-1, keepdims=True)
        exp_scores = jnp.exp2((scores - row_max) * (scale * math.log2(math.e)))
        inverse = 1.0 / jnp.sum(exp_scores, axis=-1, keepdims=True)
        weights = (exp_scores * inverse).astype(jnp.bfloat16)
        heads.append(
            jnp.dot(weights, keys_vals[:, vcols], preferred_element_type=jnp.float32).astype(
                jnp.bfloat16
            )
        )
    out_ref[...] = jnp.concatenate(heads, axis=1)


def window_attend(queries, padded_kv, band, valid_tab):
    atoms, channels = queries.shape
    extra = atoms + K_SPAN - Q_TILE - padded_kv.shape[0]
    padded_kv = jnp.pad(padded_kv, ((0, extra), (0, 0)))
    return pl.pallas_call(
        attend_kernel,
        grid=(atoms // Q_TILE,),
        in_specs=[
            pl.BlockSpec((Q_TILE, channels), lambda t: (t, 0)),
            pl.BlockSpec(padded_kv.shape, lambda t: (0, 0)),
            pl.BlockSpec(band.shape, lambda t: (0, 0)),
            pl.BlockSpec(valid_tab.shape, lambda t: (0, 0)),
        ],
        out_specs=pl.BlockSpec((Q_TILE, channels), lambda t: (t, 0)),
        out_shape=jax.ShapeDtypeStruct((atoms, channels), jnp.bfloat16),
    )(queries, padded_kv, band, valid_tab)

ROW_CHUNK = 64


def lddt_kernel(slots_ref, lo_ref, count_ref, own_ref, coord_ref, out_ref, cols_ref):
    block = pl.program_id(0)
    live = count_ref[block]
    first = lo_ref[block]
    blocks = count_ref.shape[0]
    max_slots = slots_ref.shape[0] // blocks
    shape = (ROW_CHUNK, PAIR_BLK)
    lane = lax.broadcasted_iota(jnp.int32, shape, 1)
    for chunk in range(PAIR_BLK // ROW_CHUNK):
        rows = slice(chunk * ROW_CHUNK, (chunk + 1) * ROW_CHUNK)
        own = own_ref[rows, :]
        for d in range(6):
            cols_ref[d, rows, :] = jnp.broadcast_to(own[:, d : d + 1], shape)

    def row_body(row_index, carry):
        row = pl.multiple_of(row_index * ROW_CHUNK, ROW_CHUNK)

        def slot_body(slot_index, accs):
            slot = slots_ref[block * max_slots + slot_index]
            peer = slot // blocks
            start = pl.multiple_of((slot % blocks) * PAIR_BLK, PAIR_BLK)
            part = coord_ref[peer, :, pl.ds(start, PAIR_BLK)]
            part_pred = part[0:3]
            part_true = part[3:6]
            gaps = [cols_ref[d, pl.ds(row, ROW_CHUNK), :] - part_pred[d : d + 1, :] for d in range(3)]
            true_gaps = [
                cols_ref[3 + d, pl.ds(row, ROW_CHUNK), :] - part_true[d : d + 1, :] for d in range(3)
            ]
            square_pred = gaps[0] * gaps[0] + gaps[1] * gaps[1] + gaps[2] * gaps[2] + 1.0
            square_true = (
                true_gaps[0] * true_gaps[0] + true_gaps[1] * true_gaps[1] + true_gaps[2] * true_gaps[2]
            ) + 1.0
            inv_pred = lax.rsqrt(square_pred)
            gap_dist = square_pred * inv_pred - square_true * lax.rsqrt(square_true)
            square_err = gap_dist * gap_dist + 0.01
            inv_err = lax.rsqrt(square_err)
            decay = jnp.exp(-(square_err * inv_err))
            ys = [decay * math.exp(t) for t in thresholds]
            dens = [(1.0 + y) * (1.0 + y) for y in ys]
            low = dens[0] * dens[1]
            high = dens[2] * dens[3]
            numer = (ys[0] * dens[1] + ys[1] * dens[0]) * high + (ys[2] * dens[3] + ys[3] * dens[2]) * low
            coef = (numer * gap_dist * (inv_err * inv_pred)) / (low * high)
            return tuple(acc + coef * gap for acc, gap in zip(accs, gaps))

        zero = jnp.zeros(shape, jnp.float32)
        accs = lax.fori_loop(first, live, slot_body, (zero, zero, zero))
        sums = [-0.25 * jnp.sum(acc, axis=1, keepdims=True) for acc in accs]
        tile = jnp.where(lane == 0, sums[0], jnp.where(lane == 1, sums[1], jnp.where(lane == 2, sums[2], 0.0)))
        out_ref[pl.ds(row, ROW_CHUNK), :] = tile
        return carry

    lax.fori_loop(0, PAIR_BLK // ROW_CHUNK, row_body, 0)


def lddt_sums(slots, lows, counts, own_tab, coord_parts):
    blocks = counts.shape[0]
    out = pl.pallas_call(
        lddt_kernel,
        grid_spec=pltpu.PrefetchScalarGridSpec(
            num_scalar_prefetch=3,
            grid=(blocks,),
            in_specs=[
                pl.BlockSpec((PAIR_BLK, own_tab.shape[1]), lambda b, *_: (b, 0)),
                pl.BlockSpec(coord_parts.shape, lambda b, *_: (0, 0, 0)),
            ],
            out_specs=pl.BlockSpec((PAIR_BLK, PAIR_BLK), lambda b, *_: (b, 0)),
            scratch_shapes=[pltpu.VMEM((6, PAIR_BLK, PAIR_BLK), jnp.float32)],
        ),
        out_shape=jax.ShapeDtypeStruct((blocks * PAIR_BLK, PAIR_BLK), jnp.float32),
    )(slots, lows, counts, own_tab, coord_parts)
    return out[:, :3].T

def dense(left, right):
    return jnp.einsum("sac,cf->saf", left, right, preferred_element_type=jnp.float32)


def on_device(
    token_feats,
    proj_w,
    atom_single,
    atom_token,
    true_coords,
    noise,
    sigma,
    coord_in,
    w_qkv,
    w_o,
    w_gu,
    w_down,
    gains,
    w_out,
    pair_blocks,
    pair_count,
):
    atom_rank = lax.axis_index("atoms")
    tok_rows = token_feats.shape[0]
    atom_rows = atom_single.shape[0]
    total_atoms = atom_rows * lax.axis_size("atoms")
    samples = noise.shape[0]
    feat_parts = ring_parts(token_feats, "samples")
    proj_parts = ring_parts(proj_w, "samples")
    token_sum = jnp.einsum(
        "kti,kio->to", feat_parts, proj_parts, preferred_element_type=jnp.float32
    )
    token_proj = token_sum.astype(jnp.bfloat16)
    padded_tok = extended(token_proj, (("atoms", 0),), HALO_TOK)
    first_token = atom_rank * tok_rows - HALO_TOK
    relative = atom_token - first_token
    onehot = (
        relative[:, None] == jnp.arange(tok_rows + 2 * HALO_TOK, dtype=jnp.int32)[None, :]
    ).astype(jnp.bfloat16)
    atom_base = atom_single.astype(jnp.float32) + jnp.dot(
        onehot, padded_tok, preferred_element_type=jnp.float32
    )
    sigma_col = sigma[:, None, None]
    noisy = true_coords[None] + sigma_col * noise
    noise_total = sigma_col * sigma_col + sigma_data * sigma_data
    scaled = noisy / jnp.sqrt(noise_total)
    hidden = atom_base[None] + jnp.einsum(
        "sda,dc->sac", scaled, coord_in, precision=lax.Precision.HIGHEST
    )
    key_halo = (KWIN - QBLK) // 2
    reaches = [0]
    for _ in range(LAYERS - 1):
        reaches.insert(0, -(-(reaches[0] + key_halo) // QBLK) * QBLK)
    buffer_start = -(reaches[0] + key_halo)
    hidden = extended(hidden, (("atoms", 1),), -buffer_start)
    query_win = jnp.arange(Q_TILE, dtype=jnp.int32)[:, None] // QBLK * QBLK
    key_index = jnp.arange(K_SPAN, dtype=jnp.int32)[None, :]
    band = ((key_index >= query_win) & (key_index < query_win + KWIN)).astype(jnp.float32)
    channels = hidden.shape[2]
    for layer_index in range(LAYERS):
        reach = reaches[layer_index]
        kv_off = -(reach + key_halo) - buffer_start
        q_off = kv_off + key_halo
        tiles = -(-(atom_rows + 2 * reach) // Q_TILE)
        tile_start = atom_rank * atom_rows - reach - key_halo + Q_TILE * jnp.arange(
            tiles, dtype=jnp.int32
        )
        position = tile_start[:, None] + key_index
        valid_tab = ((position >= 0) & (position < total_atoms)).astype(jnp.float32)
        normed = (rms_norm(hidden) * gains[layer_index, 0]).astype(jnp.bfloat16)
        qkv_all = dense(normed, w_qkv[layer_index]).astype(jnp.bfloat16)
        span_rows = kv_off + tiles * Q_TILE + K_SPAN - Q_TILE
        qkv_all = jnp.pad(qkv_all, ((0, 0), (0, max(0, span_rows - qkv_all.shape[1])), (0, 0)))
        queries = qkv_all[:, q_off : q_off + tiles * Q_TILE, :channels]
        key_vals = qkv_all[:, kv_off:span_rows, channels:]
        attended = jnp.stack(
            [window_attend(queries[s], key_vals[s], band, valid_tab) for s in range(samples)]
        )
        hidden = jnp.pad(hidden, ((0, 0), (0, max(0, span_rows - hidden.shape[1])), (0, 0)))
        hidden = hidden[:, q_off : q_off + tiles * Q_TILE] + dense(attended, w_o[layer_index])
        buffer_start = -reach
        normed = (rms_norm(hidden) * gains[layer_index, 1]).astype(jnp.bfloat16)
        gate_up = dense(normed, w_gu[layer_index])
        inner_act = (jax.nn.silu(gate_up[..., :FF_ATOM]) * gate_up[..., FF_ATOM:]).astype(
            jnp.bfloat16
        )
        hidden = hidden + dense(inner_act, w_down[layer_index])
    hidden = hidden[:, -buffer_start : -buffer_start + atom_rows]
    update = jnp.einsum("sac,cd->sda", rms_norm(hidden), w_out, precision=lax.Precision.HIGHEST)
    predicted = (
        sigma_data * sigma_data / noise_total * noisy
        + sigma_col * sigma_data / jnp.sqrt(noise_total) * update
    )
    mse_part = (
        2.0 / 3.0 * (noise_total / (sigma_col * sigma_data) ** 2) * (predicted - true_coords[None])
    )
    block_count = atom_rows // PAIR_BLK
    atom_peers = lax.axis_size("atoms")
    count_row = jnp.zeros((1, atom_rows), jnp.float32).at[0, 0].set(
        jnp.sum(pair_count.astype(jnp.float32) * (PAIR_BLK * PAIR_BLK) - PAIR_BLK)
    )
    coord_parts = ring_parts(jnp.concatenate([predicted[0], true_coords, count_row], axis=0), "atoms")
    pair_total = jnp.sum(coord_parts[:, 6, 0])
    own_tab = jnp.concatenate(
        [predicted[0], true_coords, jnp.zeros((2, atom_rows), jnp.float32)], axis=0
    ).T
    source = (atom_rank - pair_blocks // block_count) % atom_peers
    slot_ids = jnp.arange(pair_blocks.shape[1], dtype=jnp.int32)[None, :]
    live_slot = slot_ids < pair_count[:, None]
    order = jnp.argsort(
        jnp.where(live_slot, (source != 0).astype(jnp.int32), 2) * pair_blocks.shape[1] + slot_ids,
        axis=1,
    )
    slots = jnp.take_along_axis(source * block_count + pair_blocks % block_count, order, axis=1)
    slots = slots.reshape(-1)
    local_count = jnp.sum((live_slot & (source == 0)).astype(jnp.int32), axis=1)
    no_slots = jnp.zeros_like(pair_count)
    own_coords = jnp.concatenate([predicted[0], true_coords, count_row], axis=0)[None]
    near = lddt_sums(slots, no_slots, local_count, own_tab, own_coords)
    far = lddt_sums(slots, local_count, pair_count, own_tab, coord_parts)
    pair_grad = 2.0 * (near + far)[None]
    lddt_grad = total_atoms * PAIR_BLK / pair_total * pair_grad.reshape(samples, 3, atom_rows)
    coord_grad = mse_part - lddt_grad / PAIR_BLK
    return (coord_grad, lddt_grad)


def solution(mesh):
    in_specs = (
        P("atoms", "samples"),
        P("samples", None),
        P("atoms", None),
        P("atoms"),
        P(None, "atoms"),
        P("samples", None, "atoms"),
        P("samples"),
        P(),
        P(),
        P(),
        P(),
        P(),
        P(),
        P(),
        P("atoms", None),
        P("atoms"),
    )
    out_specs = (P("samples", None, "atoms"), P("samples", None, "atoms"))
    return jax.shard_map(
        on_device, mesh=mesh, in_specs=in_specs, out_specs=out_specs, check_vma=False
    )
```

```python
import math

import jax
import jax.numpy as jnp
from jax import lax
from jax.experimental import pallas as pl
from jax.experimental.pallas import tpu as pltpu
from jax.sharding import PartitionSpec as P

HEADS = 4
FF_ATOM = 256
LAYERS = 3
QBLK = 32
KWIN = 128
HALO_TOK = 16
PAIR_BLK = 128


sigma_data = 2.0
norm_epsilon = 1e-05
thresholds = (0.5, 1.0, 2.0, 4.0)


def extended(value, sides, width):
    for axis, dim in sides:
        peers, length = (lax.axis_size(axis), value.shape[dim])
        up = [(i, (i + 1) % peers) for i in range(peers - 1)]
        down = [(j, i) for i, j in up]
        last = lax.slice_in_dim(value, length - width, length, axis=dim)
        first = lax.slice_in_dim(value, 0, width, axis=dim)
        before = lax.ppermute(last, axis, up)
        after = lax.ppermute(first, axis, down)
        value = jnp.concatenate([before, value, after], axis=dim)
    return value


def ring_parts(value, axis):
    peers = lax.axis_size(axis)
    parts = value[None]
    span = 1
    while span < peers and peers % (2 * span) == 0:
        pairs = [(i, (i + span) % peers) for i in range(peers)]
        parts = jnp.concatenate([parts, lax.ppermute(parts, axis, pairs)])
        span *= 2
    if span < peers:
        extra = [value[None]]
        for shift in range(span, peers):
            pairs = [(i, (i + shift) % peers) for i in range(peers)]
            extra.append(lax.ppermute(value, axis, pairs)[None])
        parts = jnp.concatenate([parts] + extra[1:])
    return parts

def rms_norm(tensor):
    return tensor * lax.rsqrt(jnp.mean(tensor * tensor, axis=-1, keepdims=True) + norm_epsilon)


Q_TILE = 128
K_SPAN = 256


def attend_kernel(q_ref, kv_ref, band_ref, valid_ref, out_ref):
    tile = pl.program_id(0)
    head_dim = q_ref.shape[1] // HEADS
    channels = q_ref.shape[1]
    scale = head_dim ** (-0.5)
    start = pl.multiple_of(tile * Q_TILE, Q_TILE)
    keys_vals = kv_ref[pl.ds(start, K_SPAN), :]
    live = (band_ref[...] * valid_ref[pl.ds(tile, 1), :]) > 0.0
    query_rows = q_ref[...]
    heads = []
    for head in range(HEADS):
        cols = slice(head * head_dim, (head + 1) * head_dim)
        vcols = slice(channels + head * head_dim, channels + (head + 1) * head_dim)
        scores = lax.dot_general(
            query_rows[:, cols], keys_vals[:, cols], (((1,), (1,)), ((), ())),
            preferred_element_type=jnp.float32,
        )
        scores = jnp.where(live, scores, -1e30)
        row_max = jnp.max(scores, axis=-1, keepdims=True)
        exp_scores = jnp.exp2((scores - row_max) * (scale * math.log2(math.e)))
        inverse = 1.0 / jnp.sum(exp_scores, axis=-1, keepdims=True)
        weights = (exp_scores * inverse).astype(jnp.bfloat16)
        heads.append(
            jnp.dot(weights, keys_vals[:, vcols], preferred_element_type=jnp.float32).astype(
                jnp.bfloat16
            )
        )
    out_ref[...] = jnp.concatenate(heads, axis=1)


def window_attend(queries, padded_kv, band, valid_tab):
    atoms, channels = queries.shape
    extra = atoms + K_SPAN - Q_TILE - padded_kv.shape[0]
    padded_kv = jnp.pad(padded_kv, ((0, extra), (0, 0)))
    return pl.pallas_call(
        attend_kernel,
        grid=(atoms // Q_TILE,),
        in_specs=[
            pl.BlockSpec((Q_TILE, channels), lambda t: (t, 0)),
            pl.BlockSpec(padded_kv.shape, lambda t: (0, 0)),
            pl.BlockSpec(band.shape, lambda t: (0, 0)),
            pl.BlockSpec(valid_tab.shape, lambda t: (0, 0)),
        ],
        out_specs=pl.BlockSpec((Q_TILE, channels), lambda t: (t, 0)),
        out_shape=jax.ShapeDtypeStruct((atoms, channels), jnp.bfloat16),
    )(queries, padded_kv, band, valid_tab)

ROW_CHUNK = 64


def lddt_kernel(slots_ref, count_ref, own_ref, coord_ref, out_ref, cols_ref):
    block = pl.program_id(0)
    live = count_ref[block]
    blocks = count_ref.shape[0]
    max_slots = slots_ref.shape[0] // blocks
    shape = (ROW_CHUNK, PAIR_BLK)
    lane = lax.broadcasted_iota(jnp.int32, shape, 1)
    for chunk in range(PAIR_BLK // ROW_CHUNK):
        rows = slice(chunk * ROW_CHUNK, (chunk + 1) * ROW_CHUNK)
        own = own_ref[rows, :]
        for d in range(6):
            cols_ref[d, rows, :] = jnp.broadcast_to(own[:, d : d + 1], shape)

    def row_body(row_index, carry):
        row = pl.multiple_of(row_index * ROW_CHUNK, ROW_CHUNK)

        def slot_body(slot_index, accs):
            slot = slots_ref[block * max_slots + slot_index]
            peer = slot // blocks
            start = pl.multiple_of((slot % blocks) * PAIR_BLK, PAIR_BLK)
            part = coord_ref[peer, :, pl.ds(start, PAIR_BLK)]
            part_pred = part[0:3]
            part_true = part[3:6]
            gaps = [cols_ref[d, pl.ds(row, ROW_CHUNK), :] - part_pred[d : d + 1, :] for d in range(3)]
            true_gaps = [
                cols_ref[3 + d, pl.ds(row, ROW_CHUNK), :] - part_true[d : d + 1, :] for d in range(3)
            ]
            square_pred = gaps[0] * gaps[0] + gaps[1] * gaps[1] + gaps[2] * gaps[2] + 1.0
            square_true = (
                true_gaps[0] * true_gaps[0] + true_gaps[1] * true_gaps[1] + true_gaps[2] * true_gaps[2]
            ) + 1.0
            inv_pred = lax.rsqrt(square_pred)
            gap_dist = square_pred * inv_pred - square_true * lax.rsqrt(square_true)
            square_err = gap_dist * gap_dist + 0.01
            inv_err = lax.rsqrt(square_err)
            half_err = 0.5 * (square_err * inv_err)
            curve = [jnp.tanh(0.5 * t - half_err) for t in thresholds]
            bend = curve[0] * curve[0] + curve[1] * curve[1] + curve[2] * curve[2] + curve[3] * curve[3]
            coef = ((4.0 - bend) * gap_dist) * (inv_err * inv_pred)
            return tuple(acc + coef * gap for acc, gap in zip(accs, gaps))

        zero = jnp.zeros(shape, jnp.float32)
        accs = lax.fori_loop(0, live, slot_body, (zero, zero, zero))
        sums = [-0.0625 * jnp.sum(acc, axis=1, keepdims=True) for acc in accs]
        tile = jnp.where(lane == 0, sums[0], jnp.where(lane == 1, sums[1], jnp.where(lane == 2, sums[2], 0.0)))
        out_ref[pl.ds(row, ROW_CHUNK), :] = tile
        return carry

    lax.fori_loop(0, PAIR_BLK // ROW_CHUNK, row_body, 0)


def lddt_sums(slots, counts, own_tab, coord_parts):
    blocks = counts.shape[0]
    out = pl.pallas_call(
        lddt_kernel,
        grid_spec=pltpu.PrefetchScalarGridSpec(
            num_scalar_prefetch=2,
            grid=(blocks,),
            in_specs=[
                pl.BlockSpec((PAIR_BLK, own_tab.shape[1]), lambda b, *_: (b, 0)),
                pl.BlockSpec(coord_parts.shape, lambda b, *_: (0, 0, 0)),
            ],
            out_specs=pl.BlockSpec((PAIR_BLK, PAIR_BLK), lambda b, *_: (b, 0)),
            scratch_shapes=[pltpu.VMEM((6, PAIR_BLK, PAIR_BLK), jnp.float32)],
        ),
        out_shape=jax.ShapeDtypeStruct((blocks * PAIR_BLK, PAIR_BLK), jnp.float32),
    )(slots, counts, own_tab, coord_parts)
    return out[:, :3].T

def dense(left, right):
    return jnp.einsum("sac,cf->saf", left, right, preferred_element_type=jnp.float32)


def on_device(
    token_feats,
    proj_w,
    atom_single,
    atom_token,
    true_coords,
    noise,
    sigma,
    coord_in,
    w_qkv,
    w_o,
    w_gu,
    w_down,
    gains,
    w_out,
    pair_blocks,
    pair_count,
):
    atom_rank = lax.axis_index("atoms")
    tok_rows = token_feats.shape[0]
    atom_rows = atom_single.shape[0]
    total_atoms = atom_rows * lax.axis_size("atoms")
    samples = noise.shape[0]
    feat_parts = ring_parts(token_feats, "samples")
    proj_parts = ring_parts(proj_w, "samples")
    token_sum = jnp.einsum(
        "kti,kio->to", feat_parts, proj_parts, preferred_element_type=jnp.float32
    )
    token_proj = token_sum.astype(jnp.bfloat16)
    padded_tok = extended(token_proj, (("atoms", 0),), HALO_TOK)
    first_token = atom_rank * tok_rows - HALO_TOK
    relative = atom_token - first_token
    onehot = (
        relative[:, None] == jnp.arange(tok_rows + 2 * HALO_TOK, dtype=jnp.int32)[None, :]
    ).astype(jnp.bfloat16)
    atom_base = atom_single.astype(jnp.float32) + jnp.dot(
        onehot, padded_tok, preferred_element_type=jnp.float32
    )
    sigma_col = sigma[:, None, None]
    noisy = true_coords[None] + sigma_col * noise
    noise_total = sigma_col * sigma_col + sigma_data * sigma_data
    scaled = noisy / jnp.sqrt(noise_total)
    hidden = atom_base[None] + jnp.einsum(
        "sda,dc->sac", scaled, coord_in, precision=lax.Precision.HIGHEST
    )
    key_halo = (KWIN - QBLK) // 2
    reaches = [0]
    for _ in range(LAYERS - 1):
        reaches.insert(0, -(-(reaches[0] + key_halo) // QBLK) * QBLK)
    buffer_start = -(reaches[0] + key_halo)
    hidden = extended(hidden, (("atoms", 1),), -buffer_start)
    query_win = jnp.arange(Q_TILE, dtype=jnp.int32)[:, None] // QBLK * QBLK
    key_index = jnp.arange(K_SPAN, dtype=jnp.int32)[None, :]
    band = ((key_index >= query_win) & (key_index < query_win + KWIN)).astype(jnp.float32)
    channels = hidden.shape[2]
    for layer_index in range(LAYERS):
        reach = reaches[layer_index]
        kv_off = -(reach + key_halo) - buffer_start
        q_off = kv_off + key_halo
        tiles = -(-(atom_rows + 2 * reach) // Q_TILE)
        tile_start = atom_rank * atom_rows - reach - key_halo + Q_TILE * jnp.arange(
            tiles, dtype=jnp.int32
        )
        position = tile_start[:, None] + key_index
        valid_tab = ((position >= 0) & (position < total_atoms)).astype(jnp.float32)
        normed = (rms_norm(hidden) * gains[layer_index, 0]).astype(jnp.bfloat16)
        qkv_all = dense(normed, w_qkv[layer_index]).astype(jnp.bfloat16)
        span_rows = kv_off + tiles * Q_TILE + K_SPAN - Q_TILE
        qkv_all = jnp.pad(qkv_all, ((0, 0), (0, max(0, span_rows - qkv_all.shape[1])), (0, 0)))
        queries = qkv_all[:, q_off : q_off + tiles * Q_TILE, :channels]
        key_vals = qkv_all[:, kv_off:span_rows, channels:]
        attended = jnp.stack(
            [window_attend(queries[s], key_vals[s], band, valid_tab) for s in range(samples)]
        )
        hidden = jnp.pad(hidden, ((0, 0), (0, max(0, span_rows - hidden.shape[1])), (0, 0)))
        hidden = hidden[:, q_off : q_off + tiles * Q_TILE] + dense(attended, w_o[layer_index])
        buffer_start = -reach
        normed = (rms_norm(hidden) * gains[layer_index, 1]).astype(jnp.bfloat16)
        gate_up = dense(normed, w_gu[layer_index])
        inner_act = (jax.nn.silu(gate_up[..., :FF_ATOM]) * gate_up[..., FF_ATOM:]).astype(
            jnp.bfloat16
        )
        hidden = hidden + dense(inner_act, w_down[layer_index])
    hidden = hidden[:, -buffer_start : -buffer_start + atom_rows]
    update = jnp.einsum("sac,cd->sda", rms_norm(hidden), w_out, precision=lax.Precision.HIGHEST)
    predicted = (
        sigma_data * sigma_data / noise_total * noisy
        + sigma_col * sigma_data / jnp.sqrt(noise_total) * update
    )
    mse_part = (
        2.0 / 3.0 * (noise_total / (sigma_col * sigma_data) ** 2) * (predicted - true_coords[None])
    )
    block_count = atom_rows // PAIR_BLK
    atom_peers = lax.axis_size("atoms")
    count_row = jnp.zeros((1, atom_rows), jnp.float32).at[0, 0].set(
        jnp.sum(pair_count.astype(jnp.float32) * (PAIR_BLK * PAIR_BLK) - PAIR_BLK)
    )
    coord_parts = ring_parts(jnp.concatenate([predicted[0], true_coords, count_row], axis=0), "atoms")
    pair_total = jnp.sum(coord_parts[:, 6, 0])
    own_tab = jnp.concatenate(
        [predicted[0], true_coords, jnp.zeros((2, atom_rows), jnp.float32)], axis=0
    ).T
    source = (atom_rank - pair_blocks // block_count) % atom_peers
    slots = (source * block_count + pair_blocks % block_count).reshape(-1)
    pair_grad = 2.0 * lddt_sums(slots, pair_count, own_tab, coord_parts)[None]
    lddt_grad = total_atoms * PAIR_BLK / pair_total * pair_grad.reshape(samples, 3, atom_rows)
    coord_grad = mse_part - lddt_grad / PAIR_BLK
    return (coord_grad, lddt_grad)


def solution(mesh):
    in_specs = (
        P("atoms", "samples"),
        P("samples", None),
        P("atoms", None),
        P("atoms"),
        P(None, "atoms"),
        P("samples", None, "atoms"),
        P("samples"),
        P(),
        P(),
        P(),
        P(),
        P(),
        P(),
        P(),
        P("atoms", None),
        P("atoms"),
    )
    out_specs = (P("samples", None, "atoms"), P("samples", None, "atoms"))
    return jax.shard_map(
        on_device, mesh=mesh, in_specs=in_specs, out_specs=out_specs, check_vma=False
    )
```

```python
import math

import jax
import jax.numpy as jnp
from jax import lax
from jax.experimental import pallas as pl
from jax.experimental.pallas import tpu as pltpu
from jax.sharding import PartitionSpec as P

HEADS = 4
FF_ATOM = 256
LAYERS = 3
QBLK = 32
KWIN = 128
HALO_TOK = 16
PAIR_BLK = 128


sigma_data = 2.0
norm_epsilon = 1e-05
thresholds = (0.5, 1.0, 2.0, 4.0)


def extended(value, sides, width):
    for axis, dim in sides:
        peers, length = (lax.axis_size(axis), value.shape[dim])
        up = [(i, (i + 1) % peers) for i in range(peers - 1)]
        down = [(j, i) for i, j in up]
        last = lax.slice_in_dim(value, length - width, length, axis=dim)
        first = lax.slice_in_dim(value, 0, width, axis=dim)
        before = lax.ppermute(last, axis, up)
        after = lax.ppermute(first, axis, down)
        value = jnp.concatenate([before, value, after], axis=dim)
    return value


def ring_parts(value, axis):
    peers = lax.axis_size(axis)
    parts = value[None]
    span = 1
    while span < peers and peers % (2 * span) == 0:
        pairs = [(i, (i + span) % peers) for i in range(peers)]
        parts = jnp.concatenate([parts, lax.ppermute(parts, axis, pairs)])
        span *= 2
    if span < peers:
        extra = [value[None]]
        for shift in range(span, peers):
            pairs = [(i, (i + shift) % peers) for i in range(peers)]
            extra.append(lax.ppermute(value, axis, pairs)[None])
        parts = jnp.concatenate([parts] + extra[1:])
    return parts

def rms_norm(tensor):
    return tensor * lax.rsqrt(jnp.mean(tensor * tensor, axis=-1, keepdims=True) + norm_epsilon)


Q_TILE = 128
K_SPAN = 256


def attend_kernel(q_ref, kv_ref, band_ref, valid_ref, out_ref):
    tile = pl.program_id(0)
    head_dim = q_ref.shape[1] // HEADS
    channels = q_ref.shape[1]
    scale = head_dim ** (-0.5)
    start = pl.multiple_of(tile * Q_TILE, Q_TILE)
    keys_vals = kv_ref[pl.ds(start, K_SPAN), :]
    live = (band_ref[...] * valid_ref[pl.ds(tile, 1), :]) > 0.0
    query_rows = q_ref[...]
    heads = []
    for head in range(HEADS):
        cols = slice(head * head_dim, (head + 1) * head_dim)
        vcols = slice(channels + head * head_dim, channels + (head + 1) * head_dim)
        scores = lax.dot_general(
            query_rows[:, cols], keys_vals[:, cols], (((1,), (1,)), ((), ())),
            preferred_element_type=jnp.float32,
        )
        scores = jnp.where(live, scores, -1e30)
        row_max = jnp.max(scores, axis=-1, keepdims=True)
        exp_scores = jnp.exp2((scores - row_max) * (scale * math.log2(math.e)))
        inverse = 1.0 / jnp.sum(exp_scores, axis=-1, keepdims=True)
        weights = (exp_scores * inverse).astype(jnp.bfloat16)
        heads.append(
            jnp.dot(weights, keys_vals[:, vcols], preferred_element_type=jnp.float32).astype(
                jnp.bfloat16
            )
        )
    out_ref[...] = jnp.concatenate(heads, axis=1)


def window_attend(queries, padded_kv, band, valid_tab):
    atoms, channels = queries.shape
    extra = atoms + K_SPAN - Q_TILE - padded_kv.shape[0]
    padded_kv = jnp.pad(padded_kv, ((0, extra), (0, 0)))
    return pl.pallas_call(
        attend_kernel,
        grid=(atoms // Q_TILE,),
        in_specs=[
            pl.BlockSpec((Q_TILE, channels), lambda t: (t, 0)),
            pl.BlockSpec(padded_kv.shape, lambda t: (0, 0)),
            pl.BlockSpec(band.shape, lambda t: (0, 0)),
            pl.BlockSpec(valid_tab.shape, lambda t: (0, 0)),
        ],
        out_specs=pl.BlockSpec((Q_TILE, channels), lambda t: (t, 0)),
        out_shape=jax.ShapeDtypeStruct((atoms, channels), jnp.bfloat16),
    )(queries, padded_kv, band, valid_tab)

ROW_CHUNK = 128


def lddt_kernel(slots_ref, count_ref, own_ref, coord_ref, out_ref, cols_ref):
    block = pl.program_id(0)
    live = count_ref[block]
    blocks = count_ref.shape[0]
    max_slots = slots_ref.shape[0] // blocks
    shape = (ROW_CHUNK, PAIR_BLK)
    lane = lax.broadcasted_iota(jnp.int32, shape, 1)
    for chunk in range(PAIR_BLK // ROW_CHUNK):
        rows = slice(chunk * ROW_CHUNK, (chunk + 1) * ROW_CHUNK)
        own = own_ref[rows, :]
        for d in range(6):
            cols_ref[d, rows, :] = jnp.broadcast_to(own[:, d : d + 1], shape)

    def row_body(row_index, carry):
        row = pl.multiple_of(row_index * ROW_CHUNK, ROW_CHUNK)

        def slot_body(slot_index, accs):
            slot = slots_ref[block * max_slots + slot_index]
            peer = slot // blocks
            start = pl.multiple_of((slot % blocks) * PAIR_BLK, PAIR_BLK)
            part = coord_ref[peer, :, pl.ds(start, PAIR_BLK)]
            part_pred = part[0:3]
            part_true = part[3:6]
            gaps = [cols_ref[d, pl.ds(row, ROW_CHUNK), :] - part_pred[d : d + 1, :] for d in range(3)]
            true_gaps = [
                cols_ref[3 + d, pl.ds(row, ROW_CHUNK), :] - part_true[d : d + 1, :] for d in range(3)
            ]
            square_pred = gaps[0] * gaps[0] + gaps[1] * gaps[1] + gaps[2] * gaps[2] + 1.0
            square_true = (
                true_gaps[0] * true_gaps[0] + true_gaps[1] * true_gaps[1] + true_gaps[2] * true_gaps[2]
            ) + 1.0
            inv_pred = lax.rsqrt(square_pred)
            gap_dist = square_pred * inv_pred - square_true * lax.rsqrt(square_true)
            square_err = gap_dist * gap_dist + 0.01
            inv_err = lax.rsqrt(square_err)
            half_err = 0.5 * (square_err * inv_err)
            curve = [jnp.tanh(0.5 * t - half_err) for t in thresholds]
            bend = curve[0] * curve[0] + curve[1] * curve[1] + curve[2] * curve[2] + curve[3] * curve[3]
            coef = ((4.0 - bend) * gap_dist) * (inv_err * inv_pred)
            return tuple(acc + coef * gap for acc, gap in zip(accs, gaps))

        zero = jnp.zeros(shape, jnp.float32)
        accs = lax.fori_loop(0, live, slot_body, (zero, zero, zero))
        sums = [-0.0625 * jnp.sum(acc, axis=1, keepdims=True) for acc in accs]
        tile = jnp.where(lane == 0, sums[0], jnp.where(lane == 1, sums[1], jnp.where(lane == 2, sums[2], 0.0)))
        out_ref[pl.ds(row, ROW_CHUNK), :] = tile
        return carry

    lax.fori_loop(0, PAIR_BLK // ROW_CHUNK, row_body, 0)


def lddt_sums(slots, counts, own_tab, coord_parts):
    blocks = counts.shape[0]
    out = pl.pallas_call(
        lddt_kernel,
        grid_spec=pltpu.PrefetchScalarGridSpec(
            num_scalar_prefetch=2,
            grid=(blocks,),
            in_specs=[
                pl.BlockSpec((PAIR_BLK, own_tab.shape[1]), lambda b, *_: (b, 0)),
                pl.BlockSpec(coord_parts.shape, lambda b, *_: (0, 0, 0)),
            ],
            out_specs=pl.BlockSpec((PAIR_BLK, PAIR_BLK), lambda b, *_: (b, 0)),
            scratch_shapes=[pltpu.VMEM((6, PAIR_BLK, PAIR_BLK), jnp.float32)],
        ),
        out_shape=jax.ShapeDtypeStruct((blocks * PAIR_BLK, PAIR_BLK), jnp.float32),
    )(slots, counts, own_tab, coord_parts)
    return out[:, :3].T

def dense(left, right):
    return jnp.einsum("sac,cf->saf", left, right, preferred_element_type=jnp.float32)


def on_device(
    token_feats,
    proj_w,
    atom_single,
    atom_token,
    true_coords,
    noise,
    sigma,
    coord_in,
    w_qkv,
    w_o,
    w_gu,
    w_down,
    gains,
    w_out,
    pair_blocks,
    pair_count,
):
    atom_rank = lax.axis_index("atoms")
    tok_rows = token_feats.shape[0]
    atom_rows = atom_single.shape[0]
    total_atoms = atom_rows * lax.axis_size("atoms")
    samples = noise.shape[0]
    feat_parts = ring_parts(token_feats, "samples")
    proj_parts = ring_parts(proj_w, "samples")
    token_sum = jnp.einsum(
        "kti,kio->to", feat_parts, proj_parts, preferred_element_type=jnp.float32
    )
    token_proj = token_sum.astype(jnp.bfloat16)
    padded_tok = extended(token_proj, (("atoms", 0),), HALO_TOK)
    first_token = atom_rank * tok_rows - HALO_TOK
    relative = atom_token - first_token
    onehot = (
        relative[:, None] == jnp.arange(tok_rows + 2 * HALO_TOK, dtype=jnp.int32)[None, :]
    ).astype(jnp.bfloat16)
    atom_base = atom_single.astype(jnp.float32) + jnp.dot(
        onehot, padded_tok, preferred_element_type=jnp.float32
    )
    sigma_col = sigma[:, None, None]
    noisy = true_coords[None] + sigma_col * noise
    noise_total = sigma_col * sigma_col + sigma_data * sigma_data
    scaled = noisy / jnp.sqrt(noise_total)
    hidden = atom_base[None] + jnp.einsum(
        "sda,dc->sac", scaled, coord_in, precision=lax.Precision.HIGHEST
    )
    key_halo = (KWIN - QBLK) // 2
    reaches = [0]
    for _ in range(LAYERS - 1):
        reaches.insert(0, -(-(reaches[0] + key_halo) // QBLK) * QBLK)
    buffer_start = -(reaches[0] + key_halo)
    hidden = extended(hidden, (("atoms", 1),), -buffer_start)
    query_win = jnp.arange(Q_TILE, dtype=jnp.int32)[:, None] // QBLK * QBLK
    key_index = jnp.arange(K_SPAN, dtype=jnp.int32)[None, :]
    band = ((key_index >= query_win) & (key_index < query_win + KWIN)).astype(jnp.float32)
    channels = hidden.shape[2]
    for layer_index in range(LAYERS):
        reach = reaches[layer_index]
        kv_off = -(reach + key_halo) - buffer_start
        q_off = kv_off + key_halo
        tiles = -(-(atom_rows + 2 * reach) // Q_TILE)
        tile_start = atom_rank * atom_rows - reach - key_halo + Q_TILE * jnp.arange(
            tiles, dtype=jnp.int32
        )
        position = tile_start[:, None] + key_index
        valid_tab = ((position >= 0) & (position < total_atoms)).astype(jnp.float32)
        normed = (rms_norm(hidden) * gains[layer_index, 0]).astype(jnp.bfloat16)
        qkv_all = dense(normed, w_qkv[layer_index]).astype(jnp.bfloat16)
        span_rows = kv_off + tiles * Q_TILE + K_SPAN - Q_TILE
        qkv_all = jnp.pad(qkv_all, ((0, 0), (0, max(0, span_rows - qkv_all.shape[1])), (0, 0)))
        queries = qkv_all[:, q_off : q_off + tiles * Q_TILE, :channels]
        key_vals = qkv_all[:, kv_off:span_rows, channels:]
        attended = jnp.stack(
            [window_attend(queries[s], key_vals[s], band, valid_tab) for s in range(samples)]
        )
        hidden = jnp.pad(hidden, ((0, 0), (0, max(0, span_rows - hidden.shape[1])), (0, 0)))
        hidden = hidden[:, q_off : q_off + tiles * Q_TILE] + dense(attended, w_o[layer_index])
        buffer_start = -reach
        normed = (rms_norm(hidden) * gains[layer_index, 1]).astype(jnp.bfloat16)
        gate_up = dense(normed, w_gu[layer_index])
        inner_act = (jax.nn.silu(gate_up[..., :FF_ATOM]) * gate_up[..., FF_ATOM:]).astype(
            jnp.bfloat16
        )
        hidden = hidden + dense(inner_act, w_down[layer_index])
    hidden = hidden[:, -buffer_start : -buffer_start + atom_rows]
    update = jnp.einsum("sac,cd->sda", rms_norm(hidden), w_out, precision=lax.Precision.HIGHEST)
    predicted = (
        sigma_data * sigma_data / noise_total * noisy
        + sigma_col * sigma_data / jnp.sqrt(noise_total) * update
    )
    mse_part = (
        2.0 / 3.0 * (noise_total / (sigma_col * sigma_data) ** 2) * (predicted - true_coords[None])
    )
    block_count = atom_rows // PAIR_BLK
    atom_peers = lax.axis_size("atoms")
    count_row = jnp.zeros((1, atom_rows), jnp.float32).at[0, 0].set(
        jnp.sum(pair_count.astype(jnp.float32) * (PAIR_BLK * PAIR_BLK) - PAIR_BLK)
    )
    coord_parts = ring_parts(jnp.concatenate([predicted[0], true_coords, count_row], axis=0), "atoms")
    pair_total = jnp.sum(coord_parts[:, 6, 0])
    own_tab = jnp.concatenate(
        [predicted[0], true_coords, jnp.zeros((2, atom_rows), jnp.float32)], axis=0
    ).T
    source = (atom_rank - pair_blocks // block_count) % atom_peers
    slots = (source * block_count + pair_blocks % block_count).reshape(-1)
    pair_grad = 2.0 * lddt_sums(slots, pair_count, own_tab, coord_parts)[None]
    lddt_grad = total_atoms * PAIR_BLK / pair_total * pair_grad.reshape(samples, 3, atom_rows)
    coord_grad = mse_part - lddt_grad / PAIR_BLK
    return (coord_grad, lddt_grad)


def solution(mesh):
    in_specs = (
        P("atoms", "samples"),
        P("samples", None),
        P("atoms", None),
        P("atoms"),
        P(None, "atoms"),
        P("samples", None, "atoms"),
        P("samples"),
        P(),
        P(),
        P(),
        P(),
        P(),
        P(),
        P(),
        P("atoms", None),
        P("atoms"),
    )
    out_specs = (P("samples", None, "atoms"), P("samples", None, "atoms"))
    return jax.shard_map(
        on_device, mesh=mesh, in_specs=in_specs, out_specs=out_specs, check_vma=False
    )
```

```python
import math

import jax
import jax.numpy as jnp
from jax import lax
from jax.experimental import pallas as pl
from jax.experimental.pallas import tpu as pltpu
from jax.sharding import PartitionSpec as P

HEADS = 4
FF_ATOM = 256
LAYERS = 3
QBLK = 32
KWIN = 128
HALO_TOK = 16
PAIR_BLK = 128


sigma_data = 2.0
norm_epsilon = 1e-05
thresholds = (0.5, 1.0, 2.0, 4.0)


def extended(value, sides, width):
    for axis, dim in sides:
        peers, length = (lax.axis_size(axis), value.shape[dim])
        up = [(i, (i + 1) % peers) for i in range(peers - 1)]
        down = [(j, i) for i, j in up]
        last = lax.slice_in_dim(value, length - width, length, axis=dim)
        first = lax.slice_in_dim(value, 0, width, axis=dim)
        before = lax.ppermute(last, axis, up)
        after = lax.ppermute(first, axis, down)
        value = jnp.concatenate([before, value, after], axis=dim)
    return value


def ring_parts(value, axis):
    peers = lax.axis_size(axis)
    parts = value[None]
    span = 1
    while span < peers and peers % (2 * span) == 0:
        pairs = [(i, (i + span) % peers) for i in range(peers)]
        parts = jnp.concatenate([parts, lax.ppermute(parts, axis, pairs)])
        span *= 2
    if span < peers:
        extra = [value[None]]
        for shift in range(span, peers):
            pairs = [(i, (i + shift) % peers) for i in range(peers)]
            extra.append(lax.ppermute(value, axis, pairs)[None])
        parts = jnp.concatenate([parts] + extra[1:])
    return parts

def rms_norm(tensor):
    return tensor * lax.rsqrt(jnp.mean(tensor * tensor, axis=-1, keepdims=True) + norm_epsilon)


Q_TILE = 128
K_SPAN = 256


def attend_kernel(q_ref, kv_ref, band_ref, valid_ref, out_ref):
    tile = pl.program_id(0)
    head_dim = q_ref.shape[1] // HEADS
    channels = q_ref.shape[1]
    scale = head_dim ** (-0.5)
    start = pl.multiple_of(tile * Q_TILE, Q_TILE)
    keys_vals = kv_ref[pl.ds(start, K_SPAN), :]
    live = (band_ref[...] * valid_ref[pl.ds(tile, 1), :]) > 0.0
    query_rows = q_ref[...]
    heads = []
    for head in range(HEADS):
        cols = slice(head * head_dim, (head + 1) * head_dim)
        vcols = slice(channels + head * head_dim, channels + (head + 1) * head_dim)
        scores = lax.dot_general(
            query_rows[:, cols], keys_vals[:, cols], (((1,), (1,)), ((), ())),
            preferred_element_type=jnp.float32,
        )
        scores = jnp.where(live, scores, -1e30)
        row_max = jnp.max(scores, axis=-1, keepdims=True)
        exp_scores = jnp.exp2((scores - row_max) * (scale * math.log2(math.e)))
        inverse = 1.0 / jnp.sum(exp_scores, axis=-1, keepdims=True)
        weights = (exp_scores * inverse).astype(jnp.bfloat16)
        heads.append(
            jnp.dot(weights, keys_vals[:, vcols], preferred_element_type=jnp.float32).astype(
                jnp.bfloat16
            )
        )
    out_ref[...] = jnp.concatenate(heads, axis=1)


def window_attend(queries, padded_kv, band, valid_tab):
    atoms, channels = queries.shape
    extra = atoms + K_SPAN - Q_TILE - padded_kv.shape[0]
    padded_kv = jnp.pad(padded_kv, ((0, extra), (0, 0)))
    return pl.pallas_call(
        attend_kernel,
        grid=(atoms // Q_TILE,),
        in_specs=[
            pl.BlockSpec((Q_TILE, channels), lambda t: (t, 0)),
            pl.BlockSpec(padded_kv.shape, lambda t: (0, 0)),
            pl.BlockSpec(band.shape, lambda t: (0, 0)),
            pl.BlockSpec(valid_tab.shape, lambda t: (0, 0)),
        ],
        out_specs=pl.BlockSpec((Q_TILE, channels), lambda t: (t, 0)),
        out_shape=jax.ShapeDtypeStruct((atoms, channels), jnp.bfloat16),
    )(queries, padded_kv, band, valid_tab)

ROW_CHUNK = 128
BLOCK_STEP = 2


def lddt_kernel(slots_ref, count_ref, own_ref, coord_ref, out_ref, cols_ref):
    for sub in range(BLOCK_STEP):
        lddt_block(pl.program_id(0) * BLOCK_STEP + sub, sub * PAIR_BLK, slots_ref, count_ref,
                   own_ref, coord_ref, out_ref, cols_ref)


def lddt_block(block, base, slots_ref, count_ref, own_ref, coord_ref, out_ref, cols_ref):
    live = count_ref[block]
    blocks = count_ref.shape[0]
    max_slots = slots_ref.shape[0] // blocks
    shape = (ROW_CHUNK, PAIR_BLK)
    lane = lax.broadcasted_iota(jnp.int32, shape, 1)
    for chunk in range(PAIR_BLK // ROW_CHUNK):
        rows = slice(chunk * ROW_CHUNK, (chunk + 1) * ROW_CHUNK)
        own = own_ref[base + chunk * ROW_CHUNK : base + (chunk + 1) * ROW_CHUNK, :]
        for d in range(6):
            cols_ref[d, rows, :] = jnp.broadcast_to(own[:, d : d + 1], shape)

    def row_body(row_index, carry):
        row = pl.multiple_of(row_index * ROW_CHUNK, ROW_CHUNK)

        def slot_body(slot_index, accs):
            slot = slots_ref[block * max_slots + slot_index]
            peer = slot // blocks
            start = pl.multiple_of((slot % blocks) * PAIR_BLK, PAIR_BLK)
            part = coord_ref[peer, :, pl.ds(start, PAIR_BLK)]
            part_pred = part[0:3]
            part_true = part[3:6]
            gaps = [cols_ref[d, pl.ds(row, ROW_CHUNK), :] - part_pred[d : d + 1, :] for d in range(3)]
            true_gaps = [
                cols_ref[3 + d, pl.ds(row, ROW_CHUNK), :] - part_true[d : d + 1, :] for d in range(3)
            ]
            square_pred = gaps[0] * gaps[0] + gaps[1] * gaps[1] + gaps[2] * gaps[2] + 1.0
            square_true = (
                true_gaps[0] * true_gaps[0] + true_gaps[1] * true_gaps[1] + true_gaps[2] * true_gaps[2]
            ) + 1.0
            inv_pred = lax.rsqrt(square_pred)
            gap_dist = square_pred * inv_pred - square_true * lax.rsqrt(square_true)
            square_err = gap_dist * gap_dist + 0.01
            inv_err = lax.rsqrt(square_err)
            half_err = 0.5 * (square_err * inv_err)
            curve = [jnp.tanh(0.5 * t - half_err) for t in thresholds]
            bend = curve[0] * curve[0] + curve[1] * curve[1] + curve[2] * curve[2] + curve[3] * curve[3]
            coef = ((4.0 - bend) * gap_dist) * (inv_err * inv_pred)
            return tuple(acc + coef * gap for acc, gap in zip(accs, gaps))

        zero = jnp.zeros(shape, jnp.float32)
        accs = lax.fori_loop(0, live, slot_body, (zero, zero, zero))
        sums = [-0.0625 * jnp.sum(acc, axis=1, keepdims=True) for acc in accs]
        tile = jnp.where(lane == 0, sums[0], jnp.where(lane == 1, sums[1], jnp.where(lane == 2, sums[2], 0.0)))
        out_ref[pl.ds(base + row, ROW_CHUNK), :] = tile
        return carry

    lax.fori_loop(0, PAIR_BLK // ROW_CHUNK, row_body, 0)


def lddt_sums(slots, counts, own_tab, coord_parts):
    blocks = counts.shape[0]
    out = pl.pallas_call(
        lddt_kernel,
        grid_spec=pltpu.PrefetchScalarGridSpec(
            num_scalar_prefetch=2,
            grid=(blocks // BLOCK_STEP,),
            in_specs=[
                pl.BlockSpec((BLOCK_STEP * PAIR_BLK, own_tab.shape[1]), lambda b, *_: (b, 0)),
                pl.BlockSpec(coord_parts.shape, lambda b, *_: (0, 0, 0)),
            ],
            out_specs=pl.BlockSpec((BLOCK_STEP * PAIR_BLK, PAIR_BLK), lambda b, *_: (b, 0)),
            scratch_shapes=[pltpu.VMEM((6, PAIR_BLK, PAIR_BLK), jnp.float32)],
        ),
        out_shape=jax.ShapeDtypeStruct((blocks * PAIR_BLK, PAIR_BLK), jnp.float32),
    )(slots, counts, own_tab, coord_parts)
    return out[:, :3].T

def dense(left, right):
    return jnp.einsum("sac,cf->saf", left, right, preferred_element_type=jnp.float32)


def on_device(
    token_feats,
    proj_w,
    atom_single,
    atom_token,
    true_coords,
    noise,
    sigma,
    coord_in,
    w_qkv,
    w_o,
    w_gu,
    w_down,
    gains,
    w_out,
    pair_blocks,
    pair_count,
):
    atom_rank = lax.axis_index("atoms")
    tok_rows = token_feats.shape[0]
    atom_rows = atom_single.shape[0]
    total_atoms = atom_rows * lax.axis_size("atoms")
    samples = noise.shape[0]
    feat_parts = ring_parts(token_feats, "samples")
    proj_parts = ring_parts(proj_w, "samples")
    token_sum = jnp.einsum(
        "kti,kio->to", feat_parts, proj_parts, preferred_element_type=jnp.float32
    )
    token_proj = token_sum.astype(jnp.bfloat16)
    padded_tok = extended(token_proj, (("atoms", 0),), HALO_TOK)
    first_token = atom_rank * tok_rows - HALO_TOK
    relative = atom_token - first_token
    onehot = (
        relative[:, None] == jnp.arange(tok_rows + 2 * HALO_TOK, dtype=jnp.int32)[None, :]
    ).astype(jnp.bfloat16)
    atom_base = atom_single.astype(jnp.float32) + jnp.dot(
        onehot, padded_tok, preferred_element_type=jnp.float32
    )
    sigma_col = sigma[:, None, None]
    noisy = true_coords[None] + sigma_col * noise
    noise_total = sigma_col * sigma_col + sigma_data * sigma_data
    scaled = noisy / jnp.sqrt(noise_total)
    hidden = atom_base[None] + jnp.einsum(
        "sda,dc->sac", scaled, coord_in, precision=lax.Precision.HIGHEST
    )
    key_halo = (KWIN - QBLK) // 2
    reaches = [0]
    for _ in range(LAYERS - 1):
        reaches.insert(0, -(-(reaches[0] + key_halo) // QBLK) * QBLK)
    buffer_start = -(reaches[0] + key_halo)
    hidden = extended(hidden, (("atoms", 1),), -buffer_start)
    query_win = jnp.arange(Q_TILE, dtype=jnp.int32)[:, None] // QBLK * QBLK
    key_index = jnp.arange(K_SPAN, dtype=jnp.int32)[None, :]
    band = ((key_index >= query_win) & (key_index < query_win + KWIN)).astype(jnp.float32)
    channels = hidden.shape[2]
    for layer_index in range(LAYERS):
        reach = reaches[layer_index]
        kv_off = -(reach + key_halo) - buffer_start
        q_off = kv_off + key_halo
        tiles = -(-(atom_rows + 2 * reach) // Q_TILE)
        tile_start = atom_rank * atom_rows - reach - key_halo + Q_TILE * jnp.arange(
            tiles, dtype=jnp.int32
        )
        position = tile_start[:, None] + key_index
        valid_tab = ((position >= 0) & (position < total_atoms)).astype(jnp.float32)
        normed = (rms_norm(hidden) * gains[layer_index, 0]).astype(jnp.bfloat16)
        qkv_all = dense(normed, w_qkv[layer_index]).astype(jnp.bfloat16)
        span_rows = kv_off + tiles * Q_TILE + K_SPAN - Q_TILE
        qkv_all = jnp.pad(qkv_all, ((0, 0), (0, max(0, span_rows - qkv_all.shape[1])), (0, 0)))
        queries = qkv_all[:, q_off : q_off + tiles * Q_TILE, :channels]
        key_vals = qkv_all[:, kv_off:span_rows, channels:]
        attended = jnp.stack(
            [window_attend(queries[s], key_vals[s], band, valid_tab) for s in range(samples)]
        )
        hidden = jnp.pad(hidden, ((0, 0), (0, max(0, span_rows - hidden.shape[1])), (0, 0)))
        hidden = hidden[:, q_off : q_off + tiles * Q_TILE] + dense(attended, w_o[layer_index])
        buffer_start = -reach
        normed = (rms_norm(hidden) * gains[layer_index, 1]).astype(jnp.bfloat16)
        gate_up = dense(normed, w_gu[layer_index])
        inner_act = (jax.nn.silu(gate_up[..., :FF_ATOM]) * gate_up[..., FF_ATOM:]).astype(
            jnp.bfloat16
        )
        hidden = hidden + dense(inner_act, w_down[layer_index])
    hidden = hidden[:, -buffer_start : -buffer_start + atom_rows]
    update = jnp.einsum("sac,cd->sda", rms_norm(hidden), w_out, precision=lax.Precision.HIGHEST)
    predicted = (
        sigma_data * sigma_data / noise_total * noisy
        + sigma_col * sigma_data / jnp.sqrt(noise_total) * update
    )
    mse_part = (
        2.0 / 3.0 * (noise_total / (sigma_col * sigma_data) ** 2) * (predicted - true_coords[None])
    )
    block_count = atom_rows // PAIR_BLK
    atom_peers = lax.axis_size("atoms")
    count_row = jnp.zeros((1, atom_rows), jnp.float32).at[0, 0].set(
        jnp.sum(pair_count.astype(jnp.float32) * (PAIR_BLK * PAIR_BLK) - PAIR_BLK)
    )
    coord_parts = ring_parts(jnp.concatenate([predicted[0], true_coords, count_row], axis=0), "atoms")
    pair_total = jnp.sum(coord_parts[:, 6, 0])
    own_tab = jnp.concatenate(
        [predicted[0], true_coords, jnp.zeros((2, atom_rows), jnp.float32)], axis=0
    ).T
    source = (atom_rank - pair_blocks // block_count) % atom_peers
    slots = (source * block_count + pair_blocks % block_count).reshape(-1)
    pair_grad = 2.0 * lddt_sums(slots, pair_count, own_tab, coord_parts)[None]
    lddt_grad = total_atoms * PAIR_BLK / pair_total * pair_grad.reshape(samples, 3, atom_rows)
    coord_grad = mse_part - lddt_grad / PAIR_BLK
    return (coord_grad, lddt_grad)


def solution(mesh):
    in_specs = (
        P("atoms", "samples"),
        P("samples", None),
        P("atoms", None),
        P("atoms"),
        P(None, "atoms"),
        P("samples", None, "atoms"),
        P("samples"),
        P(),
        P(),
        P(),
        P(),
        P(),
        P(),
        P(),
        P("atoms", None),
        P("atoms"),
    )
    out_specs = (P("samples", None, "atoms"), P("samples", None, "atoms"))
    return jax.shard_map(
        on_device, mesh=mesh, in_specs=in_specs, out_specs=out_specs, check_vma=False
    )
```

```python
import math

import jax
import jax.numpy as jnp
from jax import lax
from jax.experimental import pallas as pl
from jax.experimental.pallas import tpu as pltpu
from jax.sharding import PartitionSpec as P

HEADS = 4
FF_ATOM = 256
LAYERS = 3
QBLK = 32
KWIN = 128
HALO_TOK = 16
PAIR_BLK = 128


sigma_data = 2.0
norm_epsilon = 1e-05
thresholds = (0.5, 1.0, 2.0, 4.0)


def extended(value, sides, width):
    for axis, dim in sides:
        peers, length = (lax.axis_size(axis), value.shape[dim])
        up = [(i, (i + 1) % peers) for i in range(peers - 1)]
        down = [(j, i) for i, j in up]
        last = lax.slice_in_dim(value, length - width, length, axis=dim)
        first = lax.slice_in_dim(value, 0, width, axis=dim)
        before = lax.ppermute(last, axis, up)
        after = lax.ppermute(first, axis, down)
        value = jnp.concatenate([before, value, after], axis=dim)
    return value


def ring_parts(value, axis):
    peers = lax.axis_size(axis)
    parts = value[None]
    span = 1
    while span < peers and peers % (2 * span) == 0:
        pairs = [(i, (i + span) % peers) for i in range(peers)]
        parts = jnp.concatenate([parts, lax.ppermute(parts, axis, pairs)])
        span *= 2
    if span < peers:
        extra = [value[None]]
        for shift in range(span, peers):
            pairs = [(i, (i + shift) % peers) for i in range(peers)]
            extra.append(lax.ppermute(value, axis, pairs)[None])
        parts = jnp.concatenate([parts] + extra[1:])
    return parts

def rms_norm(tensor):
    return tensor * lax.rsqrt(jnp.mean(tensor * tensor, axis=-1, keepdims=True) + norm_epsilon)


Q_TILE = 128
K_SPAN = 256


def attend_kernel(q_ref, kv_ref, band_ref, valid_ref, out_ref):
    tile = pl.program_id(0)
    head_dim = q_ref.shape[1] // HEADS
    channels = q_ref.shape[1]
    scale = head_dim ** (-0.5)
    start = pl.multiple_of(tile * Q_TILE, Q_TILE)
    keys_vals = kv_ref[pl.ds(start, K_SPAN), :]
    live = (band_ref[...] * valid_ref[pl.ds(tile, 1), :]) > 0.0
    query_rows = q_ref[...]
    heads = []
    for head in range(HEADS):
        cols = slice(head * head_dim, (head + 1) * head_dim)
        vcols = slice(channels + head * head_dim, channels + (head + 1) * head_dim)
        scores = lax.dot_general(
            query_rows[:, cols], keys_vals[:, cols], (((1,), (1,)), ((), ())),
            preferred_element_type=jnp.float32,
        )
        scores = jnp.where(live, scores, -1e30)
        row_max = jnp.max(scores, axis=-1, keepdims=True)
        exp_scores = jnp.exp2((scores - row_max) * (scale * math.log2(math.e)))
        inverse = 1.0 / jnp.sum(exp_scores, axis=-1, keepdims=True)
        weights = (exp_scores * inverse).astype(jnp.bfloat16)
        heads.append(
            jnp.dot(weights, keys_vals[:, vcols], preferred_element_type=jnp.float32).astype(
                jnp.bfloat16
            )
        )
    out_ref[...] = jnp.concatenate(heads, axis=1)


def window_attend(queries, padded_kv, band, valid_tab):
    atoms, channels = queries.shape
    extra = atoms + K_SPAN - Q_TILE - padded_kv.shape[0]
    padded_kv = jnp.pad(padded_kv, ((0, extra), (0, 0)))
    return pl.pallas_call(
        attend_kernel,
        grid=(atoms // Q_TILE,),
        in_specs=[
            pl.BlockSpec((Q_TILE, channels), lambda t: (t, 0)),
            pl.BlockSpec(padded_kv.shape, lambda t: (0, 0)),
            pl.BlockSpec(band.shape, lambda t: (0, 0)),
            pl.BlockSpec(valid_tab.shape, lambda t: (0, 0)),
        ],
        out_specs=pl.BlockSpec((Q_TILE, channels), lambda t: (t, 0)),
        out_shape=jax.ShapeDtypeStruct((atoms, channels), jnp.bfloat16),
    )(queries, padded_kv, band, valid_tab)

ROW_CHUNK = 128


def lddt_kernel(slots_ref, count_ref, own_ref, coord_ref, out_ref, cols_ref, acc_ref):
    block = pl.program_id(0)
    live = count_ref[block]
    blocks = count_ref.shape[0]
    max_slots = slots_ref.shape[0] // blocks
    shape = (ROW_CHUNK, PAIR_BLK)
    lane = lax.broadcasted_iota(jnp.int32, shape, 1)
    for chunk in range(PAIR_BLK // ROW_CHUNK):
        rows = slice(chunk * ROW_CHUNK, (chunk + 1) * ROW_CHUNK)
        own = own_ref[rows, :]
        for d in range(6):
            cols_ref[d, rows, :] = jnp.broadcast_to(own[:, d : d + 1], shape)

    def row_body(row_index, carry):
        row = pl.multiple_of(row_index * ROW_CHUNK, ROW_CHUNK)

        def slot_body(slot_index, accs):
            slot = slots_ref[block * max_slots + slot_index]
            peer = slot // blocks
            start = pl.multiple_of((slot % blocks) * PAIR_BLK, PAIR_BLK)
            part = coord_ref[peer, :, pl.ds(start, PAIR_BLK)]
            part_pred = part[0:3]
            part_true = part[3:6]
            gaps = [cols_ref[d, pl.ds(row, ROW_CHUNK), :] - part_pred[d : d + 1, :] for d in range(3)]
            true_gaps = [
                cols_ref[3 + d, pl.ds(row, ROW_CHUNK), :] - part_true[d : d + 1, :] for d in range(3)
            ]
            square_pred = gaps[0] * gaps[0] + gaps[1] * gaps[1] + gaps[2] * gaps[2] + 1.0
            square_true = (
                true_gaps[0] * true_gaps[0] + true_gaps[1] * true_gaps[1] + true_gaps[2] * true_gaps[2]
            ) + 1.0
            inv_pred = lax.rsqrt(square_pred)
            gap_dist = square_pred * inv_pred - square_true * lax.rsqrt(square_true)
            square_err = gap_dist * gap_dist + 0.01
            inv_err = lax.rsqrt(square_err)
            half_err = 0.5 * (square_err * inv_err)
            curve = [jnp.tanh(0.5 * t - half_err) for t in thresholds]
            bend = curve[0] * curve[0] + curve[1] * curve[1] + curve[2] * curve[2] + curve[3] * curve[3]
            coef = ((4.0 - bend) * gap_dist) * (inv_err * inv_pred)
            for d in range(3):
                acc_ref[d, pl.ds(row, ROW_CHUNK), :] += coef * gaps[d]
            return accs

        for d in range(3):
            acc_ref[d, pl.ds(row, ROW_CHUNK), :] = jnp.zeros(shape, jnp.float32)
        lax.fori_loop(0, live, slot_body, 0)
        sums = [
            -0.0625 * jnp.sum(acc_ref[d, pl.ds(row, ROW_CHUNK), :], axis=1, keepdims=True)
            for d in range(3)
        ]
        tile = jnp.where(lane == 0, sums[0], jnp.where(lane == 1, sums[1], jnp.where(lane == 2, sums[2], 0.0)))
        out_ref[pl.ds(row, ROW_CHUNK), :] = tile
        return carry

    lax.fori_loop(0, PAIR_BLK // ROW_CHUNK, row_body, 0)


def lddt_sums(slots, counts, own_tab, coord_parts):
    blocks = counts.shape[0]
    out = pl.pallas_call(
        lddt_kernel,
        grid_spec=pltpu.PrefetchScalarGridSpec(
            num_scalar_prefetch=2,
            grid=(blocks,),
            in_specs=[
                pl.BlockSpec((PAIR_BLK, own_tab.shape[1]), lambda b, *_: (b, 0)),
                pl.BlockSpec(coord_parts.shape, lambda b, *_: (0, 0, 0)),
            ],
            out_specs=pl.BlockSpec((PAIR_BLK, PAIR_BLK), lambda b, *_: (b, 0)),
            scratch_shapes=[
                pltpu.VMEM((6, PAIR_BLK, PAIR_BLK), jnp.float32),
                pltpu.VMEM((3, PAIR_BLK, PAIR_BLK), jnp.float32),
            ],
        ),
        out_shape=jax.ShapeDtypeStruct((blocks * PAIR_BLK, PAIR_BLK), jnp.float32),
    )(slots, counts, own_tab, coord_parts)
    return out[:, :3].T

def dense(left, right):
    return jnp.einsum("sac,cf->saf", left, right, preferred_element_type=jnp.float32)


def on_device(
    token_feats,
    proj_w,
    atom_single,
    atom_token,
    true_coords,
    noise,
    sigma,
    coord_in,
    w_qkv,
    w_o,
    w_gu,
    w_down,
    gains,
    w_out,
    pair_blocks,
    pair_count,
):
    atom_rank = lax.axis_index("atoms")
    tok_rows = token_feats.shape[0]
    atom_rows = atom_single.shape[0]
    total_atoms = atom_rows * lax.axis_size("atoms")
    samples = noise.shape[0]
    feat_parts = ring_parts(token_feats, "samples")
    proj_parts = ring_parts(proj_w, "samples")
    token_sum = jnp.einsum(
        "kti,kio->to", feat_parts, proj_parts, preferred_element_type=jnp.float32
    )
    token_proj = token_sum.astype(jnp.bfloat16)
    padded_tok = extended(token_proj, (("atoms", 0),), HALO_TOK)
    first_token = atom_rank * tok_rows - HALO_TOK
    relative = atom_token - first_token
    onehot = (
        relative[:, None] == jnp.arange(tok_rows + 2 * HALO_TOK, dtype=jnp.int32)[None, :]
    ).astype(jnp.bfloat16)
    atom_base = atom_single.astype(jnp.float32) + jnp.dot(
        onehot, padded_tok, preferred_element_type=jnp.float32
    )
    sigma_col = sigma[:, None, None]
    noisy = true_coords[None] + sigma_col * noise
    noise_total = sigma_col * sigma_col + sigma_data * sigma_data
    scaled = noisy / jnp.sqrt(noise_total)
    hidden = atom_base[None] + jnp.einsum(
        "sda,dc->sac", scaled, coord_in, precision=lax.Precision.HIGHEST
    )
    key_halo = (KWIN - QBLK) // 2
    reaches = [0]
    for _ in range(LAYERS - 1):
        reaches.insert(0, -(-(reaches[0] + key_halo) // QBLK) * QBLK)
    buffer_start = -(reaches[0] + key_halo)
    hidden = extended(hidden, (("atoms", 1),), -buffer_start)
    query_win = jnp.arange(Q_TILE, dtype=jnp.int32)[:, None] // QBLK * QBLK
    key_index = jnp.arange(K_SPAN, dtype=jnp.int32)[None, :]
    band = ((key_index >= query_win) & (key_index < query_win + KWIN)).astype(jnp.float32)
    channels = hidden.shape[2]
    for layer_index in range(LAYERS):
        reach = reaches[layer_index]
        kv_off = -(reach + key_halo) - buffer_start
        q_off = kv_off + key_halo
        tiles = -(-(atom_rows + 2 * reach) // Q_TILE)
        tile_start = atom_rank * atom_rows - reach - key_halo + Q_TILE * jnp.arange(
            tiles, dtype=jnp.int32
        )
        position = tile_start[:, None] + key_index
        valid_tab = ((position >= 0) & (position < total_atoms)).astype(jnp.float32)
        normed = (rms_norm(hidden) * gains[layer_index, 0]).astype(jnp.bfloat16)
        qkv_all = dense(normed, w_qkv[layer_index]).astype(jnp.bfloat16)
        span_rows = kv_off + tiles * Q_TILE + K_SPAN - Q_TILE
        qkv_all = jnp.pad(qkv_all, ((0, 0), (0, max(0, span_rows - qkv_all.shape[1])), (0, 0)))
        queries = qkv_all[:, q_off : q_off + tiles * Q_TILE, :channels]
        key_vals = qkv_all[:, kv_off:span_rows, channels:]
        attended = jnp.stack(
            [window_attend(queries[s], key_vals[s], band, valid_tab) for s in range(samples)]
        )
        hidden = jnp.pad(hidden, ((0, 0), (0, max(0, span_rows - hidden.shape[1])), (0, 0)))
        hidden = hidden[:, q_off : q_off + tiles * Q_TILE] + dense(attended, w_o[layer_index])
        buffer_start = -reach
        normed = (rms_norm(hidden) * gains[layer_index, 1]).astype(jnp.bfloat16)
        gate_up = dense(normed, w_gu[layer_index])
        inner_act = (jax.nn.silu(gate_up[..., :FF_ATOM]) * gate_up[..., FF_ATOM:]).astype(
            jnp.bfloat16
        )
        hidden = hidden + dense(inner_act, w_down[layer_index])
    hidden = hidden[:, -buffer_start : -buffer_start + atom_rows]
    update = jnp.einsum("sac,cd->sda", rms_norm(hidden), w_out, precision=lax.Precision.HIGHEST)
    predicted = (
        sigma_data * sigma_data / noise_total * noisy
        + sigma_col * sigma_data / jnp.sqrt(noise_total) * update
    )
    mse_part = (
        2.0 / 3.0 * (noise_total / (sigma_col * sigma_data) ** 2) * (predicted - true_coords[None])
    )
    block_count = atom_rows // PAIR_BLK
    atom_peers = lax.axis_size("atoms")
    count_row = jnp.zeros((1, atom_rows), jnp.float32).at[0, 0].set(
        jnp.sum(pair_count.astype(jnp.float32) * (PAIR_BLK * PAIR_BLK) - PAIR_BLK)
    )
    coord_parts = ring_parts(jnp.concatenate([predicted[0], true_coords, count_row], axis=0), "atoms")
    pair_total = jnp.sum(coord_parts[:, 6, 0])
    own_tab = jnp.concatenate(
        [predicted[0], true_coords, jnp.zeros((2, atom_rows), jnp.float32)], axis=0
    ).T
    source = (atom_rank - pair_blocks // block_count) % atom_peers
    slots = (source * block_count + pair_blocks % block_count).reshape(-1)
    pair_grad = 2.0 * lddt_sums(slots, pair_count, own_tab, coord_parts)[None]
    lddt_grad = total_atoms * PAIR_BLK / pair_total * pair_grad.reshape(samples, 3, atom_rows)
    coord_grad = mse_part - lddt_grad / PAIR_BLK
    return (coord_grad, lddt_grad)


def solution(mesh):
    in_specs = (
        P("atoms", "samples"),
        P("samples", None),
        P("atoms", None),
        P("atoms"),
        P(None, "atoms"),
        P("samples", None, "atoms"),
        P("samples"),
        P(),
        P(),
        P(),
        P(),
        P(),
        P(),
        P(),
        P("atoms", None),
        P("atoms"),
    )
    out_specs = (P("samples", None, "atoms"), P("samples", None, "atoms"))
    return jax.shard_map(
        on_device, mesh=mesh, in_specs=in_specs, out_specs=out_specs, check_vma=False
    )
```

```python
import math

import jax
import jax.numpy as jnp
from jax import lax
from jax.experimental import pallas as pl
from jax.experimental.pallas import tpu as pltpu
from jax.sharding import PartitionSpec as P

HEADS = 4
FF_ATOM = 256
LAYERS = 3
QBLK = 32
KWIN = 128
HALO_TOK = 16
PAIR_BLK = 128


sigma_data = 2.0
norm_epsilon = 1e-05
thresholds = (0.5, 1.0, 2.0, 4.0)


def extended(value, sides, width):
    for axis, dim in sides:
        peers, length = (lax.axis_size(axis), value.shape[dim])
        up = [(i, (i + 1) % peers) for i in range(peers - 1)]
        down = [(j, i) for i, j in up]
        last = lax.slice_in_dim(value, length - width, length, axis=dim)
        first = lax.slice_in_dim(value, 0, width, axis=dim)
        before = lax.ppermute(last, axis, up)
        after = lax.ppermute(first, axis, down)
        value = jnp.concatenate([before, value, after], axis=dim)
    return value


def ring_parts(value, axis, direct=False):
    peers = lax.axis_size(axis)
    parts = value[None]
    span = 1
    while not direct and span < peers and peers % (2 * span) == 0:
        pairs = [(i, (i + span) % peers) for i in range(peers)]
        parts = jnp.concatenate([parts, lax.ppermute(parts, axis, pairs)])
        span *= 2
    if span < peers:
        extra = [value[None]]
        for shift in range(span, peers):
            pairs = [(i, (i + shift) % peers) for i in range(peers)]
            extra.append(lax.ppermute(value, axis, pairs)[None])
        parts = jnp.concatenate([parts] + extra[1:])
    return parts

def rms_norm(tensor):
    return tensor * lax.rsqrt(jnp.mean(tensor * tensor, axis=-1, keepdims=True) + norm_epsilon)


Q_TILE = 128
K_SPAN = 256


def attend_kernel(q_ref, kv_ref, band_ref, valid_ref, out_ref):
    tile = pl.program_id(0)
    head_dim = q_ref.shape[1] // HEADS
    channels = q_ref.shape[1]
    scale = head_dim ** (-0.5)
    start = pl.multiple_of(tile * Q_TILE, Q_TILE)
    keys_vals = kv_ref[pl.ds(start, K_SPAN), :]
    live = (band_ref[...] * valid_ref[pl.ds(tile, 1), :]) > 0.0
    query_rows = q_ref[...]
    heads = []
    for head in range(HEADS):
        cols = slice(head * head_dim, (head + 1) * head_dim)
        vcols = slice(channels + head * head_dim, channels + (head + 1) * head_dim)
        scores = lax.dot_general(
            query_rows[:, cols], keys_vals[:, cols], (((1,), (1,)), ((), ())),
            preferred_element_type=jnp.float32,
        )
        scores = jnp.where(live, scores, -1e30)
        row_max = jnp.max(scores, axis=-1, keepdims=True)
        exp_scores = jnp.exp2((scores - row_max) * (scale * math.log2(math.e)))
        inverse = 1.0 / jnp.sum(exp_scores, axis=-1, keepdims=True)
        weights = (exp_scores * inverse).astype(jnp.bfloat16)
        heads.append(
            jnp.dot(weights, keys_vals[:, vcols], preferred_element_type=jnp.float32).astype(
                jnp.bfloat16
            )
        )
    out_ref[...] = jnp.concatenate(heads, axis=1)


def window_attend(queries, padded_kv, band, valid_tab):
    atoms, channels = queries.shape
    extra = atoms + K_SPAN - Q_TILE - padded_kv.shape[0]
    padded_kv = jnp.pad(padded_kv, ((0, extra), (0, 0)))
    return pl.pallas_call(
        attend_kernel,
        grid=(atoms // Q_TILE,),
        in_specs=[
            pl.BlockSpec((Q_TILE, channels), lambda t: (t, 0)),
            pl.BlockSpec(padded_kv.shape, lambda t: (0, 0)),
            pl.BlockSpec(band.shape, lambda t: (0, 0)),
            pl.BlockSpec(valid_tab.shape, lambda t: (0, 0)),
        ],
        out_specs=pl.BlockSpec((Q_TILE, channels), lambda t: (t, 0)),
        out_shape=jax.ShapeDtypeStruct((atoms, channels), jnp.bfloat16),
    )(queries, padded_kv, band, valid_tab)

ROW_CHUNK = 128


def lddt_kernel(slots_ref, count_ref, own_ref, coord_ref, out_ref, cols_ref, acc_ref):
    block = pl.program_id(0)
    live = count_ref[block]
    blocks = count_ref.shape[0]
    max_slots = slots_ref.shape[0] // blocks
    shape = (ROW_CHUNK, PAIR_BLK)
    lane = lax.broadcasted_iota(jnp.int32, shape, 1)
    for chunk in range(PAIR_BLK // ROW_CHUNK):
        rows = slice(chunk * ROW_CHUNK, (chunk + 1) * ROW_CHUNK)
        own = own_ref[rows, :]
        for d in range(6):
            cols_ref[d, rows, :] = jnp.broadcast_to(own[:, d : d + 1], shape)

    def row_body(row_index, carry):
        row = pl.multiple_of(row_index * ROW_CHUNK, ROW_CHUNK)

        def slot_body(slot_index, accs):
            slot = slots_ref[block * max_slots + slot_index]
            peer = slot // blocks
            start = pl.multiple_of((slot % blocks) * PAIR_BLK, PAIR_BLK)
            part = coord_ref[peer, :, pl.ds(start, PAIR_BLK)]
            part_pred = part[0:3]
            part_true = part[3:6]
            gaps = [cols_ref[d, pl.ds(row, ROW_CHUNK), :] - part_pred[d : d + 1, :] for d in range(3)]
            true_gaps = [
                cols_ref[3 + d, pl.ds(row, ROW_CHUNK), :] - part_true[d : d + 1, :] for d in range(3)
            ]
            square_pred = gaps[0] * gaps[0] + gaps[1] * gaps[1] + gaps[2] * gaps[2] + 1.0
            square_true = (
                true_gaps[0] * true_gaps[0] + true_gaps[1] * true_gaps[1] + true_gaps[2] * true_gaps[2]
            ) + 1.0
            inv_pred = lax.rsqrt(square_pred)
            gap_dist = square_pred * inv_pred - square_true * lax.rsqrt(square_true)
            square_err = gap_dist * gap_dist + 0.01
            inv_err = lax.rsqrt(square_err)
            half_err = 0.5 * (square_err * inv_err)
            curve = [jnp.tanh(0.5 * t - half_err) for t in thresholds]
            bend = curve[0] * curve[0] + curve[1] * curve[1] + curve[2] * curve[2] + curve[3] * curve[3]
            coef = ((4.0 - bend) * gap_dist) * (inv_err * inv_pred)
            for d in range(3):
                acc_ref[d, pl.ds(row, ROW_CHUNK), :] += coef * gaps[d]
            return accs

        for d in range(3):
            acc_ref[d, pl.ds(row, ROW_CHUNK), :] = jnp.zeros(shape, jnp.float32)
        lax.fori_loop(0, live, slot_body, 0)
        sums = [
            -0.0625 * jnp.sum(acc_ref[d, pl.ds(row, ROW_CHUNK), :], axis=1, keepdims=True)
            for d in range(3)
        ]
        tile = jnp.where(lane == 0, sums[0], jnp.where(lane == 1, sums[1], jnp.where(lane == 2, sums[2], 0.0)))
        out_ref[pl.ds(row, ROW_CHUNK), :] = tile
        return carry

    lax.fori_loop(0, PAIR_BLK // ROW_CHUNK, row_body, 0)


def lddt_sums(slots, counts, own_tab, coord_parts):
    blocks = counts.shape[0]
    out = pl.pallas_call(
        lddt_kernel,
        grid_spec=pltpu.PrefetchScalarGridSpec(
            num_scalar_prefetch=2,
            grid=(blocks,),
            in_specs=[
                pl.BlockSpec((PAIR_BLK, own_tab.shape[1]), lambda b, *_: (b, 0)),
                pl.BlockSpec(coord_parts.shape, lambda b, *_: (0, 0, 0)),
            ],
            out_specs=pl.BlockSpec((PAIR_BLK, PAIR_BLK), lambda b, *_: (b, 0)),
            scratch_shapes=[
                pltpu.VMEM((6, PAIR_BLK, PAIR_BLK), jnp.float32),
                pltpu.VMEM((3, PAIR_BLK, PAIR_BLK), jnp.float32),
            ],
        ),
        out_shape=jax.ShapeDtypeStruct((blocks * PAIR_BLK, PAIR_BLK), jnp.float32),
    )(slots, counts, own_tab, coord_parts)
    return out[:, :3].T

def dense(left, right):
    return jnp.einsum("sac,cf->saf", left, right, preferred_element_type=jnp.float32)


def on_device(
    token_feats,
    proj_w,
    atom_single,
    atom_token,
    true_coords,
    noise,
    sigma,
    coord_in,
    w_qkv,
    w_o,
    w_gu,
    w_down,
    gains,
    w_out,
    pair_blocks,
    pair_count,
):
    atom_rank = lax.axis_index("atoms")
    tok_rows = token_feats.shape[0]
    atom_rows = atom_single.shape[0]
    total_atoms = atom_rows * lax.axis_size("atoms")
    samples = noise.shape[0]
    feat_parts = ring_parts(token_feats, "samples")
    proj_parts = ring_parts(proj_w, "samples")
    token_sum = jnp.einsum(
        "kti,kio->to", feat_parts, proj_parts, preferred_element_type=jnp.float32
    )
    token_proj = token_sum.astype(jnp.bfloat16)
    padded_tok = extended(token_proj, (("atoms", 0),), HALO_TOK)
    first_token = atom_rank * tok_rows - HALO_TOK
    relative = atom_token - first_token
    onehot = (
        relative[:, None] == jnp.arange(tok_rows + 2 * HALO_TOK, dtype=jnp.int32)[None, :]
    ).astype(jnp.bfloat16)
    atom_base = atom_single.astype(jnp.float32) + jnp.dot(
        onehot, padded_tok, preferred_element_type=jnp.float32
    )
    sigma_col = sigma[:, None, None]
    noisy = true_coords[None] + sigma_col * noise
    noise_total = sigma_col * sigma_col + sigma_data * sigma_data
    scaled = noisy / jnp.sqrt(noise_total)
    hidden = atom_base[None] + jnp.einsum(
        "sda,dc->sac", scaled, coord_in, precision=lax.Precision.HIGHEST
    )
    key_halo = (KWIN - QBLK) // 2
    reaches = [0]
    for _ in range(LAYERS - 1):
        reaches.insert(0, -(-(reaches[0] + key_halo) // QBLK) * QBLK)
    buffer_start = -(reaches[0] + key_halo)
    hidden = extended(hidden, (("atoms", 1),), -buffer_start)
    query_win = jnp.arange(Q_TILE, dtype=jnp.int32)[:, None] // QBLK * QBLK
    key_index = jnp.arange(K_SPAN, dtype=jnp.int32)[None, :]
    band = ((key_index >= query_win) & (key_index < query_win + KWIN)).astype(jnp.float32)
    channels = hidden.shape[2]
    for layer_index in range(LAYERS):
        reach = reaches[layer_index]
        kv_off = -(reach + key_halo) - buffer_start
        q_off = kv_off + key_halo
        tiles = -(-(atom_rows + 2 * reach) // Q_TILE)
        tile_start = atom_rank * atom_rows - reach - key_halo + Q_TILE * jnp.arange(
            tiles, dtype=jnp.int32
        )
        position = tile_start[:, None] + key_index
        valid_tab = ((position >= 0) & (position < total_atoms)).astype(jnp.float32)
        normed = (rms_norm(hidden) * gains[layer_index, 0]).astype(jnp.bfloat16)
        qkv_all = dense(normed, w_qkv[layer_index]).astype(jnp.bfloat16)
        span_rows = kv_off + tiles * Q_TILE + K_SPAN - Q_TILE
        qkv_all = jnp.pad(qkv_all, ((0, 0), (0, max(0, span_rows - qkv_all.shape[1])), (0, 0)))
        queries = qkv_all[:, q_off : q_off + tiles * Q_TILE, :channels]
        key_vals = qkv_all[:, kv_off:span_rows, channels:]
        attended = jnp.stack(
            [window_attend(queries[s], key_vals[s], band, valid_tab) for s in range(samples)]
        )
        hidden = jnp.pad(hidden, ((0, 0), (0, max(0, span_rows - hidden.shape[1])), (0, 0)))
        hidden = hidden[:, q_off : q_off + tiles * Q_TILE] + dense(attended, w_o[layer_index])
        buffer_start = -reach
        normed = (rms_norm(hidden) * gains[layer_index, 1]).astype(jnp.bfloat16)
        gate_up = dense(normed, w_gu[layer_index])
        inner_act = (jax.nn.silu(gate_up[..., :FF_ATOM]) * gate_up[..., FF_ATOM:]).astype(
            jnp.bfloat16
        )
        hidden = hidden + dense(inner_act, w_down[layer_index])
    hidden = hidden[:, -buffer_start : -buffer_start + atom_rows]
    update = jnp.einsum("sac,cd->sda", rms_norm(hidden), w_out, precision=lax.Precision.HIGHEST)
    predicted = (
        sigma_data * sigma_data / noise_total * noisy
        + sigma_col * sigma_data / jnp.sqrt(noise_total) * update
    )
    mse_part = (
        2.0 / 3.0 * (noise_total / (sigma_col * sigma_data) ** 2) * (predicted - true_coords[None])
    )
    block_count = atom_rows // PAIR_BLK
    atom_peers = lax.axis_size("atoms")
    count_row = jnp.zeros((1, atom_rows), jnp.float32).at[0, 0].set(
        jnp.sum(pair_count.astype(jnp.float32) * (PAIR_BLK * PAIR_BLK) - PAIR_BLK)
    )
    coord_parts = ring_parts(
        jnp.concatenate([predicted[0], true_coords, count_row], axis=0), "atoms", direct=atom_peers <= 8
    )
    pair_total = jnp.sum(coord_parts[:, 6, 0])
    own_tab = jnp.concatenate(
        [predicted[0], true_coords, jnp.zeros((2, atom_rows), jnp.float32)], axis=0
    ).T
    source = (atom_rank - pair_blocks // block_count) % atom_peers
    slots = (source * block_count + pair_blocks % block_count).reshape(-1)
    pair_grad = 2.0 * lddt_sums(slots, pair_count, own_tab, coord_parts)[None]
    lddt_grad = total_atoms * PAIR_BLK / pair_total * pair_grad.reshape(samples, 3, atom_rows)
    coord_grad = mse_part - lddt_grad / PAIR_BLK
    return (coord_grad, lddt_grad)


def solution(mesh):
    in_specs = (
        P("atoms", "samples"),
        P("samples", None),
        P("atoms", None),
        P("atoms"),
        P(None, "atoms"),
        P("samples", None, "atoms"),
        P("samples"),
        P(),
        P(),
        P(),
        P(),
        P(),
        P(),
        P(),
        P("atoms", None),
        P("atoms"),
    )
    out_specs = (P("samples", None, "atoms"), P("samples", None, "atoms"))
    return jax.shard_map(
        on_device, mesh=mesh, in_specs=in_specs, out_specs=out_specs, check_vma=False
    )
```

```python
import math

import jax
import jax.numpy as jnp
from jax import lax
from jax.experimental import pallas as pl
from jax.experimental.pallas import tpu as pltpu
from jax.sharding import PartitionSpec as P

HEADS = 4
FF_ATOM = 256
LAYERS = 3
QBLK = 32
KWIN = 128
HALO_TOK = 16
PAIR_BLK = 128


sigma_data = 2.0
norm_epsilon = 1e-05
thresholds = (0.5, 1.0, 2.0, 4.0)


def extended(value, sides, width):
    for axis, dim in sides:
        peers, length = (lax.axis_size(axis), value.shape[dim])
        up = [(i, (i + 1) % peers) for i in range(peers - 1)]
        down = [(j, i) for i, j in up]
        last = lax.slice_in_dim(value, length - width, length, axis=dim)
        first = lax.slice_in_dim(value, 0, width, axis=dim)
        before = lax.ppermute(last, axis, up)
        after = lax.ppermute(first, axis, down)
        value = jnp.concatenate([before, value, after], axis=dim)
    return value


def ring_parts(value, axis, direct=False):
    peers = lax.axis_size(axis)
    parts = value[None]
    span = 1
    while not direct and span < peers and peers % (2 * span) == 0:
        pairs = [(i, (i + span) % peers) for i in range(peers)]
        parts = jnp.concatenate([parts, lax.ppermute(parts, axis, pairs)])
        span *= 2
    if span < peers:
        extra = [value[None]]
        for shift in range(span, peers):
            pairs = [(i, (i + shift) % peers) for i in range(peers)]
            extra.append(lax.ppermute(value, axis, pairs)[None])
        parts = jnp.concatenate([parts] + extra[1:])
    return parts

def rms_norm(tensor):
    return tensor * lax.rsqrt(jnp.mean(tensor * tensor, axis=-1, keepdims=True) + norm_epsilon)


Q_TILE = 128
K_SPAN = 256


def attend_kernel(q_ref, kv_ref, band_ref, valid_ref, out_ref):
    tile = pl.program_id(0)
    head_dim = q_ref.shape[1] // HEADS
    channels = q_ref.shape[1]
    scale = head_dim ** (-0.5)
    start = pl.multiple_of(tile * Q_TILE, Q_TILE)
    keys_vals = kv_ref[pl.ds(start, K_SPAN), :]
    live = (band_ref[...] * valid_ref[pl.ds(tile, 1), :]) > 0.0
    query_rows = q_ref[...]
    heads = []
    for head in range(HEADS):
        cols = slice(head * head_dim, (head + 1) * head_dim)
        vcols = slice(channels + head * head_dim, channels + (head + 1) * head_dim)
        scores = lax.dot_general(
            query_rows[:, cols], keys_vals[:, cols], (((1,), (1,)), ((), ())),
            preferred_element_type=jnp.float32,
        )
        scores = jnp.where(live, scores, -1e30)
        row_max = jnp.max(scores, axis=-1, keepdims=True)
        exp_scores = jnp.exp2((scores - row_max) * (scale * math.log2(math.e)))
        inverse = 1.0 / jnp.sum(exp_scores, axis=-1, keepdims=True)
        weights = (exp_scores * inverse).astype(jnp.bfloat16)
        heads.append(
            jnp.dot(weights, keys_vals[:, vcols], preferred_element_type=jnp.float32).astype(
                jnp.bfloat16
            )
        )
    out_ref[...] = jnp.concatenate(heads, axis=1)


def window_attend(queries, padded_kv, band, valid_tab):
    atoms, channels = queries.shape
    extra = atoms + K_SPAN - Q_TILE - padded_kv.shape[0]
    padded_kv = jnp.pad(padded_kv, ((0, extra), (0, 0)))
    return pl.pallas_call(
        attend_kernel,
        grid=(atoms // Q_TILE,),
        in_specs=[
            pl.BlockSpec((Q_TILE, channels), lambda t: (t, 0)),
            pl.BlockSpec(padded_kv.shape, lambda t: (0, 0)),
            pl.BlockSpec(band.shape, lambda t: (0, 0)),
            pl.BlockSpec(valid_tab.shape, lambda t: (0, 0)),
        ],
        out_specs=pl.BlockSpec((Q_TILE, channels), lambda t: (t, 0)),
        out_shape=jax.ShapeDtypeStruct((atoms, channels), jnp.bfloat16),
    )(queries, padded_kv, band, valid_tab)

ROW_CHUNK = 128


def lddt_kernel(slots_ref, count_ref, own_ref, coord_ref, out_ref, cols_ref, acc_ref):
    block = pl.program_id(0)
    live = count_ref[block]
    blocks = count_ref.shape[0]
    max_slots = slots_ref.shape[0] // blocks
    shape = (ROW_CHUNK, PAIR_BLK)
    lane = lax.broadcasted_iota(jnp.int32, shape, 1)
    for chunk in range(PAIR_BLK // ROW_CHUNK):
        rows = slice(chunk * ROW_CHUNK, (chunk + 1) * ROW_CHUNK)
        own = own_ref[rows, :]
        for d in range(6):
            cols_ref[d, rows, :] = jnp.broadcast_to(own[:, d : d + 1], shape)

    def row_body(row_index, carry):
        row = pl.multiple_of(row_index * ROW_CHUNK, ROW_CHUNK)

        def slot_body(slot_index, accs):
            slot = slots_ref[block * max_slots + slot_index]
            peer = slot // blocks
            start = pl.multiple_of((slot % blocks) * PAIR_BLK, PAIR_BLK)
            part = coord_ref[peer, :, pl.ds(start, PAIR_BLK)]
            part_pred = part[0:3]
            part_true = part[3:6]
            gaps = [cols_ref[d, pl.ds(row, ROW_CHUNK), :] - part_pred[d : d + 1, :] for d in range(3)]
            true_gaps = [
                cols_ref[3 + d, pl.ds(row, ROW_CHUNK), :] - part_true[d : d + 1, :] for d in range(3)
            ]
            square_pred = gaps[0] * gaps[0] + gaps[1] * gaps[1] + gaps[2] * gaps[2] + 1.0
            square_true = (
                true_gaps[0] * true_gaps[0] + true_gaps[1] * true_gaps[1] + true_gaps[2] * true_gaps[2]
            ) + 1.0
            inv_pred = lax.rsqrt(square_pred)
            gap_dist = square_pred * inv_pred - square_true * lax.rsqrt(square_true)
            square_err = gap_dist * gap_dist + 0.01
            inv_err = lax.rsqrt(square_err)
            half_err = 0.5 * (square_err * inv_err)
            curve = [jnp.tanh(0.5 * t - half_err) for t in thresholds]
            bend = curve[0] * curve[0] + curve[1] * curve[1] + curve[2] * curve[2] + curve[3] * curve[3]
            coef = ((4.0 - bend) * gap_dist) * (inv_err * inv_pred)
            for d in range(3):
                acc_ref[d, pl.ds(row, ROW_CHUNK), :] += coef * gaps[d]
            return accs

        for d in range(3):
            acc_ref[d, pl.ds(row, ROW_CHUNK), :] = jnp.zeros(shape, jnp.float32)
        lax.fori_loop(0, live, slot_body, 0)
        sums = [
            -0.0625 * jnp.sum(acc_ref[d, pl.ds(row, ROW_CHUNK), :], axis=1, keepdims=True)
            for d in range(3)
        ]
        tile = jnp.where(lane == 0, sums[0], jnp.where(lane == 1, sums[1], jnp.where(lane == 2, sums[2], 0.0)))
        out_ref[pl.ds(row, ROW_CHUNK), :] = tile[:, : out_ref.shape[1]]
        return carry

    lax.fori_loop(0, PAIR_BLK // ROW_CHUNK, row_body, 0)


def lddt_sums(slots, counts, own_tab, coord_parts):
    blocks = counts.shape[0]
    out = pl.pallas_call(
        lddt_kernel,
        grid_spec=pltpu.PrefetchScalarGridSpec(
            num_scalar_prefetch=2,
            grid=(blocks,),
            in_specs=[
                pl.BlockSpec((PAIR_BLK, own_tab.shape[1]), lambda b, *_: (b, 0)),
                pl.BlockSpec(coord_parts.shape, lambda b, *_: (0, 0, 0)),
            ],
            out_specs=pl.BlockSpec((PAIR_BLK, 8), lambda b, *_: (b, 0)),
            scratch_shapes=[
                pltpu.VMEM((6, PAIR_BLK, PAIR_BLK), jnp.float32),
                pltpu.VMEM((3, PAIR_BLK, PAIR_BLK), jnp.float32),
            ],
        ),
        out_shape=jax.ShapeDtypeStruct((blocks * PAIR_BLK, 8), jnp.float32),
    )(slots, counts, own_tab, coord_parts)
    return out[:, :3].T

def dense(left, right):
    return jnp.einsum("sac,cf->saf", left, right, preferred_element_type=jnp.float32)


def on_device(
    token_feats,
    proj_w,
    atom_single,
    atom_token,
    true_coords,
    noise,
    sigma,
    coord_in,
    w_qkv,
    w_o,
    w_gu,
    w_down,
    gains,
    w_out,
    pair_blocks,
    pair_count,
):
    atom_rank = lax.axis_index("atoms")
    tok_rows = token_feats.shape[0]
    atom_rows = atom_single.shape[0]
    total_atoms = atom_rows * lax.axis_size("atoms")
    samples = noise.shape[0]
    feat_parts = ring_parts(token_feats, "samples")
    proj_parts = ring_parts(proj_w, "samples")
    token_sum = jnp.einsum(
        "kti,kio->to", feat_parts, proj_parts, preferred_element_type=jnp.float32
    )
    token_proj = token_sum.astype(jnp.bfloat16)
    padded_tok = extended(token_proj, (("atoms", 0),), HALO_TOK)
    first_token = atom_rank * tok_rows - HALO_TOK
    relative = atom_token - first_token
    onehot = (
        relative[:, None] == jnp.arange(tok_rows + 2 * HALO_TOK, dtype=jnp.int32)[None, :]
    ).astype(jnp.bfloat16)
    atom_base = atom_single.astype(jnp.float32) + jnp.dot(
        onehot, padded_tok, preferred_element_type=jnp.float32
    )
    sigma_col = sigma[:, None, None]
    noisy = true_coords[None] + sigma_col * noise
    noise_total = sigma_col * sigma_col + sigma_data * sigma_data
    scaled = noisy / jnp.sqrt(noise_total)
    hidden = atom_base[None] + jnp.einsum(
        "sda,dc->sac", scaled, coord_in, precision=lax.Precision.HIGHEST
    )
    key_halo = (KWIN - QBLK) // 2
    reaches = [0]
    for _ in range(LAYERS - 1):
        reaches.insert(0, -(-(reaches[0] + key_halo) // QBLK) * QBLK)
    buffer_start = -(reaches[0] + key_halo)
    hidden = extended(hidden, (("atoms", 1),), -buffer_start)
    query_win = jnp.arange(Q_TILE, dtype=jnp.int32)[:, None] // QBLK * QBLK
    key_index = jnp.arange(K_SPAN, dtype=jnp.int32)[None, :]
    band = ((key_index >= query_win) & (key_index < query_win + KWIN)).astype(jnp.float32)
    channels = hidden.shape[2]
    for layer_index in range(LAYERS):
        reach = reaches[layer_index]
        kv_off = -(reach + key_halo) - buffer_start
        q_off = kv_off + key_halo
        tiles = -(-(atom_rows + 2 * reach) // Q_TILE)
        tile_start = atom_rank * atom_rows - reach - key_halo + Q_TILE * jnp.arange(
            tiles, dtype=jnp.int32
        )
        position = tile_start[:, None] + key_index
        valid_tab = ((position >= 0) & (position < total_atoms)).astype(jnp.float32)
        normed = (rms_norm(hidden) * gains[layer_index, 0]).astype(jnp.bfloat16)
        qkv_all = dense(normed, w_qkv[layer_index]).astype(jnp.bfloat16)
        span_rows = kv_off + tiles * Q_TILE + K_SPAN - Q_TILE
        qkv_all = jnp.pad(qkv_all, ((0, 0), (0, max(0, span_rows - qkv_all.shape[1])), (0, 0)))
        queries = qkv_all[:, q_off : q_off + tiles * Q_TILE, :channels]
        key_vals = qkv_all[:, kv_off:span_rows, channels:]
        attended = jnp.stack(
            [window_attend(queries[s], key_vals[s], band, valid_tab) for s in range(samples)]
        )
        hidden = jnp.pad(hidden, ((0, 0), (0, max(0, span_rows - hidden.shape[1])), (0, 0)))
        hidden = hidden[:, q_off : q_off + tiles * Q_TILE] + dense(attended, w_o[layer_index])
        buffer_start = -reach
        normed = (rms_norm(hidden) * gains[layer_index, 1]).astype(jnp.bfloat16)
        gate_up = dense(normed, w_gu[layer_index])
        inner_act = (jax.nn.silu(gate_up[..., :FF_ATOM]) * gate_up[..., FF_ATOM:]).astype(
            jnp.bfloat16
        )
        hidden = hidden + dense(inner_act, w_down[layer_index])
    hidden = hidden[:, -buffer_start : -buffer_start + atom_rows]
    update = jnp.einsum("sac,cd->sda", rms_norm(hidden), w_out, precision=lax.Precision.HIGHEST)
    predicted = (
        sigma_data * sigma_data / noise_total * noisy
        + sigma_col * sigma_data / jnp.sqrt(noise_total) * update
    )
    mse_part = (
        2.0 / 3.0 * (noise_total / (sigma_col * sigma_data) ** 2) * (predicted - true_coords[None])
    )
    block_count = atom_rows // PAIR_BLK
    atom_peers = lax.axis_size("atoms")
    count_row = jnp.zeros((1, atom_rows), jnp.float32).at[0, 0].set(
        jnp.sum(pair_count.astype(jnp.float32) * (PAIR_BLK * PAIR_BLK) - PAIR_BLK)
    )
    coord_parts = ring_parts(
        jnp.concatenate([predicted[0], true_coords, count_row], axis=0), "atoms", direct=atom_peers <= 8
    )
    pair_total = jnp.sum(coord_parts[:, 6, 0])
    own_tab = jnp.concatenate(
        [predicted[0], true_coords, jnp.zeros((2, atom_rows), jnp.float32)], axis=0
    ).T
    source = (atom_rank - pair_blocks // block_count) % atom_peers
    slots = (source * block_count + pair_blocks % block_count).reshape(-1)
    pair_grad = 2.0 * lddt_sums(slots, pair_count, own_tab, coord_parts)[None]
    lddt_grad = total_atoms * PAIR_BLK / pair_total * pair_grad.reshape(samples, 3, atom_rows)
    coord_grad = mse_part - lddt_grad / PAIR_BLK
    return (coord_grad, lddt_grad)


def solution(mesh):
    in_specs = (
        P("atoms", "samples"),
        P("samples", None),
        P("atoms", None),
        P("atoms"),
        P(None, "atoms"),
        P("samples", None, "atoms"),
        P("samples"),
        P(),
        P(),
        P(),
        P(),
        P(),
        P(),
        P(),
        P("atoms", None),
        P("atoms"),
    )
    out_specs = (P("samples", None, "atoms"), P("samples", None, "atoms"))
    return jax.shard_map(
        on_device, mesh=mesh, in_specs=in_specs, out_specs=out_specs, check_vma=False
    )
```

```python
import functools
import math

import jax
import jax.numpy as jnp
from jax import lax
from jax.experimental import pallas as pl
from jax.experimental.pallas import tpu as pltpu
from jax.sharding import PartitionSpec as P

HEADS = 4
FF_ATOM = 256
LAYERS = 3
QBLK = 32
KWIN = 128
HALO_TOK = 16
PAIR_BLK = 128


sigma_data = 2.0
norm_epsilon = 1e-05
thresholds = (0.5, 1.0, 2.0, 4.0)


def extended(value, sides, width):
    for axis, dim in sides:
        peers, length = (lax.axis_size(axis), value.shape[dim])
        up = [(i, (i + 1) % peers) for i in range(peers - 1)]
        down = [(j, i) for i, j in up]
        last = lax.slice_in_dim(value, length - width, length, axis=dim)
        first = lax.slice_in_dim(value, 0, width, axis=dim)
        before = lax.ppermute(last, axis, up)
        after = lax.ppermute(first, axis, down)
        value = jnp.concatenate([before, value, after], axis=dim)
    return value


def ring_parts(value, axis, direct=False):
    peers = lax.axis_size(axis)
    parts = value[None]
    span = 1
    while not direct and span < peers and peers % (2 * span) == 0:
        pairs = [(i, (i + span) % peers) for i in range(peers)]
        parts = jnp.concatenate([parts, lax.ppermute(parts, axis, pairs)])
        span *= 2
    if span < peers:
        extra = [value[None]]
        for shift in range(span, peers):
            pairs = [(i, (i + shift) % peers) for i in range(peers)]
            extra.append(lax.ppermute(value, axis, pairs)[None])
        parts = jnp.concatenate([parts] + extra[1:])
    return parts

def rms_norm(tensor):
    return tensor * lax.rsqrt(jnp.mean(tensor * tensor, axis=-1, keepdims=True) + norm_epsilon)


Q_TILE = 128
K_SPAN = 256


def attend_kernel(qkv_ref, band_ref, valid_ref, out_ref, *, kv_off):
    tile = pl.program_id(0)
    channels = out_ref.shape[1]
    head_dim = channels // HEADS
    scale = head_dim ** (-0.5)
    start = pl.multiple_of(tile * Q_TILE, Q_TILE)
    block = qkv_ref[pl.ds(start + kv_off, K_SPAN), :]
    keys_vals = block[:, channels:]
    query_rows = qkv_ref[pl.ds(start + kv_off + (KWIN - QBLK) // 2, Q_TILE), :][:, :channels]
    live = (band_ref[...] * valid_ref[pl.ds(tile, 1), :]) > 0.0
    heads = []
    for head in range(HEADS):
        cols = slice(head * head_dim, (head + 1) * head_dim)
        vcols = slice(channels + head * head_dim, channels + (head + 1) * head_dim)
        scores = lax.dot_general(
            query_rows[:, cols], keys_vals[:, cols], (((1,), (1,)), ((), ())),
            preferred_element_type=jnp.float32,
        )
        scores = jnp.where(live, scores, -1e30)
        row_max = jnp.max(scores, axis=-1, keepdims=True)
        exp_scores = jnp.exp2((scores - row_max) * (scale * math.log2(math.e)))
        inverse = 1.0 / jnp.sum(exp_scores, axis=-1, keepdims=True)
        weights = (exp_scores * inverse).astype(jnp.bfloat16)
        heads.append(
            jnp.dot(weights, keys_vals[:, vcols], preferred_element_type=jnp.float32).astype(
                jnp.bfloat16
            )
        )
    out_ref[...] = jnp.concatenate(heads, axis=1)


def window_attend(qkv, kv_off, tiles, band, valid_tab):
    channels = qkv.shape[1] // 3
    return pl.pallas_call(
        functools.partial(attend_kernel, kv_off=kv_off),
        grid=(tiles,),
        in_specs=[
            pl.BlockSpec(qkv.shape, lambda t: (0, 0)),
            pl.BlockSpec(band.shape, lambda t: (0, 0)),
            pl.BlockSpec(valid_tab.shape, lambda t: (0, 0)),
        ],
        out_specs=pl.BlockSpec((Q_TILE, channels), lambda t: (t, 0)),
        out_shape=jax.ShapeDtypeStruct((tiles * Q_TILE, channels), jnp.bfloat16),
    )(qkv, band, valid_tab)

ROW_CHUNK = 128


def lddt_kernel(slots_ref, count_ref, own_ref, coord_ref, out_ref, cols_ref, acc_ref):
    block = pl.program_id(0)
    live = count_ref[block]
    blocks = count_ref.shape[0]
    max_slots = slots_ref.shape[0] // blocks
    shape = (ROW_CHUNK, PAIR_BLK)
    lane = lax.broadcasted_iota(jnp.int32, shape, 1)
    for chunk in range(PAIR_BLK // ROW_CHUNK):
        rows = slice(chunk * ROW_CHUNK, (chunk + 1) * ROW_CHUNK)
        own = own_ref[rows, :]
        for d in range(6):
            cols_ref[d, rows, :] = jnp.broadcast_to(own[:, d : d + 1], shape)

    def row_body(row_index, carry):
        row = pl.multiple_of(row_index * ROW_CHUNK, ROW_CHUNK)

        def slot_body(slot_index, accs):
            slot = slots_ref[block * max_slots + slot_index]
            peer = slot // blocks
            start = pl.multiple_of((slot % blocks) * PAIR_BLK, PAIR_BLK)
            part = coord_ref[peer, :, pl.ds(start, PAIR_BLK)]
            part_pred = part[0:3]
            part_true = part[3:6]
            gaps = [cols_ref[d, pl.ds(row, ROW_CHUNK), :] - part_pred[d : d + 1, :] for d in range(3)]
            true_gaps = [
                cols_ref[3 + d, pl.ds(row, ROW_CHUNK), :] - part_true[d : d + 1, :] for d in range(3)
            ]
            square_pred = gaps[0] * gaps[0] + gaps[1] * gaps[1] + gaps[2] * gaps[2] + 1.0
            square_true = (
                true_gaps[0] * true_gaps[0] + true_gaps[1] * true_gaps[1] + true_gaps[2] * true_gaps[2]
            ) + 1.0
            inv_pred = lax.rsqrt(square_pred)
            gap_dist = square_pred * inv_pred - square_true * lax.rsqrt(square_true)
            square_err = gap_dist * gap_dist + 0.01
            inv_err = lax.rsqrt(square_err)
            half_err = 0.5 * (square_err * inv_err)
            curve = [jnp.tanh(0.5 * t - half_err) for t in thresholds]
            bend = curve[0] * curve[0] + curve[1] * curve[1] + curve[2] * curve[2] + curve[3] * curve[3]
            coef = ((4.0 - bend) * gap_dist) * (inv_err * inv_pred)
            for d in range(3):
                acc_ref[d, pl.ds(row, ROW_CHUNK), :] += coef * gaps[d]
            return accs

        for d in range(3):
            acc_ref[d, pl.ds(row, ROW_CHUNK), :] = jnp.zeros(shape, jnp.float32)
        lax.fori_loop(0, live, slot_body, 0)
        sums = [
            -0.0625 * jnp.sum(acc_ref[d, pl.ds(row, ROW_CHUNK), :], axis=1, keepdims=True)
            for d in range(3)
        ]
        tile = jnp.where(lane == 0, sums[0], jnp.where(lane == 1, sums[1], jnp.where(lane == 2, sums[2], 0.0)))
        out_ref[pl.ds(row, ROW_CHUNK), :] = tile[:, : out_ref.shape[1]]
        return carry

    lax.fori_loop(0, PAIR_BLK // ROW_CHUNK, row_body, 0)


def lddt_sums(slots, counts, own_tab, coord_parts):
    blocks = counts.shape[0]
    out = pl.pallas_call(
        lddt_kernel,
        grid_spec=pltpu.PrefetchScalarGridSpec(
            num_scalar_prefetch=2,
            grid=(blocks,),
            in_specs=[
                pl.BlockSpec((PAIR_BLK, own_tab.shape[1]), lambda b, *_: (b, 0)),
                pl.BlockSpec(coord_parts.shape, lambda b, *_: (0, 0, 0)),
            ],
            out_specs=pl.BlockSpec((PAIR_BLK, 8), lambda b, *_: (b, 0)),
            scratch_shapes=[
                pltpu.VMEM((6, PAIR_BLK, PAIR_BLK), jnp.float32),
                pltpu.VMEM((3, PAIR_BLK, PAIR_BLK), jnp.float32),
            ],
        ),
        out_shape=jax.ShapeDtypeStruct((blocks * PAIR_BLK, 8), jnp.float32),
    )(slots, counts, own_tab, coord_parts)
    return out[:, :3].T

def dense(left, right):
    return jnp.einsum("sac,cf->saf", left, right, preferred_element_type=jnp.float32)


def on_device(
    token_feats,
    proj_w,
    atom_single,
    atom_token,
    true_coords,
    noise,
    sigma,
    coord_in,
    w_qkv,
    w_o,
    w_gu,
    w_down,
    gains,
    w_out,
    pair_blocks,
    pair_count,
):
    atom_rank = lax.axis_index("atoms")
    tok_rows = token_feats.shape[0]
    atom_rows = atom_single.shape[0]
    total_atoms = atom_rows * lax.axis_size("atoms")
    samples = noise.shape[0]
    feat_parts = ring_parts(token_feats, "samples")
    proj_parts = ring_parts(proj_w, "samples")
    token_sum = jnp.einsum(
        "kti,kio->to", feat_parts, proj_parts, preferred_element_type=jnp.float32
    )
    token_proj = token_sum.astype(jnp.bfloat16)
    padded_tok = extended(token_proj, (("atoms", 0),), HALO_TOK)
    first_token = atom_rank * tok_rows - HALO_TOK
    relative = atom_token - first_token
    onehot = (
        relative[:, None] == jnp.arange(tok_rows + 2 * HALO_TOK, dtype=jnp.int32)[None, :]
    ).astype(jnp.bfloat16)
    atom_base = atom_single.astype(jnp.float32) + jnp.dot(
        onehot, padded_tok, preferred_element_type=jnp.float32
    )
    sigma_col = sigma[:, None, None]
    noisy = true_coords[None] + sigma_col * noise
    noise_total = sigma_col * sigma_col + sigma_data * sigma_data
    scaled = noisy / jnp.sqrt(noise_total)
    hidden = atom_base[None] + jnp.einsum(
        "sda,dc->sac", scaled, coord_in, precision=lax.Precision.HIGHEST
    )
    key_halo = (KWIN - QBLK) // 2
    reaches = [0]
    for _ in range(LAYERS - 1):
        reaches.insert(0, -(-(reaches[0] + key_halo) // QBLK) * QBLK)
    buffer_start = -(reaches[0] + key_halo)
    hidden = extended(hidden, (("atoms", 1),), -buffer_start)
    query_win = jnp.arange(Q_TILE, dtype=jnp.int32)[:, None] // QBLK * QBLK
    key_index = jnp.arange(K_SPAN, dtype=jnp.int32)[None, :]
    band = ((key_index >= query_win) & (key_index < query_win + KWIN)).astype(jnp.float32)
    channels = hidden.shape[2]
    for layer_index in range(LAYERS):
        reach = reaches[layer_index]
        kv_off = -(reach + key_halo) - buffer_start
        q_off = kv_off + key_halo
        tiles = -(-(atom_rows + 2 * reach) // Q_TILE)
        tile_start = atom_rank * atom_rows - reach - key_halo + Q_TILE * jnp.arange(
            tiles, dtype=jnp.int32
        )
        position = tile_start[:, None] + key_index
        valid_tab = ((position >= 0) & (position < total_atoms)).astype(jnp.float32)
        normed = (rms_norm(hidden) * gains[layer_index, 0]).astype(jnp.bfloat16)
        qkv_all = dense(normed, w_qkv[layer_index]).astype(jnp.bfloat16)
        span_rows = kv_off + tiles * Q_TILE + K_SPAN - Q_TILE
        qkv_all = jnp.pad(qkv_all, ((0, 0), (0, max(0, span_rows - qkv_all.shape[1])), (0, 0)))
        attended = jnp.stack(
            [window_attend(qkv_all[s], kv_off, tiles, band, valid_tab) for s in range(samples)]
        )
        hidden = jnp.pad(hidden, ((0, 0), (0, max(0, span_rows - hidden.shape[1])), (0, 0)))
        hidden = hidden[:, q_off : q_off + tiles * Q_TILE] + dense(attended, w_o[layer_index])
        buffer_start = -reach
        normed = (rms_norm(hidden) * gains[layer_index, 1]).astype(jnp.bfloat16)
        gate_up = dense(normed, w_gu[layer_index])
        inner_act = (jax.nn.silu(gate_up[..., :FF_ATOM]) * gate_up[..., FF_ATOM:]).astype(
            jnp.bfloat16
        )
        hidden = hidden + dense(inner_act, w_down[layer_index])
    hidden = hidden[:, -buffer_start : -buffer_start + atom_rows]
    update = jnp.einsum("sac,cd->sda", rms_norm(hidden), w_out, precision=lax.Precision.HIGHEST)
    predicted = (
        sigma_data * sigma_data / noise_total * noisy
        + sigma_col * sigma_data / jnp.sqrt(noise_total) * update
    )
    mse_part = (
        2.0 / 3.0 * (noise_total / (sigma_col * sigma_data) ** 2) * (predicted - true_coords[None])
    )
    block_count = atom_rows // PAIR_BLK
    atom_peers = lax.axis_size("atoms")
    count_row = jnp.zeros((1, atom_rows), jnp.float32).at[0, 0].set(
        jnp.sum(pair_count.astype(jnp.float32) * (PAIR_BLK * PAIR_BLK) - PAIR_BLK)
    )
    coord_parts = ring_parts(
        jnp.concatenate([predicted[0], true_coords, count_row], axis=0), "atoms", direct=atom_peers <= 8
    )
    pair_total = jnp.sum(coord_parts[:, 6, 0])
    own_tab = jnp.concatenate(
        [predicted[0], true_coords, jnp.zeros((2, atom_rows), jnp.float32)], axis=0
    ).T
    source = (atom_rank - pair_blocks // block_count) % atom_peers
    slots = (source * block_count + pair_blocks % block_count).reshape(-1)
    pair_grad = 2.0 * lddt_sums(slots, pair_count, own_tab, coord_parts)[None]
    lddt_grad = total_atoms * PAIR_BLK / pair_total * pair_grad.reshape(samples, 3, atom_rows)
    coord_grad = mse_part - lddt_grad / PAIR_BLK
    return (coord_grad, lddt_grad)


def solution(mesh):
    in_specs = (
        P("atoms", "samples"),
        P("samples", None),
        P("atoms", None),
        P("atoms"),
        P(None, "atoms"),
        P("samples", None, "atoms"),
        P("samples"),
        P(),
        P(),
        P(),
        P(),
        P(),
        P(),
        P(),
        P("atoms", None),
        P("atoms"),
    )
    out_specs = (P("samples", None, "atoms"), P("samples", None, "atoms"))
    return jax.shard_map(
        on_device, mesh=mesh, in_specs=in_specs, out_specs=out_specs, check_vma=False
    )
```
